128 devices in a mesh: req: 32 (over y, z, core), hid: 4 (over x).
Axes of the slice: x: 4, y: 4, z: 4, core: 2. Of those that a mesh axis runs over, the one named last changes fastest.
Arguments:
- hidden_in: bfloat16 [32, 512, 1536], P('req', 'hid'), may hold values from -6 to 6
- queries: bfloat16 [32, 512, 1536], P('req', 'hid'), may hold values from -4 to 4
- cache_keys: bfloat16 [32, 4096, 256], P('req', 'hid'), may hold values from -6 to 6
- cache_values: bfloat16 [32, 4096, 256], P('req', 'hid'), may hold values from -6 to 6
- lengths: int32 [32], P('req'), may hold values from 256 to 4096, as said below
- routes: int32 [32, 512, 4], P('req'), may hold values from 0 to 31, all different within a row; in each aligned block of 128 rows (0 to 127, 128 to 255, ..., all dimensions but the last counted through in order) at most 32 rows name the same one
- attn_gain: float32 [1536], replicated, may hold values from 0.25 to 1.75
- key_proj: bfloat16 [1536, 256], replicated, may hold values from -0.15625 to 0.15625
- value_proj: bfloat16 [1536, 256], replicated, may hold values from -0.15625 to 0.15625
- out_proj: bfloat16 [1536, 1536], replicated, may hold values from -0.15625 to 0.15625
- moe_gain: float32 [1536], replicated, may hold values from 0.25 to 1.75
- router: bfloat16 [1536, 32], replicated, may hold values from -0.3125 to 0.3125
- gate_up: bfloat16 [32, 2, 1536, 768], P('req', None, None, 'hid'), may hold values from -0.15625 to 0.15625
- down_proj: bfloat16 [32, 768, 1536], P('req', 'hid'), may hold values from -0.21875 to 0.21875
Outputs:
- layer_out: bfloat16 [32, 512, 1536], P('req', 'hid')
- new_keys: bfloat16 [32, 512, 256], P('req', 'hid')
- new_values: bfloat16 [32, 512, 256], P('req', 'hid')
The draws below stay inside these ranges and needn't reach their ends.
Inputs may be any that keep to these rules, and one draw needn't show every extreme that they name: `routes`: each row names 4 different experts; within each aligned block of 128 tokens (the tokens of one device) no expert is named by more than 32 tokens, and in some block one expert is named by exactly 32. `lengths`: some request holds exactly 4096 cached positions and some other exactly 256.
All inputs are finite; a program needn't handle non-finite values.
Results may differ from the reference program's by a relative error of at most 0.015.
Values may be sent and summed in bfloat16 or wider, within the bound.
No kernel may reach another device: no remote copies, remote signals or barrier semaphores. Data moves between devices by JAX's collectives and lax.ppermute only.
A program may use at most 128 MiB of HBM per device.

```python
import math
import jax
import jax.numpy as jnp
import numpy as np
from jax import lax

D = 1536
QH = 12
KVH = 2
HD = 128
FF = 768
TOP = 4
EXPERTS = 32
QW = 1536
KVW = 256
TOK_DEV = 128
SPAN = 512
CACHE = 4096
REQUESTS = 32
CAP = 32
N_HID = 4


def draw_queries(key, part):
    base_key = jax.random.fold_in(key, 11)
    values = jnp.clip(jax.random.normal(base_key, (REQUESTS, SPAN, QW), jnp.float32), -4.0, 4.0)
    return values.astype(jnp.bfloat16)


def draw_cache_keys(key, part):
    base_key = jax.random.fold_in(key, 23)
    values = jnp.clip(jax.random.normal(base_key, (REQUESTS, CACHE, KVW), jnp.float32), -6.0, 6.0)
    return values.astype(jnp.bfloat16)


def draw_lengths(key, part):
    drawn = jax.random.randint(jax.random.fold_in(key, 41), (REQUESTS,), CACHE // 16, CACHE + 1)
    longest = jax.random.randint(jax.random.fold_in(key, 43), (), 0, REQUESTS)
    other_step = jax.random.randint(jax.random.fold_in(key, 47), (), 1, REQUESTS)
    shortest = (longest + other_step) % REQUESTS
    drawn = drawn.at[longest].set(CACHE)
    drawn = drawn.at[shortest].set(CACHE // 16)
    return drawn.astype(jnp.int32)


def level_of(stream_key, extent, cuts, smallest, largest):
    gain = 1.0
    for axis_at, parts in cuts:
        steps = jax.random.uniform(jax.random.fold_in(jax.random.fold_in(stream_key, 6), axis_at), (parts,), jnp.float32, smallest / len(cuts), largest / len(cuts))
        gain = gain * jnp.repeat(jnp.exp(steps), extent[axis_at] // parts).reshape((-1,) + (1,) * (len(extent) - 1 - axis_at))
    return gain


def assign_block(stream_key, own, number, rows, number_of, top, most, slope):
    ranking = jax.random.permutation(stream_key, number_of)
    crowded, usual = shares(number_of, rows * top, most, slope, True), shares(number_of, rows * top, most, slope, False)
    places = jnp.arange(number_of)

    def named(sizes, offset_by):
        used = int((sizes > 0).sum())
        fixed = max(1, used // 4)
        moved = fixed + (places - fixed + offset_by * (used - fixed)) % max(1, number_of - fixed)
        return jnp.zeros((number_of,), jnp.int32).at[ranking[jnp.where(places < fixed, places, moved)]].set(jnp.asarray(sizes, jnp.int32))

    sizes = jnp.where(number % 4 == 0, named(crowded, number // 4), named(usual, number - number // 4 - 1))
    mixed = jax.random.permutation(jax.random.fold_in(own, 3), number_of)
    donor, sink = mixed[0:number_of // 2 * 2:2], mixed[1:number_of // 2 * 2:2]
    margin = jnp.minimum(sizes[donor] - 1, most - sizes[sink]) // 2
    margin = jnp.where((donor == ranking[0]) | (sink == ranking[0]) | (sizes[sink] == 0), 0, jnp.maximum(margin, 0))
    moved = jax.random.randint(jax.random.fold_in(own, 4), (number_of // 2,), 0, 1 << 20) % (margin + 1)
    sizes = sizes.at[donor].add(-moved).at[sink].add(moved)
    labels = jnp.searchsorted(jnp.cumsum(sizes), jnp.arange(rows * top), side="right").astype(jnp.int32)
    listing = labels.reshape(top, rows).T
    listing = listing[jax.random.permutation(jax.random.fold_in(own, 1), rows)]
    offset_by = jax.random.randint(jax.random.fold_in(own, 2), (rows, 1), 0, top)
    return jnp.take_along_axis(listing, (jnp.arange(top)[None, :] + offset_by) % top, axis=1)


def shares(count, total, limit, skew, full):
    weights = [(1 << 20) // math.isqrt(standing ** skew) + 1 for standing in range(1, count + 1)]
    largest = limit if full else min(limit, max(-(-total // count), total * weights[0] // sum(weights)))
    least = 1 if total - largest >= count - 1 else 0
    holding, surplus = [largest] + [least] * (count - 1), total - largest - least * (count - 1)
    while surplus > 0:
        free = [i for i in range(1, count) if holding[i] < largest] or [i for i in range(1, count) if holding[i] < limit]
        mass, remaining = sum([weights[i] for i in free]), surplus
        for i in free:
            extra = min(limit - holding[i], max(1, remaining * weights[i] // mass), surplus)
            holding[i] = holding[i] + extra
            surplus = surplus - extra
    return np.array(holding)


def bell_draw(stream_key, shape, scale, most, split=(), kind=jnp.bfloat16):
    entries = scale * jax.random.normal(stream_key, shape, jnp.float32)
    if split:
        entries = entries * level_of(stream_key, shape, split, -0.22, 0.18)
    return jnp.clip(entries, -most, most).astype(kind)


def setup_inputs(seed: int = 0) -> dict:
    splits = jax.random.split(jax.random.key(seed), 15)
    hidden_in = bell_draw(splits[0], (REQUESTS, SPAN, D), 1.0, 6.0, ((0, 32), (1, 4)))
    queries = draw_queries(jax.random.fold_in(splits[14], 71), 0)
    cache_keys = draw_cache_keys(jax.random.fold_in(splits[14], 71), 0)
    cache_values = bell_draw(splits[3], (REQUESTS, CACHE, KVW), 1.0, 6.0, ((0, 32), (1, 4)))
    lengths = draw_lengths(jax.random.fold_in(splits[14], 71), 0)
    routes_keys = jax.random.split(jax.random.fold_in(splits[5], 1), REQUESTS * SPAN // TOK_DEV)
    routes_turns = jax.random.permutation(jax.random.fold_in(splits[5], 3), REQUESTS * SPAN // TOK_DEV)
    routes = jax.vmap(lambda own, number: assign_block(jax.random.fold_in(splits[5], 2), own, number, TOK_DEV, EXPERTS, TOP, CAP, 2))(routes_keys, routes_turns).reshape((REQUESTS, SPAN, TOP))
    attn_gain = jnp.clip(1.0 + 0.15 * jax.random.normal(splits[6], (D,), jnp.float32), 0.25, 1.75)
    key_proj = bell_draw(splits[7], (D, KVW), D ** -0.5, 0.15625)
    value_proj = bell_draw(splits[8], (D, KVW), D ** -0.5, 0.15625)
    out_proj = bell_draw(splits[9], (QW, D), QW ** -0.5, 0.15625)
    moe_gain = jnp.clip(1.0 + 0.15 * jax.random.normal(splits[10], (D,), jnp.float32), 0.25, 1.75)
    router = bell_draw(splits[11], (D, EXPERTS), (D // 4) ** -0.5, 0.3125)
    gate_up = bell_draw(splits[12], (EXPERTS, 2, D, FF), D ** -0.5, 0.15625, ((0, 32), (3, 4)))
    down_proj = bell_draw(splits[13], (EXPERTS, FF, D), FF ** -0.5, 0.21875, ((0, 32), (1, 4)))
    return {"hidden_in": hidden_in, "queries": queries, "cache_keys": cache_keys, "cache_values": cache_values, "lengths": lengths, "routes": routes, "attn_gain": attn_gain, "key_proj": key_proj, "value_proj": value_proj, "out_proj": out_proj, "moe_gain": moe_gain, "router": router, "gate_up": gate_up, "down_proj": down_proj}


EPS = 1e-06
MASKED_SCORE = -1e+30

def normalize(row_data, gain_vector):
    row_data = row_data.astype(jnp.float32)
    return row_data * lax.rsqrt(lax.optimization_barrier(jnp.mean(row_data * row_data, axis=-1, keepdims=True)) + EPS) * gain_vector.astype(jnp.float32)

def attend(packed):
    queries, keys_old, values_old, keys_new, values_new, length = packed
    group_size = QH // KVH
    grouped = queries.astype(jnp.float32).reshape(SPAN, KVH, group_size, HD)
    key_rows = jnp.concatenate([keys_old, keys_new], axis=0).astype(jnp.float32).reshape(CACHE + SPAN, KVH, HD)
    value_rows = jnp.concatenate([values_old, values_new], axis=0).astype(jnp.float32).reshape(CACHE + SPAN, KVH, HD)
    scores = jnp.einsum('tgsd,kgd->gstk', grouped, key_rows) * HD ** (-0.5)
    positions = jnp.arange(CACHE + SPAN, dtype=jnp.int32)
    token_pos = jnp.arange(SPAN, dtype=jnp.int32)
    visible = jnp.where(positions[None, :] < CACHE, positions[None, :] < length, positions[None, :] - CACHE <= token_pos[:, None])
    scores = jnp.where(visible, scores, MASKED_SCORE)
    row_max = lax.optimization_barrier(jnp.max(scores, axis=-1, keepdims=True))
    weights = jnp.where(visible, jnp.exp(scores - row_max), 0.0)
    totals = lax.optimization_barrier(jnp.sum(weights, axis=-1))
    probs = lax.optimization_barrier(weights.astype(jnp.bfloat16))
    mixture = jnp.einsum('gstk,kgd->tgsd', probs.astype(jnp.float32), value_rows)
    mixture = mixture / jnp.transpose(totals, (2, 0, 1))[..., None]
    return mixture.reshape(SPAN, QW).astype(jnp.bfloat16)

def reference(hidden_in, queries, cache_keys, cache_values, lengths, routes, attn_gain, key_proj, value_proj, out_proj, moe_gain, router, gate_up, down_proj):
    flat_in = hidden_in.reshape(REQUESTS * SPAN, D)
    normed = normalize(flat_in, attn_gain).astype(jnp.bfloat16)
    new_keys = jnp.dot(normed, key_proj, preferred_element_type=jnp.float32).astype(jnp.bfloat16).reshape(REQUESTS, SPAN, KVW)
    new_values = jnp.dot(normed, value_proj, preferred_element_type=jnp.float32).astype(jnp.bfloat16).reshape(REQUESTS, SPAN, KVW)
    attended = lax.map(attend, (queries, cache_keys, cache_values, new_keys, new_values, lengths))
    mid_stream = (flat_in.astype(jnp.float32) + jnp.dot(attended.reshape(REQUESTS * SPAN, QW), out_proj, preferred_element_type=jnp.float32)).astype(jnp.bfloat16)
    moe_in = normalize(mid_stream, moe_gain).astype(jnp.bfloat16)
    logits = jnp.dot(moe_in, router, preferred_element_type=jnp.float32)
    chosen = routes.reshape(REQUESTS * SPAN, TOP).astype(jnp.int32)
    picked = jnp.take_along_axis(logits, chosen, axis=1)
    gate_values = jax.nn.sigmoid(picked)
    weights = gate_values / lax.optimization_barrier(jnp.sum(gate_values, axis=1, keepdims=True))
    block_count = REQUESTS * SPAN // TOK_DEV
    pair_count = TOK_DEV * TOP
    blocks = chosen.reshape(block_count, pair_count)
    onehot = (blocks[..., None] == jnp.arange(EXPERTS, dtype=jnp.int32)).astype(jnp.int32)
    slot_ids = lax.optimization_barrier(jnp.sum((jnp.cumsum(onehot, axis=1) - 1) * onehot, axis=-1)).astype(jnp.int32)
    block_ids = jnp.arange(block_count, dtype=jnp.int32)[:, None]
    pair_token = jnp.broadcast_to((jnp.arange(pair_count, dtype=jnp.int32) // TOP)[None, :], (block_count, pair_count))
    slot_table = jnp.full((block_count, EXPERTS, CAP), TOK_DEV, jnp.int32)
    slot_table = slot_table.at[block_ids, blocks, slot_ids].set(pair_token)
    padded = jnp.concatenate([moe_in.reshape(block_count, TOK_DEV, D), jnp.zeros((block_count, 1, D), jnp.bfloat16)], axis=1)
    slice_width = FF // N_HID

    def run_expert(packed):
        indices, gate_weights, down_weights = packed
        row_data = padded[block_ids, indices].reshape(block_count * CAP, D)
        gate_out = jnp.dot(row_data, gate_weights[0], preferred_element_type=jnp.float32)
        up_out = jnp.dot(row_data, gate_weights[1], preferred_element_type=jnp.float32)
        activation = (jnp.maximum(gate_out, 0.0) * up_out).astype(jnp.bfloat16)
        partials = jnp.stack([jnp.dot(activation[:, portion * slice_width:(portion + 1) * slice_width], down_weights[portion * slice_width:(portion + 1) * slice_width], preferred_element_type=jnp.float32).astype(jnp.bfloat16) for portion in range(N_HID)])
        partials = lax.optimization_barrier(partials)
        return lax.optimization_barrier(jnp.sum(partials.astype(jnp.float32), axis=0)).astype(jnp.bfloat16).reshape(block_count, CAP, D)
    results = lax.map(run_expert, (jnp.transpose(slot_table, (1, 0, 2)), gate_up, down_proj))
    fetched = results[blocks, block_ids, slot_ids].reshape(REQUESTS * SPAN, TOP, D).astype(jnp.float32)
    moe_out = lax.optimization_barrier(jnp.sum(weights[..., None] * fetched, axis=1))
    layer_out = (mid_stream.astype(jnp.float32) + moe_out).astype(jnp.bfloat16).reshape(REQUESTS, SPAN, D)
    return (layer_out, new_keys, new_values)
```

```python
import jax
import jax.numpy as jnp
from jax import lax
from jax.sharding import PartitionSpec as P

QH = 12
KVH = 2
HD = 128


EPS = 1e-06
MASKED_SCORE = -1e30
KEY_BLOCK = 512


def normalize(row_data, gain_vector):
    row_data = row_data.astype(jnp.float32)
    return (
        row_data
        * lax.rsqrt(jnp.mean(row_data * row_data, axis=-1, keepdims=True) + EPS)
        * gain_vector
    )


def absorb(state_now, grouped, key_rows, value_rows, visible):
    row_max, totals, accumulated = state_now
    scores = jnp.einsum(
        "tgsd,kgd->gstk", grouped, key_rows.reshape(-1, KVH, HD), preferred_element_type=jnp.float32
    ) * HD ** (-0.5)
    scores = jnp.where(visible, scores, MASKED_SCORE)
    new_max = jnp.maximum(row_max, jnp.max(scores, axis=-1))
    weights = jnp.where(visible, jnp.exp(scores - new_max[..., None]), 0.0)
    rescale = jnp.exp(row_max - new_max)
    totals = totals * rescale + jnp.sum(weights, axis=-1)
    accumulated = accumulated * rescale[..., None] + jnp.einsum(
        "gstk,kgd->gstd",
        weights.astype(jnp.bfloat16),
        value_rows.reshape(-1, KVH, HD),
        preferred_element_type=jnp.float32,
    )
    return (new_max, totals, accumulated)


def cache_block(state_now, grouped, key_rows, value_rows, first_pos, length):
    positions = first_pos + jnp.arange(key_rows.shape[0], dtype=jnp.int32)
    visible = (positions < length)[None, :]
    return lax.cond(
        first_pos < length,
        lambda current: absorb(current, grouped, key_rows, value_rows, visible),
        lambda current: current,
        state_now,
    )


def span_block(state_now, grouped, key_rows, value_rows, first_pos, query_pos):
    positions = first_pos + jnp.arange(key_rows.shape[0], dtype=jnp.int32)
    visible = positions[None, :] <= query_pos[:, None]
    return lax.cond(
        first_pos <= query_pos[-1],
        lambda current: absorb(current, grouped, key_rows, value_rows, visible),
        lambda current: current,
        state_now,
    )


def block_size(extent):
    return max(min(KEY_BLOCK, extent), extent // 8)


def empty_state(query_count):
    group_size = QH // KVH
    return (
        jnp.full((KVH, group_size, query_count), MASKED_SCORE, jnp.float32),
        jnp.zeros((KVH, group_size, query_count), jnp.float32),
        jnp.zeros((KVH, group_size, query_count, HD), jnp.float32),
    )


def expert_activation(row_data, gate_weights):
    gate_out = jnp.dot(row_data, gate_weights[0], preferred_element_type=jnp.float32)
    up_out = jnp.dot(row_data, gate_weights[1], preferred_element_type=jnp.float32)
    return (jnp.maximum(gate_out, 0.0) * up_out).astype(jnp.bfloat16)


def body(
    hidden_in,
    queries,
    cache_keys,
    cache_values,
    lengths,
    routes,
    attn_gain,
    key_proj,
    value_proj,
    out_proj,
    moe_gain,
    router,
    gate_up,
    down_proj,
):
    own_count = hidden_in.shape[1]
    model_width = hidden_in.shape[2]
    hid_index = lax.axis_index("hid")
    hid_count = lax.axis_size("hid")
    group_size = QH // KVH
    normed = normalize(hidden_in[0], attn_gain).astype(jnp.bfloat16)
    new_keys = jnp.dot(normed, key_proj, preferred_element_type=jnp.float32).astype(jnp.bfloat16)
    new_values = jnp.dot(normed, value_proj, preferred_element_type=jnp.float32).astype(jnp.bfloat16)
    length = lengths[0]
    cache_local = cache_keys.shape[1]
    all_keys = lax.all_gather(jnp.concatenate([cache_keys[0], new_keys], axis=0), "hid", axis=0)
    all_values = lax.all_gather(jnp.concatenate([cache_values[0], new_values], axis=0), "hid", axis=0)
    all_gate_up = lax.all_gather(gate_up[0], "hid", axis=0)
    all_down = lax.all_gather(down_proj[0], "hid", axis=0)
    grouped = queries[0].reshape(own_count, KVH, group_size, HD)
    query_pos = hid_index * own_count + jnp.arange(own_count, dtype=jnp.int32)
    attn_state = empty_state(own_count)
    step_size = block_size(cache_local)
    for part in range(hid_count):
        for offset in range(0, cache_local, step_size):
            attn_state = cache_block(
                attn_state,
                grouped,
                all_keys[part, offset : offset + step_size],
                all_values[part, offset : offset + step_size],
                part * cache_local + offset,
                length,
            )
        attn_state = span_block(
            attn_state,
            grouped,
            all_keys[part, cache_local:],
            all_values[part, cache_local:],
            part * own_count,
            query_pos,
        )
    row_max, totals, accumulated = attn_state
    attended = (
        jnp.transpose(accumulated / totals[..., None], (2, 0, 1, 3))
        .reshape(own_count, QH * HD)
        .astype(jnp.bfloat16)
    )
    mid_stream = (
        hidden_in[0].astype(jnp.float32)
        + jnp.dot(attended, out_proj, preferred_element_type=jnp.float32)
    ).astype(jnp.bfloat16)
    moe_in = normalize(mid_stream, moe_gain).astype(jnp.bfloat16)
    logits = jnp.dot(moe_in, router, preferred_element_type=jnp.float32)
    expert_count = router.shape[1]
    top_count = routes.shape[2]
    capacity = 2 * own_count * top_count // expert_count
    own_routes = lax.dynamic_slice_in_dim(routes[0], hid_index * own_count, own_count, axis=0)
    flat_routes = own_routes.reshape(-1)
    onehot = (flat_routes[:, None] == jnp.arange(expert_count, dtype=jnp.int32)[None, :]).astype(
        jnp.int32
    )
    slot_ids = jnp.sum((jnp.cumsum(onehot, axis=0) - 1) * onehot, axis=-1)
    targets = flat_routes * capacity + slot_ids
    slot_count = expert_count * capacity
    pick = targets[None, :] == jnp.arange(slot_count, dtype=jnp.int32)[:, None]
    pick_rows = jnp.any(pick.reshape(slot_count, own_count, top_count), axis=-1).astype(jnp.bfloat16)
    send_rows = jnp.dot(pick_rows, moe_in, preferred_element_type=jnp.float32).astype(jnp.bfloat16)
    grouped_rows = lax.all_to_all(
        send_rows.reshape(expert_count, capacity, model_width), "req", 0, 0, tiled=True
    )
    flat_rows = grouped_rows.reshape(-1, model_width)
    gate_out = jnp.einsum(
        "nd,hdf->hnf", flat_rows, all_gate_up[:, 0], preferred_element_type=jnp.float32
    )
    up_out = jnp.einsum(
        "nd,hdf->hnf", flat_rows, all_gate_up[:, 1], preferred_element_type=jnp.float32
    )
    activation = (jnp.maximum(gate_out, 0.0) * up_out).astype(jnp.bfloat16)
    partials = jnp.einsum(
        "hnf,hfd->hnd", activation, all_down, preferred_element_type=jnp.float32
    ).astype(jnp.bfloat16)
    expert_out = jnp.sum(partials.astype(jnp.float32), axis=0).astype(jnp.bfloat16)
    returned = lax.all_to_all(
        expert_out.reshape(-1, capacity, model_width), "req", 0, 0, tiled=True
    )
    fetched = jnp.dot(
        pick.T.astype(jnp.bfloat16),
        returned.reshape(slot_count, model_width),
        preferred_element_type=jnp.float32,
    ).reshape(own_count, top_count, model_width)
    picked = jnp.take_along_axis(logits, own_routes, axis=1)
    gate_values = jax.nn.sigmoid(picked)
    weights = gate_values / jnp.sum(gate_values, axis=1, keepdims=True)
    moe_out = jnp.sum(weights[..., None] * fetched, axis=1)
    final_rows = (mid_stream.astype(jnp.float32) + moe_out).astype(jnp.bfloat16)
    return (final_rows[None], new_keys[None], new_values[None])


def solution(mesh):
    in_specs = (
        P("req", "hid", None),
        P("req", "hid", None),
        P("req", "hid", None),
        P("req", "hid", None),
        P("req"),
        P("req", None, None),
        P(),
        P(),
        P(),
        P(),
        P(),
        P(),
        P("req", None, None, "hid"),
        P("req", "hid", None),
    )
    out_specs = (P("req", "hid", None), P("req", "hid", None), P("req", "hid", None))
    return jax.shard_map(body, mesh=mesh, in_specs=in_specs, out_specs=out_specs, check_vma=False)
```

```python
import jax
import jax.numpy as jnp
from jax import lax
from jax.sharding import PartitionSpec as P
from jax.experimental import pallas as pl
from jax.experimental.pallas import tpu as pltpu
import functools

QH = 12
KVH = 2
HD = 128


EPS = 1e-06
MASKED_SCORE = -1e30
KEY_BLOCK = 512


def normalize(row_data, gain_vector):
    row_data = row_data.astype(jnp.float32)
    return (
        row_data
        * lax.rsqrt(jnp.mean(row_data * row_data, axis=-1, keepdims=True) + EPS)
        * gain_vector
    )


def absorb(state_now, grouped, key_rows, value_rows, visible):
    row_max, totals, accumulated = state_now
    scores = jnp.einsum(
        "tgsd,kgd->gstk", grouped, key_rows.reshape(-1, KVH, HD), preferred_element_type=jnp.float32
    ) * HD ** (-0.5)
    scores = jnp.where(visible, scores, MASKED_SCORE)
    new_max = jnp.maximum(row_max, jnp.max(scores, axis=-1))
    weights = jnp.where(visible, jnp.exp(scores - new_max[..., None]), 0.0)
    rescale = jnp.exp(row_max - new_max)
    totals = totals * rescale + jnp.sum(weights, axis=-1)
    accumulated = accumulated * rescale[..., None] + jnp.einsum(
        "gstk,kgd->gstd",
        weights.astype(jnp.bfloat16),
        value_rows.reshape(-1, KVH, HD),
        preferred_element_type=jnp.float32,
    )
    return (new_max, totals, accumulated)


def cache_block(state_now, grouped, key_rows, value_rows, first_pos, length):
    positions = first_pos + jnp.arange(key_rows.shape[0], dtype=jnp.int32)
    visible = (positions < length)[None, :]
    return lax.cond(
        first_pos < length,
        lambda current: absorb(current, grouped, key_rows, value_rows, visible),
        lambda current: current,
        state_now,
    )


def span_block(state_now, grouped, key_rows, value_rows, first_pos, query_pos):
    positions = first_pos + jnp.arange(key_rows.shape[0], dtype=jnp.int32)
    visible = positions[None, :] <= query_pos[:, None]
    return lax.cond(
        first_pos <= query_pos[-1],
        lambda current: absorb(current, grouped, key_rows, value_rows, visible),
        lambda current: current,
        state_now,
    )


def block_size(extent):
    return max(min(KEY_BLOCK, extent), extent // 8)


def empty_state(query_count):
    group_size = QH // KVH
    return (
        jnp.full((KVH, group_size, query_count), MASKED_SCORE, jnp.float32),
        jnp.zeros((KVH, group_size, query_count), jnp.float32),
        jnp.zeros((KVH, group_size, query_count, HD), jnp.float32),
    )


def attention_kernel(token_count, scalars, q_ref, k_ref, v_ref, o_ref, m_ref, l_ref, acc_ref):
    length = scalars[0]
    hid_index = scalars[1]
    parts, part_rows, _ = k_ref.shape
    rows = q_ref.shape[1]
    cache_rows = part_rows - token_count
    q = q_ref[0]
    m_ref[...] = jnp.full(m_ref.shape, MASKED_SCORE, jnp.float32)
    l_ref[...] = jnp.zeros(l_ref.shape, jnp.float32)
    acc_ref[...] = jnp.zeros(acc_ref.shape, jnp.float32)
    blocks = []
    for part in range(parts):
        for first in range(0, cache_rows, KEY_BLOCK):
            blocks.append((part, first, min(KEY_BLOCK, cache_rows - first), True))
        blocks.append((part, cache_rows, token_count, False))

    def live(part, first, is_cache):
        if is_cache:
            return part * cache_rows + first < length
        return part <= hid_index

    def visible(part, first, size, is_cache):
        if is_cache:
            pos = part * cache_rows + first + lax.broadcasted_iota(jnp.int32, (1, size), 1)
            return pos < length
        key_pos = part * token_count + lax.broadcasted_iota(jnp.int32, (1, size), 1)
        row_ids = lax.broadcasted_iota(jnp.int32, (rows, 1), 0)
        return key_pos <= hid_index * token_count + row_ids % token_count

    def scores(part, first, size):
        k = k_ref[part, pl.ds(first, size), :]
        raw = lax.dot_general(q, k, (((1,), (1,)), ((), ())), preferred_element_type=jnp.float32)
        return raw * HD ** (-0.5)

    for part, first, size, is_cache in blocks:

        @pl.when(live(part, first, is_cache))
        def _():
            s = jnp.where(visible(part, first, size, is_cache), scores(part, first, size), MASKED_SCORE)
            m_ref[...] = jnp.maximum(m_ref[...], jnp.max(s, axis=-1, keepdims=True))

    for part, first, size, is_cache in blocks:

        @pl.when(live(part, first, is_cache))
        def _():
            s = scores(part, first, size)
            w = jnp.where(visible(part, first, size, is_cache), jnp.exp(s - m_ref[...]), 0.0)
            l_ref[...] += jnp.sum(w, axis=-1, keepdims=True)
            v = v_ref[part, pl.ds(first, size), :]
            acc_ref[...] += jnp.dot(w.astype(jnp.bfloat16), v, preferred_element_type=jnp.float32)

    o_ref[0] = (acc_ref[...] / l_ref[...]).astype(o_ref.dtype)


def attention(grouped, all_keys, all_values, length, hid_index, token_count, interpret=False):
    groups, rows, head = grouped.shape
    parts, part_rows, _ = all_keys.shape
    scalars = jnp.stack([length, hid_index]).astype(jnp.int32)
    kv_spec = pl.BlockSpec((parts, part_rows, head), lambda g, s: (0, 0, g))
    row_spec = pl.BlockSpec((1, rows, head), lambda g, s: (g, 0, 0))
    return pl.pallas_call(
        functools.partial(attention_kernel, token_count),
        out_shape=jax.ShapeDtypeStruct((groups, rows, head), jnp.bfloat16),
        grid_spec=pltpu.PrefetchScalarGridSpec(
            num_scalar_prefetch=1,
            grid=(groups,),
            in_specs=[row_spec, kv_spec, kv_spec],
            out_specs=row_spec,
            scratch_shapes=[
                pltpu.VMEM((rows, 1), jnp.float32),
                pltpu.VMEM((rows, 1), jnp.float32),
                pltpu.VMEM((rows, head), jnp.float32),
            ],
        ),
        interpret=interpret,
    )(scalars, grouped, all_keys, all_values)


def expert_activation(row_data, gate_weights):
    gate_out = jnp.dot(row_data, gate_weights[0], preferred_element_type=jnp.float32)
    up_out = jnp.dot(row_data, gate_weights[1], preferred_element_type=jnp.float32)
    return (jnp.maximum(gate_out, 0.0) * up_out).astype(jnp.bfloat16)


def body(
    hidden_in,
    queries,
    cache_keys,
    cache_values,
    lengths,
    routes,
    attn_gain,
    key_proj,
    value_proj,
    out_proj,
    moe_gain,
    router,
    gate_up,
    down_proj,
):
    own_count = hidden_in.shape[1]
    model_width = hidden_in.shape[2]
    hid_index = lax.axis_index("hid")
    hid_count = lax.axis_size("hid")
    group_size = QH // KVH
    normed = normalize(hidden_in[0], attn_gain).astype(jnp.bfloat16)
    new_keys = jnp.dot(normed, key_proj, preferred_element_type=jnp.float32).astype(jnp.bfloat16)
    new_values = jnp.dot(normed, value_proj, preferred_element_type=jnp.float32).astype(jnp.bfloat16)
    length = lengths[0]
    cache_local = cache_keys.shape[1]
    all_keys = lax.all_gather(jnp.concatenate([cache_keys[0], new_keys], axis=0), "hid", axis=0)
    all_values = lax.all_gather(jnp.concatenate([cache_values[0], new_values], axis=0), "hid", axis=0)
    all_weights = lax.all_gather(
        jnp.concatenate([gate_up[0], down_proj[0].T[None]], axis=0), "hid", axis=0
    )
    grouped = (
        queries[0]
        .reshape(own_count, KVH, group_size, HD)
        .transpose(1, 2, 0, 3)
        .reshape(KVH, group_size * own_count, HD)
    )
    attended = (
        attention(grouped, all_keys, all_values, length, hid_index, own_count)
        .reshape(KVH, group_size, own_count, HD)
        .transpose(2, 0, 1, 3)
        .reshape(own_count, QH * HD)
    )
    mid_stream = (
        hidden_in[0].astype(jnp.float32)
        + jnp.dot(attended, out_proj, preferred_element_type=jnp.float32)
    ).astype(jnp.bfloat16)
    moe_in = normalize(mid_stream, moe_gain).astype(jnp.bfloat16)
    logits = jnp.dot(moe_in, router, preferred_element_type=jnp.float32)
    expert_count = router.shape[1]
    top_count = routes.shape[2]
    capacity = 2 * own_count * top_count // expert_count
    own_routes = lax.dynamic_slice_in_dim(routes[0], hid_index * own_count, own_count, axis=0)
    flat_routes = own_routes.reshape(-1)
    onehot = (flat_routes[:, None] == jnp.arange(expert_count, dtype=jnp.int32)[None, :]).astype(
        jnp.int32
    )
    slot_ids = jnp.sum((jnp.cumsum(onehot, axis=0) - 1) * onehot, axis=-1)
    targets = flat_routes * capacity + slot_ids
    slot_count = expert_count * capacity
    pick = targets[None, :] == jnp.arange(slot_count, dtype=jnp.int32)[:, None]
    pick_rows = jnp.any(pick.reshape(slot_count, own_count, top_count), axis=-1).astype(jnp.bfloat16)
    send_rows = jnp.dot(pick_rows, moe_in, preferred_element_type=jnp.float32).astype(jnp.bfloat16)
    grouped_rows = lax.all_to_all(
        send_rows.reshape(expert_count, capacity, model_width), "req", 0, 0, tiled=True
    )
    flat_rows = grouped_rows.reshape(-1, model_width)
    gate_out = jnp.einsum(
        "nd,hdf->hnf", flat_rows, all_weights[:, 0], preferred_element_type=jnp.float32
    )
    up_out = jnp.einsum(
        "nd,hdf->hnf", flat_rows, all_weights[:, 1], preferred_element_type=jnp.float32
    )
    activation = (jnp.maximum(gate_out, 0.0) * up_out).astype(jnp.bfloat16)
    partials = jnp.einsum(
        "hnf,hdf->hnd", activation, all_weights[:, 2], preferred_element_type=jnp.float32
    ).astype(jnp.bfloat16)
    expert_out = jnp.sum(partials.astype(jnp.float32), axis=0).astype(jnp.bfloat16)
    returned = lax.all_to_all(
        expert_out.reshape(-1, capacity, model_width), "req", 0, 0, tiled=True
    )
    fetched = jnp.dot(
        pick.T.astype(jnp.bfloat16),
        returned.reshape(slot_count, model_width),
        preferred_element_type=jnp.float32,
    ).reshape(own_count, top_count, model_width)
    picked = jnp.take_along_axis(logits, own_routes, axis=1)
    gate_values = jax.nn.sigmoid(picked)
    weights = gate_values / jnp.sum(gate_values, axis=1, keepdims=True)
    moe_out = jnp.sum(weights[..., None] * fetched, axis=1)
    final_rows = (mid_stream.astype(jnp.float32) + moe_out).astype(jnp.bfloat16)
    return (final_rows[None], new_keys[None], new_values[None])


def solution(mesh):
    in_specs = (
        P("req", "hid", None),
        P("req", "hid", None),
        P("req", "hid", None),
        P("req", "hid", None),
        P("req"),
        P("req", None, None),
        P(),
        P(),
        P(),
        P(),
        P(),
        P(),
        P("req", None, None, "hid"),
        P("req", "hid", None),
    )
    out_specs = (P("req", "hid", None), P("req", "hid", None), P("req", "hid", None))
    return jax.shard_map(body, mesh=mesh, in_specs=in_specs, out_specs=out_specs, check_vma=False)
```

```python
import jax
import jax.numpy as jnp
from jax import lax
from jax.sharding import PartitionSpec as P
from jax.experimental import pallas as pl
from jax.experimental.pallas import tpu as pltpu
import functools

QH = 12
KVH = 2
HD = 128


EPS = 1e-06
MASKED_SCORE = -1e30
KEY_BLOCK = 512


def normalize(row_data, gain_vector):
    row_data = row_data.astype(jnp.float32)
    return (
        row_data
        * lax.rsqrt(jnp.mean(row_data * row_data, axis=-1, keepdims=True) + EPS)
        * gain_vector
    )


def absorb(state_now, grouped, key_rows, value_rows, visible):
    row_max, totals, accumulated = state_now
    scores = jnp.einsum(
        "tgsd,kgd->gstk", grouped, key_rows.reshape(-1, KVH, HD), preferred_element_type=jnp.float32
    ) * HD ** (-0.5)
    scores = jnp.where(visible, scores, MASKED_SCORE)
    new_max = jnp.maximum(row_max, jnp.max(scores, axis=-1))
    weights = jnp.where(visible, jnp.exp(scores - new_max[..., None]), 0.0)
    rescale = jnp.exp(row_max - new_max)
    totals = totals * rescale + jnp.sum(weights, axis=-1)
    accumulated = accumulated * rescale[..., None] + jnp.einsum(
        "gstk,kgd->gstd",
        weights.astype(jnp.bfloat16),
        value_rows.reshape(-1, KVH, HD),
        preferred_element_type=jnp.float32,
    )
    return (new_max, totals, accumulated)


def cache_block(state_now, grouped, key_rows, value_rows, first_pos, length):
    positions = first_pos + jnp.arange(key_rows.shape[0], dtype=jnp.int32)
    visible = (positions < length)[None, :]
    return lax.cond(
        first_pos < length,
        lambda current: absorb(current, grouped, key_rows, value_rows, visible),
        lambda current: current,
        state_now,
    )


def span_block(state_now, grouped, key_rows, value_rows, first_pos, query_pos):
    positions = first_pos + jnp.arange(key_rows.shape[0], dtype=jnp.int32)
    visible = positions[None, :] <= query_pos[:, None]
    return lax.cond(
        first_pos <= query_pos[-1],
        lambda current: absorb(current, grouped, key_rows, value_rows, visible),
        lambda current: current,
        state_now,
    )


def block_size(extent):
    return max(min(KEY_BLOCK, extent), extent // 8)


def empty_state(query_count):
    group_size = QH // KVH
    return (
        jnp.full((KVH, group_size, query_count), MASKED_SCORE, jnp.float32),
        jnp.zeros((KVH, group_size, query_count), jnp.float32),
        jnp.zeros((KVH, group_size, query_count, HD), jnp.float32),
    )


def attention_kernel(token_count, scalars, q_ref, k_ref, v_ref, o_ref, m_ref, l_ref, acc_ref, s_ref):
    length = scalars[0]
    hid_index = scalars[1]
    parts, part_rows, _ = k_ref.shape
    rows = q_ref.shape[1]
    cache_rows = part_rows - token_count
    q = q_ref[0]
    m_ref[...] = jnp.full(m_ref.shape, MASKED_SCORE, jnp.float32)
    l_ref[...] = jnp.zeros(l_ref.shape, jnp.float32)
    acc_ref[...] = jnp.zeros(acc_ref.shape, jnp.float32)
    blocks = []
    for part in range(parts):
        for first in range(0, cache_rows, KEY_BLOCK):
            blocks.append((part, first, min(KEY_BLOCK, cache_rows - first), True))
        blocks.append((part, cache_rows, token_count, False))

    def live(part, first, is_cache):
        if is_cache:
            return part * cache_rows + first < length
        return part <= hid_index

    def visible(part, first, size, is_cache):
        if is_cache:
            pos = part * cache_rows + first + lax.broadcasted_iota(jnp.int32, (1, size), 1)
            return pos < length
        key_pos = part * token_count + lax.broadcasted_iota(jnp.int32, (1, size), 1)
        row_ids = lax.broadcasted_iota(jnp.int32, (rows, 1), 0)
        return key_pos <= hid_index * token_count + row_ids % token_count

    for part, first, size, is_cache in blocks:

        @pl.when(live(part, first, is_cache))
        def _():
            k = k_ref[part, pl.ds(first, size), :]
            raw = lax.dot_general(q, k, (((1,), (1,)), ((), ())), preferred_element_type=jnp.float32)
            s = jnp.where(visible(part, first, size, is_cache), raw * HD ** (-0.5), MASKED_SCORE)
            s_ref[:, pl.ds(part * part_rows + first, size)] = s
            m_ref[...] = jnp.maximum(m_ref[...], jnp.max(s, axis=-1, keepdims=True))

    for part, first, size, is_cache in blocks:

        @pl.when(live(part, first, is_cache))
        def _():
            w = jnp.exp(s_ref[:, pl.ds(part * part_rows + first, size)] - m_ref[...])
            l_ref[...] += jnp.sum(w, axis=-1, keepdims=True)
            v = v_ref[part, pl.ds(first, size), :]
            acc_ref[...] += jnp.dot(w.astype(jnp.bfloat16), v, preferred_element_type=jnp.float32)

    o_ref[0] = (acc_ref[...] / l_ref[...]).astype(o_ref.dtype)


def attention(grouped, all_kv, length, hid_index, token_count, interpret=False):
    groups, rows, head = grouped.shape
    parts, part_rows, _ = all_kv.shape
    scalars = jnp.stack([length, hid_index]).astype(jnp.int32)
    k_spec = pl.BlockSpec((parts, part_rows, head), lambda g, s: (0, 0, g))
    v_spec = pl.BlockSpec((parts, part_rows, head), lambda g, s: (0, 0, groups + g))
    row_spec = pl.BlockSpec((1, rows, head), lambda g, s: (g, 0, 0))
    return pl.pallas_call(
        functools.partial(attention_kernel, token_count),
        out_shape=jax.ShapeDtypeStruct((groups, rows, head), jnp.bfloat16),
        grid_spec=pltpu.PrefetchScalarGridSpec(
            num_scalar_prefetch=1,
            grid=(groups,),
            in_specs=[row_spec, k_spec, v_spec],
            out_specs=row_spec,
            scratch_shapes=[
                pltpu.VMEM((rows, 1), jnp.float32),
                pltpu.VMEM((rows, 1), jnp.float32),
                pltpu.VMEM((rows, head), jnp.float32),
                pltpu.VMEM((rows, parts * part_rows), jnp.float32),
            ],
        ),
        interpret=interpret,
    )(scalars, grouped, all_kv, all_kv)


def expert_activation(row_data, gate_weights):
    gate_out = jnp.dot(row_data, gate_weights[0], preferred_element_type=jnp.float32)
    up_out = jnp.dot(row_data, gate_weights[1], preferred_element_type=jnp.float32)
    return (jnp.maximum(gate_out, 0.0) * up_out).astype(jnp.bfloat16)


def body(
    hidden_in,
    queries,
    cache_keys,
    cache_values,
    lengths,
    routes,
    attn_gain,
    key_proj,
    value_proj,
    out_proj,
    moe_gain,
    router,
    gate_up,
    down_proj,
):
    own_count = hidden_in.shape[1]
    model_width = hidden_in.shape[2]
    hid_index = lax.axis_index("hid")
    hid_count = lax.axis_size("hid")
    group_size = QH // KVH
    normed = normalize(hidden_in[0], attn_gain).astype(jnp.bfloat16)
    new_keys = jnp.dot(normed, key_proj, preferred_element_type=jnp.float32).astype(jnp.bfloat16)
    new_values = jnp.dot(normed, value_proj, preferred_element_type=jnp.float32).astype(jnp.bfloat16)
    length = lengths[0]
    cache_local = cache_keys.shape[1]
    all_kv = lax.all_gather(
        jnp.concatenate(
            [
                jnp.concatenate([cache_keys[0], new_keys], axis=0),
                jnp.concatenate([cache_values[0], new_values], axis=0),
            ],
            axis=1,
        ),
        "hid",
        axis=0,
    )
    all_weights = lax.all_gather(
        jnp.concatenate([gate_up[0], down_proj[0].T[None]], axis=0), "hid", axis=0
    )
    grouped = (
        queries[0]
        .reshape(own_count, KVH, group_size, HD)
        .transpose(1, 2, 0, 3)
        .reshape(KVH, group_size * own_count, HD)
    )
    attended = (
        attention(grouped, all_kv, length, hid_index, own_count)
        .reshape(KVH, group_size, own_count, HD)
        .transpose(2, 0, 1, 3)
        .reshape(own_count, QH * HD)
    )
    mid_stream = (
        hidden_in[0].astype(jnp.float32)
        + jnp.dot(attended, out_proj, preferred_element_type=jnp.float32)
    ).astype(jnp.bfloat16)
    moe_in = normalize(mid_stream, moe_gain).astype(jnp.bfloat16)
    logits = jnp.dot(moe_in, router, preferred_element_type=jnp.float32)
    expert_count = router.shape[1]
    top_count = routes.shape[2]
    capacity = 2 * own_count * top_count // expert_count
    own_routes = lax.dynamic_slice_in_dim(routes[0], hid_index * own_count, own_count, axis=0)
    flat_routes = own_routes.reshape(-1)
    onehot = (flat_routes[:, None] == jnp.arange(expert_count, dtype=jnp.int32)[None, :]).astype(
        jnp.int32
    )
    slot_ids = jnp.sum((jnp.cumsum(onehot, axis=0) - 1) * onehot, axis=-1)
    targets = flat_routes * capacity + slot_ids
    slot_count = expert_count * capacity
    pick = targets[None, :] == jnp.arange(slot_count, dtype=jnp.int32)[:, None]
    pick_rows = jnp.any(pick.reshape(slot_count, own_count, top_count), axis=-1).astype(jnp.bfloat16)
    send_rows = jnp.dot(pick_rows, moe_in, preferred_element_type=jnp.float32).astype(jnp.bfloat16)
    grouped_rows = lax.all_to_all(
        send_rows.reshape(expert_count, capacity, model_width), "req", 0, 0, tiled=True
    )
    flat_rows = grouped_rows.reshape(-1, model_width)
    gate_out = jnp.einsum(
        "nd,hdf->hnf", flat_rows, all_weights[:, 0], preferred_element_type=jnp.float32
    )
    up_out = jnp.einsum(
        "nd,hdf->hnf", flat_rows, all_weights[:, 1], preferred_element_type=jnp.float32
    )
    activation = (jnp.maximum(gate_out, 0.0) * up_out).astype(jnp.bfloat16)
    partials = jnp.einsum(
        "hnf,hdf->hnd", activation, all_weights[:, 2], preferred_element_type=jnp.float32
    ).astype(jnp.bfloat16)
    expert_out = jnp.sum(partials.astype(jnp.float32), axis=0).astype(jnp.bfloat16)
    returned = lax.all_to_all(
        expert_out.reshape(-1, capacity, model_width), "req", 0, 0, tiled=True
    )
    fetched = jnp.dot(
        pick.T.astype(jnp.bfloat16),
        returned.reshape(slot_count, model_width),
        preferred_element_type=jnp.float32,
    ).reshape(own_count, top_count, model_width)
    picked = jnp.take_along_axis(logits, own_routes, axis=1)
    gate_values = jax.nn.sigmoid(picked)
    weights = gate_values / jnp.sum(gate_values, axis=1, keepdims=True)
    moe_out = jnp.sum(weights[..., None] * fetched, axis=1)
    final_rows = (mid_stream.astype(jnp.float32) + moe_out).astype(jnp.bfloat16)
    return (final_rows[None], new_keys[None], new_values[None])


def solution(mesh):
    in_specs = (
        P("req", "hid", None),
        P("req", "hid", None),
        P("req", "hid", None),
        P("req", "hid", None),
        P("req"),
        P("req", None, None),
        P(),
        P(),
        P(),
        P(),
        P(),
        P(),
        P("req", None, None, "hid"),
        P("req", "hid", None),
    )
    out_specs = (P("req", "hid", None), P("req", "hid", None), P("req", "hid", None))
    return jax.shard_map(body, mesh=mesh, in_specs=in_specs, out_specs=out_specs, check_vma=False)
```

```python
import jax
import jax.numpy as jnp
from jax import lax
from jax.sharding import PartitionSpec as P
from jax.experimental import pallas as pl
from jax.experimental.pallas import tpu as pltpu
import functools

QH = 12
KVH = 2
HD = 128


EPS = 1e-06
MASKED_SCORE = -1e30
KEY_BLOCK = 512


def normalize(row_data, gain_vector):
    row_data = row_data.astype(jnp.float32)
    return (
        row_data
        * lax.rsqrt(jnp.mean(row_data * row_data, axis=-1, keepdims=True) + EPS)
        * gain_vector
    )


def absorb(state_now, grouped, key_rows, value_rows, visible):
    row_max, totals, accumulated = state_now
    scores = jnp.einsum(
        "tgsd,kgd->gstk", grouped, key_rows.reshape(-1, KVH, HD), preferred_element_type=jnp.float32
    ) * HD ** (-0.5)
    scores = jnp.where(visible, scores, MASKED_SCORE)
    new_max = jnp.maximum(row_max, jnp.max(scores, axis=-1))
    weights = jnp.where(visible, jnp.exp(scores - new_max[..., None]), 0.0)
    rescale = jnp.exp(row_max - new_max)
    totals = totals * rescale + jnp.sum(weights, axis=-1)
    accumulated = accumulated * rescale[..., None] + jnp.einsum(
        "gstk,kgd->gstd",
        weights.astype(jnp.bfloat16),
        value_rows.reshape(-1, KVH, HD),
        preferred_element_type=jnp.float32,
    )
    return (new_max, totals, accumulated)


def cache_block(state_now, grouped, key_rows, value_rows, first_pos, length):
    positions = first_pos + jnp.arange(key_rows.shape[0], dtype=jnp.int32)
    visible = (positions < length)[None, :]
    return lax.cond(
        first_pos < length,
        lambda current: absorb(current, grouped, key_rows, value_rows, visible),
        lambda current: current,
        state_now,
    )


def span_block(state_now, grouped, key_rows, value_rows, first_pos, query_pos):
    positions = first_pos + jnp.arange(key_rows.shape[0], dtype=jnp.int32)
    visible = positions[None, :] <= query_pos[:, None]
    return lax.cond(
        first_pos <= query_pos[-1],
        lambda current: absorb(current, grouped, key_rows, value_rows, visible),
        lambda current: current,
        state_now,
    )


def block_size(extent):
    return max(min(KEY_BLOCK, extent), extent // 8)


def empty_state(query_count):
    group_size = QH // KVH
    return (
        jnp.full((KVH, group_size, query_count), MASKED_SCORE, jnp.float32),
        jnp.zeros((KVH, group_size, query_count), jnp.float32),
        jnp.zeros((KVH, group_size, query_count, HD), jnp.float32),
    )


def attention_kernel(token_count, scalars, q_ref, k_ref, v_ref, o_ref, m_ref, l_ref, acc_ref, s_ref):
    length = scalars[0]
    hid_index = scalars[1]
    parts, part_rows, _ = k_ref.shape
    rows = q_ref.shape[1]
    cache_rows = part_rows - token_count
    q = q_ref[0]
    m_ref[...] = jnp.full(m_ref.shape, MASKED_SCORE, jnp.float32)
    l_ref[...] = jnp.zeros(l_ref.shape, jnp.float32)
    acc_ref[...] = jnp.zeros(acc_ref.shape, jnp.float32)
    blocks = []
    for part in range(parts):
        for first in range(0, cache_rows, KEY_BLOCK):
            blocks.append((part, first, min(KEY_BLOCK, cache_rows - first), True))
        blocks.append((part, cache_rows, token_count, False))

    def live(part, first, size, is_cache):
        if is_cache:
            return part * cache_rows + first < length
        return part <= hid_index

    def whole(part, first, size, is_cache):
        if is_cache:
            return part * cache_rows + first + size <= length
        return part < hid_index

    def visible(part, first, size, is_cache):
        if is_cache:
            pos = part * cache_rows + first + lax.broadcasted_iota(jnp.int32, (1, size), 1)
            return pos < length
        key_pos = part * token_count + lax.broadcasted_iota(jnp.int32, (1, size), 1)
        row_ids = lax.broadcasted_iota(jnp.int32, (rows, 1), 0)
        return key_pos <= hid_index * token_count + row_ids % token_count

    def first_pass(part, first, size, is_cache, masked):
        k = k_ref[part, pl.ds(first, size), :]
        raw = lax.dot_general(q, k, (((1,), (1,)), ((), ())), preferred_element_type=jnp.float32)
        s = raw * HD ** (-0.5)
        if masked:
            s = jnp.where(visible(part, first, size, is_cache), s, MASKED_SCORE)
        s_ref[:, pl.ds(part * part_rows + first, size)] = s
        m_ref[...] = jnp.maximum(m_ref[...], jnp.max(s, axis=-1, keepdims=True))

    for part, first, size, is_cache in blocks:
        is_whole = whole(part, first, size, is_cache)
        pl.when(is_whole)(functools.partial(first_pass, part, first, size, is_cache, False))
        pl.when(jnp.logical_and(live(part, first, size, is_cache), jnp.logical_not(is_whole)))(
            functools.partial(first_pass, part, first, size, is_cache, True)
        )

    for part, first, size, is_cache in blocks:

        @pl.when(live(part, first, size, is_cache))
        def _():
            w = jnp.exp(s_ref[:, pl.ds(part * part_rows + first, size)] - m_ref[...])
            l_ref[...] += jnp.sum(w, axis=-1, keepdims=True)
            v = v_ref[part, pl.ds(first, size), :]
            acc_ref[...] += jnp.dot(w.astype(jnp.bfloat16), v, preferred_element_type=jnp.float32)

    o_ref[0] = (acc_ref[...] / l_ref[...]).astype(o_ref.dtype)


def attention(grouped, all_kv, length, hid_index, token_count, interpret=False):
    groups, rows, head = grouped.shape
    parts, part_rows, _ = all_kv.shape
    scalars = jnp.stack([length, hid_index]).astype(jnp.int32)
    k_spec = pl.BlockSpec((parts, part_rows, head), lambda g, s: (0, 0, g))
    v_spec = pl.BlockSpec((parts, part_rows, head), lambda g, s: (0, 0, groups + g))
    row_spec = pl.BlockSpec((1, rows, head), lambda g, s: (g, 0, 0))
    return pl.pallas_call(
        functools.partial(attention_kernel, token_count),
        out_shape=jax.ShapeDtypeStruct((groups, rows, head), jnp.bfloat16),
        grid_spec=pltpu.PrefetchScalarGridSpec(
            num_scalar_prefetch=1,
            grid=(groups,),
            in_specs=[row_spec, k_spec, v_spec],
            out_specs=row_spec,
            scratch_shapes=[
                pltpu.VMEM((rows, 1), jnp.float32),
                pltpu.VMEM((rows, 1), jnp.float32),
                pltpu.VMEM((rows, head), jnp.float32),
                pltpu.VMEM((rows, parts * part_rows), jnp.float32),
            ],
        ),
        interpret=interpret,
    )(scalars, grouped, all_kv, all_kv)


def expert_activation(row_data, gate_weights):
    gate_out = jnp.dot(row_data, gate_weights[0], preferred_element_type=jnp.float32)
    up_out = jnp.dot(row_data, gate_weights[1], preferred_element_type=jnp.float32)
    return (jnp.maximum(gate_out, 0.0) * up_out).astype(jnp.bfloat16)


def body(
    hidden_in,
    queries,
    cache_keys,
    cache_values,
    lengths,
    routes,
    attn_gain,
    key_proj,
    value_proj,
    out_proj,
    moe_gain,
    router,
    gate_up,
    down_proj,
):
    own_count = hidden_in.shape[1]
    model_width = hidden_in.shape[2]
    hid_index = lax.axis_index("hid")
    hid_count = lax.axis_size("hid")
    group_size = QH // KVH
    normed = normalize(hidden_in[0], attn_gain).astype(jnp.bfloat16)
    new_keys = jnp.dot(normed, key_proj, preferred_element_type=jnp.float32).astype(jnp.bfloat16)
    new_values = jnp.dot(normed, value_proj, preferred_element_type=jnp.float32).astype(jnp.bfloat16)
    length = lengths[0]
    cache_local = cache_keys.shape[1]
    all_kv = lax.all_gather(
        jnp.concatenate(
            [
                jnp.concatenate([cache_keys[0], new_keys], axis=0),
                jnp.concatenate([cache_values[0], new_values], axis=0),
            ],
            axis=1,
        ),
        "hid",
        axis=0,
    )
    all_weights = lax.all_gather(
        jnp.concatenate([gate_up[0], down_proj[0].T[None]], axis=0), "hid", axis=0
    )
    grouped = (
        queries[0]
        .reshape(own_count, KVH, group_size, HD)
        .transpose(1, 2, 0, 3)
        .reshape(KVH, group_size * own_count, HD)
    )
    attended = (
        attention(grouped, all_kv, length, hid_index, own_count)
        .reshape(KVH, group_size, own_count, HD)
        .transpose(2, 0, 1, 3)
        .reshape(own_count, QH * HD)
    )
    mid_stream = (
        hidden_in[0].astype(jnp.float32)
        + jnp.dot(attended, out_proj, preferred_element_type=jnp.float32)
    ).astype(jnp.bfloat16)
    moe_in = normalize(mid_stream, moe_gain).astype(jnp.bfloat16)
    logits = jnp.dot(moe_in, router, preferred_element_type=jnp.float32)
    expert_count = router.shape[1]
    top_count = routes.shape[2]
    capacity = 2 * own_count * top_count // expert_count
    own_routes = lax.dynamic_slice_in_dim(routes[0], hid_index * own_count, own_count, axis=0)
    flat_routes = own_routes.reshape(-1)
    onehot = (flat_routes[:, None] == jnp.arange(expert_count, dtype=jnp.int32)[None, :]).astype(
        jnp.int32
    )
    slot_ids = jnp.sum((jnp.cumsum(onehot, axis=0) - 1) * onehot, axis=-1)
    targets = flat_routes * capacity + slot_ids
    slot_count = expert_count * capacity
    pick = targets[None, :] == jnp.arange(slot_count, dtype=jnp.int32)[:, None]
    pick_rows = jnp.any(pick.reshape(slot_count, own_count, top_count), axis=-1).astype(jnp.bfloat16)
    send_rows = jnp.dot(pick_rows, moe_in, preferred_element_type=jnp.float32).astype(jnp.bfloat16)
    grouped_rows = lax.all_to_all(
        send_rows.reshape(expert_count, capacity, model_width), "req", 0, 0, tiled=True
    )
    flat_rows = grouped_rows.reshape(-1, model_width)
    gate_out = jnp.einsum(
        "nd,hdf->hnf", flat_rows, all_weights[:, 0], preferred_element_type=jnp.float32
    )
    up_out = jnp.einsum(
        "nd,hdf->hnf", flat_rows, all_weights[:, 1], preferred_element_type=jnp.float32
    )
    activation = (jnp.maximum(gate_out, 0.0) * up_out).astype(jnp.bfloat16)
    partials = jnp.einsum(
        "hnf,hdf->hnd", activation, all_weights[:, 2], preferred_element_type=jnp.float32
    ).astype(jnp.bfloat16)
    expert_out = jnp.sum(partials.astype(jnp.float32), axis=0).astype(jnp.bfloat16)
    returned = lax.all_to_all(
        expert_out.reshape(-1, capacity, model_width), "req", 0, 0, tiled=True
    )
    fetched = jnp.dot(
        pick.T.astype(jnp.bfloat16),
        returned.reshape(slot_count, model_width),
        preferred_element_type=jnp.float32,
    ).reshape(own_count, top_count, model_width)
    picked = jnp.take_along_axis(logits, own_routes, axis=1)
    gate_values = jax.nn.sigmoid(picked)
    weights = gate_values / jnp.sum(gate_values, axis=1, keepdims=True)
    moe_out = jnp.sum(weights[..., None] * fetched, axis=1)
    final_rows = (mid_stream.astype(jnp.float32) + moe_out).astype(jnp.bfloat16)
    return (final_rows[None], new_keys[None], new_values[None])


def solution(mesh):
    in_specs = (
        P("req", "hid", None),
        P("req", "hid", None),
        P("req", "hid", None),
        P("req", "hid", None),
        P("req"),
        P("req", None, None),
        P(),
        P(),
        P(),
        P(),
        P(),
        P(),
        P("req", None, None, "hid"),
        P("req", "hid", None),
    )
    out_specs = (P("req", "hid", None), P("req", "hid", None), P("req", "hid", None))
    return jax.shard_map(body, mesh=mesh, in_specs=in_specs, out_specs=out_specs, check_vma=False)
```

```python
import jax
import jax.numpy as jnp
from jax import lax
from jax.sharding import PartitionSpec as P
from jax.experimental import pallas as pl
from jax.experimental.pallas import tpu as pltpu
import functools

QH = 12
KVH = 2
HD = 128


EPS = 1e-06
MASKED_SCORE = -1e30
KEY_BLOCK = 512


def normalize(row_data, gain_vector):
    row_data = row_data.astype(jnp.float32)
    return (
        row_data
        * lax.rsqrt(jnp.mean(row_data * row_data, axis=-1, keepdims=True) + EPS)
        * gain_vector
    )


def absorb(state_now, grouped, key_rows, value_rows, visible):
    row_max, totals, accumulated = state_now
    scores = jnp.einsum(
        "tgsd,kgd->gstk", grouped, key_rows.reshape(-1, KVH, HD), preferred_element_type=jnp.float32
    ) * HD ** (-0.5)
    scores = jnp.where(visible, scores, MASKED_SCORE)
    new_max = jnp.maximum(row_max, jnp.max(scores, axis=-1))
    weights = jnp.where(visible, jnp.exp(scores - new_max[..., None]), 0.0)
    rescale = jnp.exp(row_max - new_max)
    totals = totals * rescale + jnp.sum(weights, axis=-1)
    accumulated = accumulated * rescale[..., None] + jnp.einsum(
        "gstk,kgd->gstd",
        weights.astype(jnp.bfloat16),
        value_rows.reshape(-1, KVH, HD),
        preferred_element_type=jnp.float32,
    )
    return (new_max, totals, accumulated)


def cache_block(state_now, grouped, key_rows, value_rows, first_pos, length):
    positions = first_pos + jnp.arange(key_rows.shape[0], dtype=jnp.int32)
    visible = (positions < length)[None, :]
    return lax.cond(
        first_pos < length,
        lambda current: absorb(current, grouped, key_rows, value_rows, visible),
        lambda current: current,
        state_now,
    )


def span_block(state_now, grouped, key_rows, value_rows, first_pos, query_pos):
    positions = first_pos + jnp.arange(key_rows.shape[0], dtype=jnp.int32)
    visible = positions[None, :] <= query_pos[:, None]
    return lax.cond(
        first_pos <= query_pos[-1],
        lambda current: absorb(current, grouped, key_rows, value_rows, visible),
        lambda current: current,
        state_now,
    )


def block_size(extent):
    return max(min(KEY_BLOCK, extent), extent // 8)


def empty_state(query_count):
    group_size = QH // KVH
    return (
        jnp.full((KVH, group_size, query_count), MASKED_SCORE, jnp.float32),
        jnp.zeros((KVH, group_size, query_count), jnp.float32),
        jnp.zeros((KVH, group_size, query_count, HD), jnp.float32),
    )


def attention_kernel(token_count, scalars, q_ref, k_ref, v_ref, o_ref, m_ref, l_ref, acc_ref, s_ref):
    length = scalars[0]
    hid_index = scalars[1]
    parts, part_rows, _ = k_ref.shape
    rows = q_ref.shape[1]
    cache_rows = part_rows - token_count
    q = q_ref[0]
    m_ref[...] = jnp.full(m_ref.shape, MASKED_SCORE, jnp.float32)
    l_ref[...] = jnp.zeros(l_ref.shape, jnp.float32)
    acc_ref[...] = jnp.zeros(acc_ref.shape, jnp.float32)
    blocks = []
    for part in range(parts):
        for first in range(0, cache_rows, KEY_BLOCK):
            blocks.append((part, first, min(KEY_BLOCK, cache_rows - first), True))
        blocks.append((part, cache_rows, token_count, False))

    def live(part, first, size, is_cache):
        if is_cache:
            return part * cache_rows + first < length
        return part <= hid_index

    def whole(part, first, size, is_cache):
        if is_cache:
            return part * cache_rows + first + size <= length
        return part < hid_index

    def visible(part, first, size, is_cache):
        if is_cache:
            pos = part * cache_rows + first + lax.broadcasted_iota(jnp.int32, (1, size), 1)
            return pos < length
        key_pos = part * token_count + lax.broadcasted_iota(jnp.int32, (1, size), 1)
        row_ids = lax.broadcasted_iota(jnp.int32, (rows, 1), 0)
        return key_pos <= hid_index * token_count + row_ids % token_count

    def first_pass(part, first, size, is_cache, masked):
        k = k_ref[part, pl.ds(first, size), :]
        raw = lax.dot_general(q, k, (((1,), (1,)), ((), ())), preferred_element_type=jnp.float32)
        s = raw * HD ** (-0.5)
        if masked:
            s = jnp.where(visible(part, first, size, is_cache), s, MASKED_SCORE)
        s_ref[:, pl.ds(part * part_rows + first, size)] = s
        m_ref[...] = jnp.maximum(m_ref[...], jnp.max(s, axis=-1, keepdims=True))

    for part, first, size, is_cache in blocks:
        is_whole = whole(part, first, size, is_cache)
        pl.when(is_whole)(functools.partial(first_pass, part, first, size, is_cache, False))
        pl.when(jnp.logical_and(live(part, first, size, is_cache), jnp.logical_not(is_whole)))(
            functools.partial(first_pass, part, first, size, is_cache, True)
        )

    for part, first, size, is_cache in blocks:

        @pl.when(live(part, first, size, is_cache))
        def _():
            w = jnp.exp(s_ref[:, pl.ds(part * part_rows + first, size)] - m_ref[...])
            l_ref[...] += jnp.sum(w, axis=-1, keepdims=True)
            v = v_ref[part, pl.ds(first, size), :]
            acc_ref[...] += jnp.dot(w.astype(jnp.bfloat16), v, preferred_element_type=jnp.float32)

    o_ref[0] = (acc_ref[...] / l_ref[...]).astype(o_ref.dtype)


def attention(grouped, all_kv, length, hid_index, token_count, interpret=False):
    groups, rows, head = grouped.shape
    parts, part_rows, _ = all_kv.shape
    scalars = jnp.stack([length, hid_index]).astype(jnp.int32)
    k_spec = pl.BlockSpec((parts, part_rows, head), lambda g, s: (0, 0, g))
    v_spec = pl.BlockSpec((parts, part_rows, head), lambda g, s: (0, 0, groups + g))
    row_spec = pl.BlockSpec((1, rows, head), lambda g, s: (g, 0, 0))
    return pl.pallas_call(
        functools.partial(attention_kernel, token_count),
        out_shape=jax.ShapeDtypeStruct((groups, rows, head), jnp.bfloat16),
        grid_spec=pltpu.PrefetchScalarGridSpec(
            num_scalar_prefetch=1,
            grid=(groups,),
            in_specs=[row_spec, k_spec, v_spec],
            out_specs=row_spec,
            scratch_shapes=[
                pltpu.VMEM((rows, 1), jnp.float32),
                pltpu.VMEM((rows, 1), jnp.float32),
                pltpu.VMEM((rows, head), jnp.float32),
                pltpu.VMEM((rows, parts * part_rows), jnp.float32),
            ],
        ),
        interpret=interpret,
    )(scalars, grouped, all_kv, all_kv)


def expert_activation(row_data, gate_weights):
    gate_out = jnp.dot(row_data, gate_weights[0], preferred_element_type=jnp.float32)
    up_out = jnp.dot(row_data, gate_weights[1], preferred_element_type=jnp.float32)
    return (jnp.maximum(gate_out, 0.0) * up_out).astype(jnp.bfloat16)


def body(
    hidden_in,
    queries,
    cache_keys,
    cache_values,
    lengths,
    routes,
    attn_gain,
    key_proj,
    value_proj,
    out_proj,
    moe_gain,
    router,
    gate_up,
    down_proj,
):
    own_count = hidden_in.shape[1]
    model_width = hidden_in.shape[2]
    hid_index = lax.axis_index("hid")
    hid_count = lax.axis_size("hid")
    group_size = QH // KVH
    normed = normalize(hidden_in[0], attn_gain).astype(jnp.bfloat16)
    new_keys = jnp.dot(normed, key_proj, preferred_element_type=jnp.float32).astype(jnp.bfloat16)
    new_values = jnp.dot(normed, value_proj, preferred_element_type=jnp.float32).astype(jnp.bfloat16)
    length = lengths[0]
    cache_local = cache_keys.shape[1]
    all_kv = lax.all_gather(
        jnp.concatenate(
            [
                jnp.concatenate([cache_keys[0], new_keys], axis=0),
                jnp.concatenate([cache_values[0], new_values], axis=0),
            ],
            axis=1,
        ),
        "hid",
        axis=0,
    )
    all_weights = lax.all_gather(
        jnp.concatenate([gate_up[0], down_proj[0].T[None]], axis=0), "hid", axis=0
    )
    grouped = (
        queries[0]
        .reshape(own_count, KVH, group_size, HD)
        .transpose(1, 2, 0, 3)
        .reshape(KVH, group_size * own_count, HD)
    )
    attended = (
        attention(grouped, all_kv, length, hid_index, own_count)
        .reshape(KVH, group_size, own_count, HD)
        .transpose(2, 0, 1, 3)
        .reshape(own_count, QH * HD)
    )
    mid_stream = (
        hidden_in[0].astype(jnp.float32)
        + jnp.dot(attended, out_proj, preferred_element_type=jnp.float32)
    ).astype(jnp.bfloat16)
    moe_in = normalize(mid_stream, moe_gain).astype(jnp.bfloat16)
    logits = jnp.dot(moe_in, router, preferred_element_type=jnp.float32)
    expert_count = router.shape[1]
    top_count = routes.shape[2]
    capacity = 2 * own_count * top_count // expert_count
    own_routes = lax.dynamic_slice_in_dim(routes[0], hid_index * own_count, own_count, axis=0)
    flat_routes = own_routes.reshape(-1)
    onehot = (flat_routes[:, None] == jnp.arange(expert_count, dtype=jnp.int32)[None, :]).astype(
        jnp.int32
    )
    slot_ids = jnp.sum((jnp.cumsum(onehot, axis=0) - 1) * onehot, axis=-1)
    targets = flat_routes * capacity + slot_ids
    slot_count = expert_count * capacity
    pick = targets[None, :] == jnp.arange(slot_count, dtype=jnp.int32)[:, None]
    pick_rows = jnp.any(pick.reshape(slot_count, own_count, top_count), axis=-1).astype(jnp.bfloat16)
    send_rows = jnp.dot(pick_rows, moe_in, preferred_element_type=jnp.float32).astype(jnp.bfloat16)
    chunk_count = 2
    chunk = capacity // chunk_count
    send_rows = send_rows.reshape(expert_count, capacity, model_width)
    pick_slots = pick.T.astype(jnp.bfloat16).reshape(own_count * top_count, expert_count, capacity)
    fetched = None
    for index in range(chunk_count):
        grouped_rows = lax.all_to_all(
            send_rows[:, index * chunk : (index + 1) * chunk], "req", 0, 0, tiled=True
        )
        flat_rows = grouped_rows.reshape(-1, model_width)
        gate_out = jnp.einsum(
            "nd,hdf->hnf", flat_rows, all_weights[:, 0], preferred_element_type=jnp.float32
        )
        up_out = jnp.einsum(
            "nd,hdf->hnf", flat_rows, all_weights[:, 1], preferred_element_type=jnp.float32
        )
        activation = (jnp.maximum(gate_out, 0.0) * up_out).astype(jnp.bfloat16)
        partials = jnp.einsum(
            "hnf,hdf->hnd", activation, all_weights[:, 2], preferred_element_type=jnp.float32
        ).astype(jnp.bfloat16)
        expert_out = jnp.sum(partials.astype(jnp.float32), axis=0).astype(jnp.bfloat16)
        returned = lax.all_to_all(
            expert_out.reshape(-1, chunk, model_width), "req", 0, 0, tiled=True
        )
        part = jnp.dot(
            pick_slots[:, :, index * chunk : (index + 1) * chunk].reshape(own_count * top_count, -1),
            returned.reshape(-1, model_width),
            preferred_element_type=jnp.float32,
        )
        fetched = part if fetched is None else fetched + part
    fetched = fetched.reshape(own_count, top_count, model_width)
    picked = jnp.take_along_axis(logits, own_routes, axis=1)
    gate_values = jax.nn.sigmoid(picked)
    weights = gate_values / jnp.sum(gate_values, axis=1, keepdims=True)
    moe_out = jnp.sum(weights[..., None] * fetched, axis=1)
    final_rows = (mid_stream.astype(jnp.float32) + moe_out).astype(jnp.bfloat16)
    return (final_rows[None], new_keys[None], new_values[None])


def solution(mesh):
    in_specs = (
        P("req", "hid", None),
        P("req", "hid", None),
        P("req", "hid", None),
        P("req", "hid", None),
        P("req"),
        P("req", None, None),
        P(),
        P(),
        P(),
        P(),
        P(),
        P(),
        P("req", None, None, "hid"),
        P("req", "hid", None),
    )
    out_specs = (P("req", "hid", None), P("req", "hid", None), P("req", "hid", None))
    return jax.shard_map(body, mesh=mesh, in_specs=in_specs, out_specs=out_specs, check_vma=False)
```

```python
import jax
import jax.numpy as jnp
from jax import lax
from jax.sharding import PartitionSpec as P
from jax.experimental import pallas as pl
from jax.experimental.pallas import tpu as pltpu
import functools

QH = 12
KVH = 2
HD = 128


EPS = 1e-06
MASKED_SCORE = -1e30
KEY_BLOCK = 512


def normalize(row_data, gain_vector):
    row_data = row_data.astype(jnp.float32)
    return (
        row_data
        * lax.rsqrt(jnp.mean(row_data * row_data, axis=-1, keepdims=True) + EPS)
        * gain_vector
    )


def absorb(state_now, grouped, key_rows, value_rows, visible):
    row_max, totals, accumulated = state_now
    scores = jnp.einsum(
        "tgsd,kgd->gstk", grouped, key_rows.reshape(-1, KVH, HD), preferred_element_type=jnp.float32
    ) * HD ** (-0.5)
    scores = jnp.where(visible, scores, MASKED_SCORE)
    new_max = jnp.maximum(row_max, jnp.max(scores, axis=-1))
    weights = jnp.where(visible, jnp.exp(scores - new_max[..., None]), 0.0)
    rescale = jnp.exp(row_max - new_max)
    totals = totals * rescale + jnp.sum(weights, axis=-1)
    accumulated = accumulated * rescale[..., None] + jnp.einsum(
        "gstk,kgd->gstd",
        weights.astype(jnp.bfloat16),
        value_rows.reshape(-1, KVH, HD),
        preferred_element_type=jnp.float32,
    )
    return (new_max, totals, accumulated)


def cache_block(state_now, grouped, key_rows, value_rows, first_pos, length):
    positions = first_pos + jnp.arange(key_rows.shape[0], dtype=jnp.int32)
    visible = (positions < length)[None, :]
    return lax.cond(
        first_pos < length,
        lambda current: absorb(current, grouped, key_rows, value_rows, visible),
        lambda current: current,
        state_now,
    )


def span_block(state_now, grouped, key_rows, value_rows, first_pos, query_pos):
    positions = first_pos + jnp.arange(key_rows.shape[0], dtype=jnp.int32)
    visible = positions[None, :] <= query_pos[:, None]
    return lax.cond(
        first_pos <= query_pos[-1],
        lambda current: absorb(current, grouped, key_rows, value_rows, visible),
        lambda current: current,
        state_now,
    )


def block_size(extent):
    return max(min(KEY_BLOCK, extent), extent // 8)


def empty_state(query_count):
    group_size = QH // KVH
    return (
        jnp.full((KVH, group_size, query_count), MASKED_SCORE, jnp.float32),
        jnp.zeros((KVH, group_size, query_count), jnp.float32),
        jnp.zeros((KVH, group_size, query_count, HD), jnp.float32),
    )


def attention_kernel(token_count, scalars, q_ref, k_ref, v_ref, o_ref, m_ref, l_ref, acc_ref, s_ref):
    length = scalars[0]
    hid_index = scalars[1]
    parts, part_rows, _ = k_ref.shape
    rows = q_ref.shape[1]
    cache_rows = part_rows - token_count
    q = q_ref[0]
    m_ref[...] = jnp.full(m_ref.shape, MASKED_SCORE, jnp.float32)
    l_ref[...] = jnp.zeros(l_ref.shape, jnp.float32)
    acc_ref[...] = jnp.zeros(acc_ref.shape, jnp.float32)
    blocks = []
    for part in range(parts):
        for first in range(0, cache_rows, KEY_BLOCK):
            blocks.append((part, first, min(KEY_BLOCK, cache_rows - first), True))
        blocks.append((part, cache_rows, token_count, False))

    def live(part, first, size, is_cache):
        if is_cache:
            return part * cache_rows + first < length
        return part <= hid_index

    def whole(part, first, size, is_cache):
        if is_cache:
            return part * cache_rows + first + size <= length
        return part < hid_index

    def visible(part, first, size, is_cache):
        if is_cache:
            pos = part * cache_rows + first + lax.broadcasted_iota(jnp.int32, (1, size), 1)
            return pos < length
        key_pos = part * token_count + lax.broadcasted_iota(jnp.int32, (1, size), 1)
        row_ids = lax.broadcasted_iota(jnp.int32, (rows, 1), 0)
        return key_pos <= hid_index * token_count + row_ids % token_count

    def first_pass(part, first, size, is_cache, masked):
        k = k_ref[part, pl.ds(first, size), :]
        raw = lax.dot_general(q, k, (((1,), (1,)), ((), ())), preferred_element_type=jnp.float32)
        s = raw * HD ** (-0.5)
        if masked:
            s = jnp.where(visible(part, first, size, is_cache), s, MASKED_SCORE)
        s_ref[:, pl.ds(part * part_rows + first, size)] = s
        m_ref[...] = jnp.maximum(m_ref[...], jnp.max(s, axis=-1, keepdims=True))

    for part, first, size, is_cache in blocks:
        is_whole = whole(part, first, size, is_cache)
        pl.when(is_whole)(functools.partial(first_pass, part, first, size, is_cache, False))
        pl.when(jnp.logical_and(live(part, first, size, is_cache), jnp.logical_not(is_whole)))(
            functools.partial(first_pass, part, first, size, is_cache, True)
        )

    for part, first, size, is_cache in blocks:

        @pl.when(live(part, first, size, is_cache))
        def _():
            w = jnp.exp(s_ref[:, pl.ds(part * part_rows + first, size)] - m_ref[...])
            l_ref[...] += jnp.sum(w, axis=-1, keepdims=True)
            v = v_ref[part, pl.ds(first, size), :]
            acc_ref[...] += jnp.dot(w.astype(jnp.bfloat16), v, preferred_element_type=jnp.float32)

    o_ref[0] = (acc_ref[...] / l_ref[...]).astype(o_ref.dtype)


def attention(grouped, all_kv, length, hid_index, token_count, interpret=False):
    groups, rows, head = grouped.shape
    parts, part_rows, _ = all_kv.shape
    scalars = jnp.stack([length, hid_index]).astype(jnp.int32)
    k_spec = pl.BlockSpec((parts, part_rows, head), lambda g, s: (0, 0, g))
    v_spec = pl.BlockSpec((parts, part_rows, head), lambda g, s: (0, 0, groups + g))
    row_spec = pl.BlockSpec((1, rows, head), lambda g, s: (g, 0, 0))
    return pl.pallas_call(
        functools.partial(attention_kernel, token_count),
        out_shape=jax.ShapeDtypeStruct((groups, rows, head), jnp.bfloat16),
        grid_spec=pltpu.PrefetchScalarGridSpec(
            num_scalar_prefetch=1,
            grid=(groups,),
            in_specs=[row_spec, k_spec, v_spec],
            out_specs=row_spec,
            scratch_shapes=[
                pltpu.VMEM((rows, 1), jnp.float32),
                pltpu.VMEM((rows, 1), jnp.float32),
                pltpu.VMEM((rows, head), jnp.float32),
                pltpu.VMEM((rows, parts * part_rows), jnp.float32),
            ],
        ),
        interpret=interpret,
    )(scalars, grouped, all_kv, all_kv)


def expert_activation(row_data, gate_weights):
    gate_out = jnp.dot(row_data, gate_weights[0], preferred_element_type=jnp.float32)
    up_out = jnp.dot(row_data, gate_weights[1], preferred_element_type=jnp.float32)
    return (jnp.maximum(gate_out, 0.0) * up_out).astype(jnp.bfloat16)


def body(
    hidden_in,
    queries,
    cache_keys,
    cache_values,
    lengths,
    routes,
    attn_gain,
    key_proj,
    value_proj,
    out_proj,
    moe_gain,
    router,
    gate_up,
    down_proj,
):
    own_count = hidden_in.shape[1]
    model_width = hidden_in.shape[2]
    hid_index = lax.axis_index("hid")
    hid_count = lax.axis_size("hid")
    group_size = QH // KVH
    normed = normalize(hidden_in[0], attn_gain).astype(jnp.bfloat16)
    key_width = key_proj.shape[1]
    new_kv = jnp.dot(
        normed, jnp.concatenate([key_proj, value_proj], axis=1), preferred_element_type=jnp.float32
    ).astype(jnp.bfloat16)
    new_keys = new_kv[:, :key_width]
    new_values = new_kv[:, key_width:]
    length = lengths[0]
    cache_local = cache_keys.shape[1]
    kv_buffer = jnp.concatenate(
        [
            jnp.concatenate([cache_keys[0], cache_values[0]], axis=1),
            jnp.zeros((own_count, 2 * key_width), jnp.bfloat16),
        ],
        axis=0,
    )
    kv_buffer = lax.dynamic_update_slice(kv_buffer, new_kv, (cache_local, 0))
    all_kv = lax.all_gather(kv_buffer, "hid", axis=0)
    all_weights = lax.all_gather(
        jnp.concatenate([gate_up[0], down_proj[0].T[None]], axis=0), "hid", axis=0
    )
    grouped = (
        queries[0]
        .reshape(own_count, KVH, group_size, HD)
        .transpose(1, 2, 0, 3)
        .reshape(KVH, group_size * own_count, HD)
    )
    attended = (
        attention(grouped, all_kv, length, hid_index, own_count)
        .reshape(KVH, group_size, own_count, HD)
        .transpose(2, 0, 1, 3)
        .reshape(own_count, QH * HD)
    )
    mid_stream = (
        hidden_in[0].astype(jnp.float32)
        + jnp.dot(attended, out_proj, preferred_element_type=jnp.float32)
    ).astype(jnp.bfloat16)
    moe_in = normalize(mid_stream, moe_gain).astype(jnp.bfloat16)
    logits = jnp.dot(moe_in, router, preferred_element_type=jnp.float32)
    expert_count = router.shape[1]
    top_count = routes.shape[2]
    capacity = 2 * own_count * top_count // expert_count
    own_routes = lax.dynamic_slice_in_dim(routes[0], hid_index * own_count, own_count, axis=0)
    flat_routes = own_routes.reshape(-1)
    onehot = (flat_routes[:, None] == jnp.arange(expert_count, dtype=jnp.int32)[None, :]).astype(
        jnp.int32
    )
    slot_ids = jnp.sum((jnp.cumsum(onehot, axis=0) - 1) * onehot, axis=-1)
    targets = flat_routes * capacity + slot_ids
    slot_count = expert_count * capacity
    pick = targets[None, :] == jnp.arange(slot_count, dtype=jnp.int32)[:, None]
    pick_rows = jnp.any(pick.reshape(slot_count, own_count, top_count), axis=-1).astype(jnp.bfloat16)
    send_rows = jnp.dot(pick_rows, moe_in, preferred_element_type=jnp.float32).astype(jnp.bfloat16)
    grouped_rows = lax.all_to_all(
        send_rows.reshape(expert_count, capacity, model_width), "req", 0, 0, tiled=True
    )
    flat_rows = grouped_rows.reshape(-1, model_width)
    gate_out = jnp.einsum(
        "nd,hdf->hnf", flat_rows, all_weights[:, 0], preferred_element_type=jnp.float32
    )
    up_out = jnp.einsum(
        "nd,hdf->hnf", flat_rows, all_weights[:, 1], preferred_element_type=jnp.float32
    )
    activation = (jnp.maximum(gate_out, 0.0) * up_out).astype(jnp.bfloat16)
    partials = jnp.einsum(
        "hnf,hdf->hnd", activation, all_weights[:, 2], preferred_element_type=jnp.float32
    ).astype(jnp.bfloat16)
    expert_out = jnp.sum(partials.astype(jnp.float32), axis=0).astype(jnp.bfloat16)
    returned = lax.all_to_all(
        expert_out.reshape(-1, capacity, model_width), "req", 0, 0, tiled=True
    )
    fetched = jnp.dot(
        pick.T.astype(jnp.bfloat16),
        returned.reshape(slot_count, model_width),
        preferred_element_type=jnp.float32,
    ).reshape(own_count, top_count, model_width)
    picked = jnp.take_along_axis(logits, own_routes, axis=1)
    gate_values = jax.nn.sigmoid(picked)
    weights = gate_values / jnp.sum(gate_values, axis=1, keepdims=True)
    moe_out = jnp.sum(weights[..., None] * fetched, axis=1)
    final_rows = (mid_stream.astype(jnp.float32) + moe_out).astype(jnp.bfloat16)
    return (final_rows[None], new_keys[None], new_values[None])


def solution(mesh):
    in_specs = (
        P("req", "hid", None),
        P("req", "hid", None),
        P("req", "hid", None),
        P("req", "hid", None),
        P("req"),
        P("req", None, None),
        P(),
        P(),
        P(),
        P(),
        P(),
        P(),
        P("req", None, None, "hid"),
        P("req", "hid", None),
    )
    out_specs = (P("req", "hid", None), P("req", "hid", None), P("req", "hid", None))
    return jax.shard_map(body, mesh=mesh, in_specs=in_specs, out_specs=out_specs, check_vma=False)
```

```python
import jax
import jax.numpy as jnp
from jax import lax
from jax.sharding import PartitionSpec as P
from jax.experimental import pallas as pl
from jax.experimental.pallas import tpu as pltpu
import functools

QH = 12
KVH = 2
HD = 128


EPS = 1e-06
MASKED_SCORE = -1e30
KEY_BLOCK = 512


def normalize(row_data, gain_vector):
    row_data = row_data.astype(jnp.float32)
    return (
        row_data
        * lax.rsqrt(jnp.mean(row_data * row_data, axis=-1, keepdims=True) + EPS)
        * gain_vector
    )


def absorb(state_now, grouped, key_rows, value_rows, visible):
    row_max, totals, accumulated = state_now
    scores = jnp.einsum(
        "tgsd,kgd->gstk", grouped, key_rows.reshape(-1, KVH, HD), preferred_element_type=jnp.float32
    ) * HD ** (-0.5)
    scores = jnp.where(visible, scores, MASKED_SCORE)
    new_max = jnp.maximum(row_max, jnp.max(scores, axis=-1))
    weights = jnp.where(visible, jnp.exp(scores - new_max[..., None]), 0.0)
    rescale = jnp.exp(row_max - new_max)
    totals = totals * rescale + jnp.sum(weights, axis=-1)
    accumulated = accumulated * rescale[..., None] + jnp.einsum(
        "gstk,kgd->gstd",
        weights.astype(jnp.bfloat16),
        value_rows.reshape(-1, KVH, HD),
        preferred_element_type=jnp.float32,
    )
    return (new_max, totals, accumulated)


def cache_block(state_now, grouped, key_rows, value_rows, first_pos, length):
    positions = first_pos + jnp.arange(key_rows.shape[0], dtype=jnp.int32)
    visible = (positions < length)[None, :]
    return lax.cond(
        first_pos < length,
        lambda current: absorb(current, grouped, key_rows, value_rows, visible),
        lambda current: current,
        state_now,
    )


def span_block(state_now, grouped, key_rows, value_rows, first_pos, query_pos):
    positions = first_pos + jnp.arange(key_rows.shape[0], dtype=jnp.int32)
    visible = positions[None, :] <= query_pos[:, None]
    return lax.cond(
        first_pos <= query_pos[-1],
        lambda current: absorb(current, grouped, key_rows, value_rows, visible),
        lambda current: current,
        state_now,
    )


def block_size(extent):
    return max(min(KEY_BLOCK, extent), extent // 8)


def empty_state(query_count):
    group_size = QH // KVH
    return (
        jnp.full((KVH, group_size, query_count), MASKED_SCORE, jnp.float32),
        jnp.zeros((KVH, group_size, query_count), jnp.float32),
        jnp.zeros((KVH, group_size, query_count, HD), jnp.float32),
    )


def attention_kernel(
    token_count, scalars, q_ref, k_ref, v_ref, kn_ref, vn_ref, o_ref, m_ref, l_ref, acc_ref, s_ref
):
    length = scalars[0]
    hid_index = scalars[1]
    parts, cache_rows, _ = k_ref.shape
    part_rows = cache_rows + token_count
    rows = q_ref.shape[1]
    q = q_ref[0]
    m_ref[...] = jnp.full(m_ref.shape, MASKED_SCORE, jnp.float32)
    l_ref[...] = jnp.zeros(l_ref.shape, jnp.float32)
    acc_ref[...] = jnp.zeros(acc_ref.shape, jnp.float32)
    blocks = []
    for part in range(parts):
        for first in range(0, cache_rows, KEY_BLOCK):
            blocks.append((part, first, min(KEY_BLOCK, cache_rows - first), True))
        blocks.append((part, cache_rows, token_count, False))

    def live(part, first, size, is_cache):
        if is_cache:
            return part * cache_rows + first < length
        return part <= hid_index

    def whole(part, first, size, is_cache):
        if is_cache:
            return part * cache_rows + first + size <= length
        return part < hid_index

    def visible(part, first, size, is_cache):
        if is_cache:
            pos = part * cache_rows + first + lax.broadcasted_iota(jnp.int32, (1, size), 1)
            return pos < length
        key_pos = part * token_count + lax.broadcasted_iota(jnp.int32, (1, size), 1)
        row_ids = lax.broadcasted_iota(jnp.int32, (rows, 1), 0)
        return key_pos <= hid_index * token_count + row_ids % token_count

    def first_pass(part, first, size, is_cache, masked):
        k = k_ref[part, pl.ds(first, size), :] if is_cache else kn_ref[part]
        raw = lax.dot_general(q, k, (((1,), (1,)), ((), ())), preferred_element_type=jnp.float32)
        s = raw * HD ** (-0.5)
        if masked:
            s = jnp.where(visible(part, first, size, is_cache), s, MASKED_SCORE)
        s_ref[:, pl.ds(part * part_rows + first, size)] = s
        m_ref[...] = jnp.maximum(m_ref[...], jnp.max(s, axis=-1, keepdims=True))

    for part, first, size, is_cache in blocks:
        is_whole = whole(part, first, size, is_cache)
        pl.when(is_whole)(functools.partial(first_pass, part, first, size, is_cache, False))
        pl.when(jnp.logical_and(live(part, first, size, is_cache), jnp.logical_not(is_whole)))(
            functools.partial(first_pass, part, first, size, is_cache, True)
        )

    for part, first, size, is_cache in blocks:

        @pl.when(live(part, first, size, is_cache))
        def _():
            w = jnp.exp(s_ref[:, pl.ds(part * part_rows + first, size)] - m_ref[...])
            l_ref[...] += jnp.sum(w, axis=-1, keepdims=True)
            v = v_ref[part, pl.ds(first, size), :] if is_cache else vn_ref[part]
            acc_ref[...] += jnp.dot(w.astype(jnp.bfloat16), v, preferred_element_type=jnp.float32)

    o_ref[0] = (acc_ref[...] / l_ref[...]).astype(o_ref.dtype)


def attention(grouped, all_kv, new_kv, length, hid_index, token_count, interpret=False):
    groups, rows, head = grouped.shape
    parts, cache_rows, _ = all_kv.shape
    scalars = jnp.stack([length, hid_index]).astype(jnp.int32)
    k_spec = pl.BlockSpec((parts, cache_rows, head), lambda g, s: (0, 0, g))
    v_spec = pl.BlockSpec((parts, cache_rows, head), lambda g, s: (0, 0, groups + g))
    kn_spec = pl.BlockSpec((parts, token_count, head), lambda g, s: (0, 0, g))
    vn_spec = pl.BlockSpec((parts, token_count, head), lambda g, s: (0, 0, groups + g))
    row_spec = pl.BlockSpec((1, rows, head), lambda g, s: (g, 0, 0))
    return pl.pallas_call(
        functools.partial(attention_kernel, token_count),
        out_shape=jax.ShapeDtypeStruct((groups, rows, head), jnp.bfloat16),
        grid_spec=pltpu.PrefetchScalarGridSpec(
            num_scalar_prefetch=1,
            grid=(groups,),
            in_specs=[row_spec, k_spec, v_spec, kn_spec, vn_spec],
            out_specs=row_spec,
            scratch_shapes=[
                pltpu.VMEM((rows, 1), jnp.float32),
                pltpu.VMEM((rows, 1), jnp.float32),
                pltpu.VMEM((rows, head), jnp.float32),
                pltpu.VMEM((rows, parts * (cache_rows + token_count)), jnp.float32),
            ],
        ),
        interpret=interpret,
    )(scalars, grouped, all_kv, all_kv, new_kv, new_kv)


def expert_activation(row_data, gate_weights):
    gate_out = jnp.dot(row_data, gate_weights[0], preferred_element_type=jnp.float32)
    up_out = jnp.dot(row_data, gate_weights[1], preferred_element_type=jnp.float32)
    return (jnp.maximum(gate_out, 0.0) * up_out).astype(jnp.bfloat16)


def body(
    hidden_in,
    queries,
    cache_keys,
    cache_values,
    lengths,
    routes,
    attn_gain,
    key_proj,
    value_proj,
    out_proj,
    moe_gain,
    router,
    gate_up,
    down_proj,
):
    own_count = hidden_in.shape[1]
    model_width = hidden_in.shape[2]
    hid_index = lax.axis_index("hid")
    hid_count = lax.axis_size("hid")
    group_size = QH // KVH
    normed = normalize(hidden_in[0], attn_gain).astype(jnp.bfloat16)
    key_width = key_proj.shape[1]
    new_kv = jnp.dot(
        normed, jnp.concatenate([key_proj, value_proj], axis=1), preferred_element_type=jnp.float32
    ).astype(jnp.bfloat16)
    new_keys = new_kv[:, :key_width]
    new_values = new_kv[:, key_width:]
    length = lengths[0]
    cache_local = cache_keys.shape[1]
    all_kv = lax.all_gather(
        jnp.concatenate([cache_keys[0], cache_values[0]], axis=1), "hid", axis=0
    )
    received = [new_kv]
    for shift in range(1, hid_count):
        pairs = [(source, source + shift) for source in range(hid_count - shift)]
        received.append(lax.ppermute(new_kv, "hid", pairs))
    new_parts = []
    for part in range(hid_count):
        distance = hid_index - part
        chosen = received[-1]
        for shift in range(hid_count - 2, -1, -1):
            chosen = jnp.where(distance == shift, received[shift], chosen)
        new_parts.append(chosen)
    new_parts = jnp.stack(new_parts)
    all_weights = lax.all_gather(
        jnp.concatenate([gate_up[0], down_proj[0].T[None]], axis=0), "hid", axis=0
    )
    grouped = (
        queries[0]
        .reshape(own_count, KVH, group_size, HD)
        .transpose(1, 2, 0, 3)
        .reshape(KVH, group_size * own_count, HD)
    )
    attended = (
        attention(grouped, all_kv, new_parts, length, hid_index, own_count)
        .reshape(KVH, group_size, own_count, HD)
        .transpose(2, 0, 1, 3)
        .reshape(own_count, QH * HD)
    )
    mid_stream = (
        hidden_in[0].astype(jnp.float32)
        + jnp.dot(attended, out_proj, preferred_element_type=jnp.float32)
    ).astype(jnp.bfloat16)
    moe_in = normalize(mid_stream, moe_gain).astype(jnp.bfloat16)
    logits = jnp.dot(moe_in, router, preferred_element_type=jnp.float32)
    expert_count = router.shape[1]
    top_count = routes.shape[2]
    capacity = 2 * own_count * top_count // expert_count
    own_routes = lax.dynamic_slice_in_dim(routes[0], hid_index * own_count, own_count, axis=0)
    flat_routes = own_routes.reshape(-1)
    onehot = (flat_routes[:, None] == jnp.arange(expert_count, dtype=jnp.int32)[None, :]).astype(
        jnp.int32
    )
    slot_ids = jnp.sum((jnp.cumsum(onehot, axis=0) - 1) * onehot, axis=-1)
    targets = flat_routes * capacity + slot_ids
    slot_count = expert_count * capacity
    pick = targets[None, :] == jnp.arange(slot_count, dtype=jnp.int32)[:, None]
    pick_rows = jnp.any(pick.reshape(slot_count, own_count, top_count), axis=-1).astype(jnp.bfloat16)
    send_rows = jnp.dot(pick_rows, moe_in, preferred_element_type=jnp.float32).astype(jnp.bfloat16)
    grouped_rows = lax.all_to_all(
        send_rows.reshape(expert_count, capacity, model_width), "req", 0, 0, tiled=True
    )
    flat_rows = grouped_rows.reshape(-1, model_width)
    gate_out = jnp.einsum(
        "nd,hdf->hnf", flat_rows, all_weights[:, 0], preferred_element_type=jnp.float32
    )
    up_out = jnp.einsum(
        "nd,hdf->hnf", flat_rows, all_weights[:, 1], preferred_element_type=jnp.float32
    )
    activation = (jnp.maximum(gate_out, 0.0) * up_out).astype(jnp.bfloat16)
    partials = jnp.einsum(
        "hnf,hdf->hnd", activation, all_weights[:, 2], preferred_element_type=jnp.float32
    ).astype(jnp.bfloat16)
    expert_out = jnp.sum(partials.astype(jnp.float32), axis=0).astype(jnp.bfloat16)
    returned = lax.all_to_all(
        expert_out.reshape(-1, capacity, model_width), "req", 0, 0, tiled=True
    )
    fetched = jnp.dot(
        pick.T.astype(jnp.bfloat16),
        returned.reshape(slot_count, model_width),
        preferred_element_type=jnp.float32,
    ).reshape(own_count, top_count, model_width)
    picked = jnp.take_along_axis(logits, own_routes, axis=1)
    gate_values = jax.nn.sigmoid(picked)
    weights = gate_values / jnp.sum(gate_values, axis=1, keepdims=True)
    moe_out = jnp.sum(weights[..., None] * fetched, axis=1)
    final_rows = (mid_stream.astype(jnp.float32) + moe_out).astype(jnp.bfloat16)
    return (final_rows[None], new_keys[None], new_values[None])


def solution(mesh):
    in_specs = (
        P("req", "hid", None),
        P("req", "hid", None),
        P("req", "hid", None),
        P("req", "hid", None),
        P("req"),
        P("req", None, None),
        P(),
        P(),
        P(),
        P(),
        P(),
        P(),
        P("req", None, None, "hid"),
        P("req", "hid", None),
    )
    out_specs = (P("req", "hid", None), P("req", "hid", None), P("req", "hid", None))
    return jax.shard_map(body, mesh=mesh, in_specs=in_specs, out_specs=out_specs, check_vma=False)
```

```python
import jax
import jax.numpy as jnp
from jax import lax
from jax.sharding import PartitionSpec as P
from jax.experimental import pallas as pl
from jax.experimental.pallas import tpu as pltpu
import functools

QH = 12
KVH = 2
HD = 128


EPS = 1e-06
MASKED_SCORE = -1e30
KEY_BLOCK = 512


def normalize(row_data, gain_vector):
    row_data = row_data.astype(jnp.float32)
    return (
        row_data
        * lax.rsqrt(jnp.mean(row_data * row_data, axis=-1, keepdims=True) + EPS)
        * gain_vector
    )


def absorb(state_now, grouped, key_rows, value_rows, visible):
    row_max, totals, accumulated = state_now
    scores = jnp.einsum(
        "tgsd,kgd->gstk", grouped, key_rows.reshape(-1, KVH, HD), preferred_element_type=jnp.float32
    ) * HD ** (-0.5)
    scores = jnp.where(visible, scores, MASKED_SCORE)
    new_max = jnp.maximum(row_max, jnp.max(scores, axis=-1))
    weights = jnp.where(visible, jnp.exp(scores - new_max[..., None]), 0.0)
    rescale = jnp.exp(row_max - new_max)
    totals = totals * rescale + jnp.sum(weights, axis=-1)
    accumulated = accumulated * rescale[..., None] + jnp.einsum(
        "gstk,kgd->gstd",
        weights.astype(jnp.bfloat16),
        value_rows.reshape(-1, KVH, HD),
        preferred_element_type=jnp.float32,
    )
    return (new_max, totals, accumulated)


def cache_block(state_now, grouped, key_rows, value_rows, first_pos, length):
    positions = first_pos + jnp.arange(key_rows.shape[0], dtype=jnp.int32)
    visible = (positions < length)[None, :]
    return lax.cond(
        first_pos < length,
        lambda current: absorb(current, grouped, key_rows, value_rows, visible),
        lambda current: current,
        state_now,
    )


def span_block(state_now, grouped, key_rows, value_rows, first_pos, query_pos):
    positions = first_pos + jnp.arange(key_rows.shape[0], dtype=jnp.int32)
    visible = positions[None, :] <= query_pos[:, None]
    return lax.cond(
        first_pos <= query_pos[-1],
        lambda current: absorb(current, grouped, key_rows, value_rows, visible),
        lambda current: current,
        state_now,
    )


def block_size(extent):
    return max(min(KEY_BLOCK, extent), extent // 8)


def empty_state(query_count):
    group_size = QH // KVH
    return (
        jnp.full((KVH, group_size, query_count), MASKED_SCORE, jnp.float32),
        jnp.zeros((KVH, group_size, query_count), jnp.float32),
        jnp.zeros((KVH, group_size, query_count, HD), jnp.float32),
    )


def attention_kernel(
    token_count,
    scalars,
    q_ref,
    k_ref,
    v0_ref,
    v1_ref,
    v2_ref,
    v3_ref,
    kn_ref,
    vn_ref,
    o_ref,
    m_ref,
    l_ref,
    acc_ref,
    s_ref,
):
    length = scalars[0]
    hid_index = scalars[1]
    parts, cache_rows, _ = k_ref.shape
    rows = q_ref.shape[1]
    v_refs = (v0_ref, v1_ref, v2_ref, v3_ref)
    q = q_ref[0]
    m_ref[...] = jnp.full(m_ref.shape, MASKED_SCORE, jnp.float32)
    l_ref[...] = jnp.zeros(l_ref.shape, jnp.float32)
    acc_ref[...] = jnp.zeros(acc_ref.shape, jnp.float32)
    blocks = []
    for shift in range(parts):
        for first in range(0, cache_rows, KEY_BLOCK):
            blocks.append((shift, first, min(KEY_BLOCK, cache_rows - first), True))
    for part in range(parts):
        blocks.append((part, 0, token_count, False))

    def part_of(index, is_cache):
        return (hid_index - index + parts) % parts if is_cache else index

    def slot(index, first, is_cache):
        return index * cache_rows + first if is_cache else parts * cache_rows + index * token_count

    def live(index, first, size, is_cache):
        if is_cache:
            return part_of(index, True) * cache_rows + first < length
        return index <= hid_index

    def whole(index, first, size, is_cache):
        if is_cache:
            return part_of(index, True) * cache_rows + first + size <= length
        return index < hid_index

    def visible(index, first, size, is_cache):
        if is_cache:
            start = part_of(index, True) * cache_rows + first
            return start + lax.broadcasted_iota(jnp.int32, (1, size), 1) < length
        key_pos = index * token_count + lax.broadcasted_iota(jnp.int32, (1, size), 1)
        row_ids = lax.broadcasted_iota(jnp.int32, (rows, 1), 0)
        return key_pos <= hid_index * token_count + row_ids % token_count

    def first_pass(index, first, size, is_cache, masked):
        if is_cache:
            k = k_ref[part_of(index, True), pl.ds(first, size), :]
        else:
            k = kn_ref[index]
        raw = lax.dot_general(q, k, (((1,), (1,)), ((), ())), preferred_element_type=jnp.float32)
        s = raw * HD ** (-0.5)
        if masked:
            s = jnp.where(visible(index, first, size, is_cache), s, MASKED_SCORE)
        s_ref[:, pl.ds(slot(index, first, is_cache), size)] = s
        m_ref[...] = jnp.maximum(m_ref[...], jnp.max(s, axis=-1, keepdims=True))

    for index, first, size, is_cache in blocks:
        is_whole = whole(index, first, size, is_cache)
        pl.when(is_whole)(functools.partial(first_pass, index, first, size, is_cache, False))
        pl.when(jnp.logical_and(live(index, first, size, is_cache), jnp.logical_not(is_whole)))(
            functools.partial(first_pass, index, first, size, is_cache, True)
        )

    for index, first, size, is_cache in blocks:

        @pl.when(live(index, first, size, is_cache))
        def _():
            w = jnp.exp(s_ref[:, pl.ds(slot(index, first, is_cache), size)] - m_ref[...])
            l_ref[...] += jnp.sum(w, axis=-1, keepdims=True)
            v = v_refs[index][pl.ds(first, size), :] if is_cache else vn_ref[index]
            acc_ref[...] += jnp.dot(w.astype(jnp.bfloat16), v, preferred_element_type=jnp.float32)

    o_ref[0] = (acc_ref[...] / l_ref[...]).astype(o_ref.dtype)


def attention(grouped, all_keys, shifted_values, new_kv, length, hid_index, token_count, interpret=False):
    groups, rows, head = grouped.shape
    parts, cache_rows, _ = all_keys.shape
    scalars = jnp.stack([length, hid_index]).astype(jnp.int32)
    k_spec = pl.BlockSpec((parts, cache_rows, head), lambda g, s: (0, 0, g))
    v_spec = pl.BlockSpec((cache_rows, head), lambda g, s: (0, g))
    kn_spec = pl.BlockSpec((parts, token_count, head), lambda g, s: (0, 0, g))
    vn_spec = pl.BlockSpec((parts, token_count, head), lambda g, s: (0, 0, groups + g))
    row_spec = pl.BlockSpec((1, rows, head), lambda g, s: (g, 0, 0))
    return pl.pallas_call(
        functools.partial(attention_kernel, token_count),
        out_shape=jax.ShapeDtypeStruct((groups, rows, head), jnp.bfloat16),
        grid_spec=pltpu.PrefetchScalarGridSpec(
            num_scalar_prefetch=1,
            grid=(groups,),
            in_specs=[row_spec, k_spec] + [v_spec] * parts + [kn_spec, vn_spec],
            out_specs=row_spec,
            scratch_shapes=[
                pltpu.VMEM((rows, 1), jnp.float32),
                pltpu.VMEM((rows, 1), jnp.float32),
                pltpu.VMEM((rows, head), jnp.float32),
                pltpu.VMEM((rows, parts * (cache_rows + token_count)), jnp.float32),
            ],
        ),
        interpret=interpret,
    )(scalars, grouped, all_keys, *shifted_values, new_kv, new_kv)


def expert_activation(row_data, gate_weights):
    gate_out = jnp.dot(row_data, gate_weights[0], preferred_element_type=jnp.float32)
    up_out = jnp.dot(row_data, gate_weights[1], preferred_element_type=jnp.float32)
    return (jnp.maximum(gate_out, 0.0) * up_out).astype(jnp.bfloat16)


def body(
    hidden_in,
    queries,
    cache_keys,
    cache_values,
    lengths,
    routes,
    attn_gain,
    key_proj,
    value_proj,
    out_proj,
    moe_gain,
    router,
    gate_up,
    down_proj,
):
    own_count = hidden_in.shape[1]
    model_width = hidden_in.shape[2]
    hid_index = lax.axis_index("hid")
    hid_count = lax.axis_size("hid")
    group_size = QH // KVH
    normed = normalize(hidden_in[0], attn_gain).astype(jnp.bfloat16)
    key_width = key_proj.shape[1]
    new_kv = jnp.dot(
        normed, jnp.concatenate([key_proj, value_proj], axis=1), preferred_element_type=jnp.float32
    ).astype(jnp.bfloat16)
    new_keys = new_kv[:, :key_width]
    new_values = new_kv[:, key_width:]
    length = lengths[0]
    cache_local = cache_keys.shape[1]
    all_keys = lax.all_gather(cache_keys[0], "hid", axis=0)
    shifted_values = [cache_values[0]]
    for shift in range(1, hid_count):
        pairs = [(source, (source + shift) % hid_count) for source in range(hid_count)]
        shifted_values.append(lax.ppermute(cache_values[0], "hid", pairs))
    received = [new_kv]
    for shift in range(1, hid_count):
        pairs = [(source, source + shift) for source in range(hid_count - shift)]
        received.append(lax.ppermute(new_kv, "hid", pairs))
    new_parts = []
    for part in range(hid_count):
        distance = hid_index - part
        chosen = received[-1]
        for shift in range(hid_count - 2, -1, -1):
            chosen = jnp.where(distance == shift, received[shift], chosen)
        new_parts.append(chosen)
    new_parts = jnp.stack(new_parts)
    all_weights = lax.all_gather(
        jnp.concatenate([gate_up[0], down_proj[0].T[None]], axis=0), "hid", axis=0
    )
    grouped = (
        queries[0]
        .reshape(own_count, KVH, group_size, HD)
        .transpose(1, 2, 0, 3)
        .reshape(KVH, group_size * own_count, HD)
    )
    attended = (
        attention(grouped, all_keys, shifted_values, new_parts, length, hid_index, own_count)
        .reshape(KVH, group_size, own_count, HD)
        .transpose(2, 0, 1, 3)
        .reshape(own_count, QH * HD)
    )
    mid_stream = (
        hidden_in[0].astype(jnp.float32)
        + jnp.dot(attended, out_proj, preferred_element_type=jnp.float32)
    ).astype(jnp.bfloat16)
    moe_in = normalize(mid_stream, moe_gain).astype(jnp.bfloat16)
    logits = jnp.dot(moe_in, router, preferred_element_type=jnp.float32)
    expert_count = router.shape[1]
    top_count = routes.shape[2]
    capacity = 2 * own_count * top_count // expert_count
    own_routes = lax.dynamic_slice_in_dim(routes[0], hid_index * own_count, own_count, axis=0)
    flat_routes = own_routes.reshape(-1)
    onehot = (flat_routes[:, None] == jnp.arange(expert_count, dtype=jnp.int32)[None, :]).astype(
        jnp.int32
    )
    slot_ids = jnp.sum((jnp.cumsum(onehot, axis=0) - 1) * onehot, axis=-1)
    targets = flat_routes * capacity + slot_ids
    slot_count = expert_count * capacity
    pick = targets[None, :] == jnp.arange(slot_count, dtype=jnp.int32)[:, None]
    pick_rows = jnp.any(pick.reshape(slot_count, own_count, top_count), axis=-1).astype(jnp.bfloat16)
    send_rows = jnp.dot(pick_rows, moe_in, preferred_element_type=jnp.float32).astype(jnp.bfloat16)
    grouped_rows = lax.all_to_all(
        send_rows.reshape(expert_count, capacity, model_width), "req", 0, 0, tiled=True
    )
    flat_rows = grouped_rows.reshape(-1, model_width)
    gate_out = jnp.einsum(
        "nd,hdf->hnf", flat_rows, all_weights[:, 0], preferred_element_type=jnp.float32
    )
    up_out = jnp.einsum(
        "nd,hdf->hnf", flat_rows, all_weights[:, 1], preferred_element_type=jnp.float32
    )
    activation = (jnp.maximum(gate_out, 0.0) * up_out).astype(jnp.bfloat16)
    partials = jnp.einsum(
        "hnf,hdf->hnd", activation, all_weights[:, 2], preferred_element_type=jnp.float32
    ).astype(jnp.bfloat16)
    expert_out = jnp.sum(partials.astype(jnp.float32), axis=0).astype(jnp.bfloat16)
    returned = lax.all_to_all(
        expert_out.reshape(-1, capacity, model_width), "req", 0, 0, tiled=True
    )
    fetched = jnp.dot(
        pick.T.astype(jnp.bfloat16),
        returned.reshape(slot_count, model_width),
        preferred_element_type=jnp.float32,
    ).reshape(own_count, top_count, model_width)
    picked = jnp.take_along_axis(logits, own_routes, axis=1)
    gate_values = jax.nn.sigmoid(picked)
    weights = gate_values / jnp.sum(gate_values, axis=1, keepdims=True)
    moe_out = jnp.sum(weights[..., None] * fetched, axis=1)
    final_rows = (mid_stream.astype(jnp.float32) + moe_out).astype(jnp.bfloat16)
    return (final_rows[None], new_keys[None], new_values[None])


def solution(mesh):
    in_specs = (
        P("req", "hid", None),
        P("req", "hid", None),
        P("req", "hid", None),
        P("req", "hid", None),
        P("req"),
        P("req", None, None),
        P(),
        P(),
        P(),
        P(),
        P(),
        P(),
        P("req", None, None, "hid"),
        P("req", "hid", None),
    )
    out_specs = (P("req", "hid", None), P("req", "hid", None), P("req", "hid", None))
    return jax.shard_map(body, mesh=mesh, in_specs=in_specs, out_specs=out_specs, check_vma=False)
```

```python
import jax
import jax.numpy as jnp
from jax import lax
from jax.sharding import PartitionSpec as P
from jax.experimental import pallas as pl
from jax.experimental.pallas import tpu as pltpu
import functools

QH = 12
KVH = 2
HD = 128


EPS = 1e-06
MASKED_SCORE = -1e30
KEY_BLOCK = 512


def normalize(row_data, gain_vector):
    row_data = row_data.astype(jnp.float32)
    return (
        row_data
        * lax.rsqrt(jnp.mean(row_data * row_data, axis=-1, keepdims=True) + EPS)
        * gain_vector
    )


def absorb(state_now, grouped, key_rows, value_rows, visible):
    row_max, totals, accumulated = state_now
    scores = jnp.einsum(
        "tgsd,kgd->gstk", grouped, key_rows.reshape(-1, KVH, HD), preferred_element_type=jnp.float32
    ) * HD ** (-0.5)
    scores = jnp.where(visible, scores, MASKED_SCORE)
    new_max = jnp.maximum(row_max, jnp.max(scores, axis=-1))
    weights = jnp.where(visible, jnp.exp(scores - new_max[..., None]), 0.0)
    rescale = jnp.exp(row_max - new_max)
    totals = totals * rescale + jnp.sum(weights, axis=-1)
    accumulated = accumulated * rescale[..., None] + jnp.einsum(
        "gstk,kgd->gstd",
        weights.astype(jnp.bfloat16),
        value_rows.reshape(-1, KVH, HD),
        preferred_element_type=jnp.float32,
    )
    return (new_max, totals, accumulated)


def cache_block(state_now, grouped, key_rows, value_rows, first_pos, length):
    positions = first_pos + jnp.arange(key_rows.shape[0], dtype=jnp.int32)
    visible = (positions < length)[None, :]
    return lax.cond(
        first_pos < length,
        lambda current: absorb(current, grouped, key_rows, value_rows, visible),
        lambda current: current,
        state_now,
    )


def span_block(state_now, grouped, key_rows, value_rows, first_pos, query_pos):
    positions = first_pos + jnp.arange(key_rows.shape[0], dtype=jnp.int32)
    visible = positions[None, :] <= query_pos[:, None]
    return lax.cond(
        first_pos <= query_pos[-1],
        lambda current: absorb(current, grouped, key_rows, value_rows, visible),
        lambda current: current,
        state_now,
    )


def block_size(extent):
    return max(min(KEY_BLOCK, extent), extent // 8)


def empty_state(query_count):
    group_size = QH // KVH
    return (
        jnp.full((KVH, group_size, query_count), MASKED_SCORE, jnp.float32),
        jnp.zeros((KVH, group_size, query_count), jnp.float32),
        jnp.zeros((KVH, group_size, query_count, HD), jnp.float32),
    )


def attention_kernel(
    token_count,
    scalars,
    q_ref,
    k0_ref,
    k1_ref,
    k2_ref,
    k3_ref,
    v0_ref,
    v1_ref,
    v2_ref,
    v3_ref,
    kn_ref,
    vn_ref,
    o_ref,
    m_ref,
    l_ref,
    acc_ref,
    s_ref,
):
    length = scalars[0]
    hid_index = scalars[1]
    k_refs = (k0_ref, k1_ref, k2_ref, k3_ref)
    v_refs = (v0_ref, v1_ref, v2_ref, v3_ref)
    parts = len(k_refs)
    cache_rows = k0_ref.shape[0]
    rows = q_ref.shape[1]
    q = q_ref[0]
    m_ref[...] = jnp.full(m_ref.shape, MASKED_SCORE, jnp.float32)
    l_ref[...] = jnp.zeros(l_ref.shape, jnp.float32)
    acc_ref[...] = jnp.zeros(acc_ref.shape, jnp.float32)
    blocks = []
    for shift in range(parts):
        for first in range(0, cache_rows, KEY_BLOCK):
            blocks.append((shift, first, min(KEY_BLOCK, cache_rows - first), True))
    for part in range(parts):
        blocks.append((part, 0, token_count, False))

    def part_of(index, is_cache):
        return (hid_index - index + parts) % parts if is_cache else index

    def slot(index, first, is_cache):
        return index * cache_rows + first if is_cache else parts * cache_rows + index * token_count

    def live(index, first, size, is_cache):
        if is_cache:
            return part_of(index, True) * cache_rows + first < length
        return index <= hid_index

    def whole(index, first, size, is_cache):
        if is_cache:
            return part_of(index, True) * cache_rows + first + size <= length
        return index < hid_index

    def visible(index, first, size, is_cache):
        if is_cache:
            start = part_of(index, True) * cache_rows + first
            return start + lax.broadcasted_iota(jnp.int32, (1, size), 1) < length
        key_pos = index * token_count + lax.broadcasted_iota(jnp.int32, (1, size), 1)
        row_ids = lax.broadcasted_iota(jnp.int32, (rows, 1), 0)
        return key_pos <= hid_index * token_count + row_ids % token_count

    def first_pass(index, first, size, is_cache, masked):
        if is_cache:
            k = k_refs[index][pl.ds(first, size), :]
        else:
            k = kn_ref[index]
        raw = lax.dot_general(q, k, (((1,), (1,)), ((), ())), preferred_element_type=jnp.float32)
        s = raw * HD ** (-0.5)
        if masked:
            s = jnp.where(visible(index, first, size, is_cache), s, MASKED_SCORE)
        s_ref[:, pl.ds(slot(index, first, is_cache), size)] = s
        m_ref[...] = jnp.maximum(m_ref[...], jnp.max(s, axis=-1, keepdims=True))

    for index, first, size, is_cache in blocks:
        is_whole = whole(index, first, size, is_cache)
        pl.when(is_whole)(functools.partial(first_pass, index, first, size, is_cache, False))
        pl.when(jnp.logical_and(live(index, first, size, is_cache), jnp.logical_not(is_whole)))(
            functools.partial(first_pass, index, first, size, is_cache, True)
        )

    for index, first, size, is_cache in blocks:

        @pl.when(live(index, first, size, is_cache))
        def _():
            w = jnp.exp(s_ref[:, pl.ds(slot(index, first, is_cache), size)] - m_ref[...])
            l_ref[...] += jnp.sum(w, axis=-1, keepdims=True)
            v = v_refs[index][pl.ds(first, size), :] if is_cache else vn_ref[index]
            acc_ref[...] += jnp.dot(w.astype(jnp.bfloat16), v, preferred_element_type=jnp.float32)

    o_ref[0] = (acc_ref[...] / l_ref[...]).astype(o_ref.dtype)


def attention(grouped, shifted_kv, new_kv, length, hid_index, token_count, interpret=False):
    groups, rows, head = grouped.shape
    parts = len(shifted_kv)
    cache_rows = shifted_kv[0].shape[0]
    scalars = jnp.stack([length, hid_index]).astype(jnp.int32)
    k_spec = pl.BlockSpec((cache_rows, head), lambda g, s: (0, g))
    v_spec = pl.BlockSpec((cache_rows, head), lambda g, s: (0, groups + g))
    kn_spec = pl.BlockSpec((parts, token_count, head), lambda g, s: (0, 0, g))
    vn_spec = pl.BlockSpec((parts, token_count, head), lambda g, s: (0, 0, groups + g))
    row_spec = pl.BlockSpec((1, rows, head), lambda g, s: (g, 0, 0))
    return pl.pallas_call(
        functools.partial(attention_kernel, token_count),
        out_shape=jax.ShapeDtypeStruct((groups, rows, head), jnp.bfloat16),
        grid_spec=pltpu.PrefetchScalarGridSpec(
            num_scalar_prefetch=1,
            grid=(groups,),
            in_specs=[row_spec] + [k_spec] * parts + [v_spec] * parts + [kn_spec, vn_spec],
            out_specs=row_spec,
            scratch_shapes=[
                pltpu.VMEM((rows, 1), jnp.float32),
                pltpu.VMEM((rows, 1), jnp.float32),
                pltpu.VMEM((rows, head), jnp.float32),
                pltpu.VMEM((rows, parts * (cache_rows + token_count)), jnp.float32),
            ],
        ),
        interpret=interpret,
    )(scalars, grouped, *shifted_kv, *shifted_kv, new_kv, new_kv)


def ring_gather(shard, split_axis, axis_name="hid"):
    count = lax.axis_size(axis_name)
    up = [(source, (source + 1) % count) for source in range(count)]
    down = [(source, (source - 1) % count) for source in range(count)]
    from_below = lax.ppermute(shard, axis_name, up)
    from_above = lax.ppermute(shard, axis_name, down)
    half = shard.shape[split_axis] // 2
    far = jnp.concatenate(
        [
            lax.ppermute(lax.slice_in_dim(from_below, 0, half, axis=split_axis), axis_name, up),
            lax.ppermute(
                lax.slice_in_dim(from_above, half, shard.shape[split_axis], axis=split_axis),
                axis_name,
                down,
            ),
        ],
        axis=split_axis,
    )
    return [shard, from_below, far, from_above]


def expert_activation(row_data, gate_weights):
    gate_out = jnp.dot(row_data, gate_weights[0], preferred_element_type=jnp.float32)
    up_out = jnp.dot(row_data, gate_weights[1], preferred_element_type=jnp.float32)
    return (jnp.maximum(gate_out, 0.0) * up_out).astype(jnp.bfloat16)


def body(
    hidden_in,
    queries,
    cache_keys,
    cache_values,
    lengths,
    routes,
    attn_gain,
    key_proj,
    value_proj,
    out_proj,
    moe_gain,
    router,
    gate_up,
    down_proj,
):
    own_count = hidden_in.shape[1]
    model_width = hidden_in.shape[2]
    hid_index = lax.axis_index("hid")
    hid_count = lax.axis_size("hid")
    group_size = QH // KVH
    normed = normalize(hidden_in[0], attn_gain).astype(jnp.bfloat16)
    key_width = key_proj.shape[1]
    new_kv = jnp.dot(
        normed, jnp.concatenate([key_proj, value_proj], axis=1), preferred_element_type=jnp.float32
    ).astype(jnp.bfloat16)
    new_keys = new_kv[:, :key_width]
    new_values = new_kv[:, key_width:]
    length = lengths[0]
    cache_local = cache_keys.shape[1]
    shifted_kv = ring_gather(jnp.concatenate([cache_keys[0], cache_values[0]], axis=1), 0)
    received = [new_kv]
    for shift in range(1, hid_count):
        pairs = [(source, source + shift) for source in range(hid_count - shift)]
        received.append(lax.ppermute(new_kv, "hid", pairs))
    new_parts = []
    for part in range(hid_count):
        distance = hid_index - part
        chosen = received[-1]
        for shift in range(hid_count - 2, -1, -1):
            chosen = jnp.where(distance == shift, received[shift], chosen)
        new_parts.append(chosen)
    new_parts = jnp.stack(new_parts)
    stacked_weights, _ = lax.optimization_barrier(
        (jnp.concatenate([gate_up[0], down_proj[0].T[None]], axis=0), shifted_kv[2])
    )
    shifted_weights = ring_gather(stacked_weights, 1)
    grouped = (
        queries[0]
        .reshape(own_count, KVH, group_size, HD)
        .transpose(1, 2, 0, 3)
        .reshape(KVH, group_size * own_count, HD)
    )
    attended = (
        attention(grouped, shifted_kv, new_parts, length, hid_index, own_count)
        .reshape(KVH, group_size, own_count, HD)
        .transpose(2, 0, 1, 3)
        .reshape(own_count, QH * HD)
    )
    mid_stream = (
        hidden_in[0].astype(jnp.float32)
        + jnp.dot(attended, out_proj, preferred_element_type=jnp.float32)
    ).astype(jnp.bfloat16)
    moe_in = normalize(mid_stream, moe_gain).astype(jnp.bfloat16)
    logits = jnp.dot(moe_in, router, preferred_element_type=jnp.float32)
    expert_count = router.shape[1]
    top_count = routes.shape[2]
    capacity = 2 * own_count * top_count // expert_count
    own_routes = lax.dynamic_slice_in_dim(routes[0], hid_index * own_count, own_count, axis=0)
    flat_routes = own_routes.reshape(-1)
    onehot = (flat_routes[:, None] == jnp.arange(expert_count, dtype=jnp.int32)[None, :]).astype(
        jnp.int32
    )
    slot_ids = jnp.sum((jnp.cumsum(onehot, axis=0) - 1) * onehot, axis=-1)
    targets = flat_routes * capacity + slot_ids
    slot_count = expert_count * capacity
    pick = targets[None, :] == jnp.arange(slot_count, dtype=jnp.int32)[:, None]
    pick_rows = jnp.any(pick.reshape(slot_count, own_count, top_count), axis=-1).astype(jnp.bfloat16)
    send_rows = jnp.dot(pick_rows, moe_in, preferred_element_type=jnp.float32).astype(jnp.bfloat16)
    grouped_rows = lax.all_to_all(
        send_rows.reshape(expert_count, capacity, model_width), "req", 0, 0, tiled=True
    )
    flat_rows = grouped_rows.reshape(-1, model_width)
    expert_sum = None
    for weights_now in shifted_weights:
        gate_out = jnp.dot(flat_rows, weights_now[0], preferred_element_type=jnp.float32)
        up_out = jnp.dot(flat_rows, weights_now[1], preferred_element_type=jnp.float32)
        activation = (jnp.maximum(gate_out, 0.0) * up_out).astype(jnp.bfloat16)
        partial = lax.dot_general(
            activation, weights_now[2], (((1,), (1,)), ((), ())), preferred_element_type=jnp.float32
        ).astype(jnp.bfloat16)
        expert_sum = partial.astype(jnp.float32) if expert_sum is None else expert_sum + partial
    expert_out = expert_sum.astype(jnp.bfloat16)
    returned = lax.all_to_all(
        expert_out.reshape(-1, capacity, model_width), "req", 0, 0, tiled=True
    )
    fetched = jnp.dot(
        pick.T.astype(jnp.bfloat16),
        returned.reshape(slot_count, model_width),
        preferred_element_type=jnp.float32,
    ).reshape(own_count, top_count, model_width)
    picked = jnp.take_along_axis(logits, own_routes, axis=1)
    gate_values = jax.nn.sigmoid(picked)
    weights = gate_values / jnp.sum(gate_values, axis=1, keepdims=True)
    moe_out = jnp.sum(weights[..., None] * fetched, axis=1)
    final_rows = (mid_stream.astype(jnp.float32) + moe_out).astype(jnp.bfloat16)
    return (final_rows[None], new_keys[None], new_values[None])


def solution(mesh):
    in_specs = (
        P("req", "hid", None),
        P("req", "hid", None),
        P("req", "hid", None),
        P("req", "hid", None),
        P("req"),
        P("req", None, None),
        P(),
        P(),
        P(),
        P(),
        P(),
        P(),
        P("req", None, None, "hid"),
        P("req", "hid", None),
    )
    out_specs = (P("req", "hid", None), P("req", "hid", None), P("req", "hid", None))
    return jax.shard_map(body, mesh=mesh, in_specs=in_specs, out_specs=out_specs, check_vma=False)
```

```python
import jax
import jax.numpy as jnp
from jax import lax
from jax.sharding import PartitionSpec as P
from jax.experimental import pallas as pl
from jax.experimental.pallas import tpu as pltpu
import functools

QH = 12
KVH = 2
HD = 128


EPS = 1e-06
MASKED_SCORE = -1e30
KEY_BLOCK = 512


def normalize(row_data, gain_vector):
    row_data = row_data.astype(jnp.float32)
    return (
        row_data
        * lax.rsqrt(jnp.mean(row_data * row_data, axis=-1, keepdims=True) + EPS)
        * gain_vector
    )


def absorb(state_now, grouped, key_rows, value_rows, visible):
    row_max, totals, accumulated = state_now
    scores = jnp.einsum(
        "tgsd,kgd->gstk", grouped, key_rows.reshape(-1, KVH, HD), preferred_element_type=jnp.float32
    ) * HD ** (-0.5)
    scores = jnp.where(visible, scores, MASKED_SCORE)
    new_max = jnp.maximum(row_max, jnp.max(scores, axis=-1))
    weights = jnp.where(visible, jnp.exp(scores - new_max[..., None]), 0.0)
    rescale = jnp.exp(row_max - new_max)
    totals = totals * rescale + jnp.sum(weights, axis=-1)
    accumulated = accumulated * rescale[..., None] + jnp.einsum(
        "gstk,kgd->gstd",
        weights.astype(jnp.bfloat16),
        value_rows.reshape(-1, KVH, HD),
        preferred_element_type=jnp.float32,
    )
    return (new_max, totals, accumulated)


def cache_block(state_now, grouped, key_rows, value_rows, first_pos, length):
    positions = first_pos + jnp.arange(key_rows.shape[0], dtype=jnp.int32)
    visible = (positions < length)[None, :]
    return lax.cond(
        first_pos < length,
        lambda current: absorb(current, grouped, key_rows, value_rows, visible),
        lambda current: current,
        state_now,
    )


def span_block(state_now, grouped, key_rows, value_rows, first_pos, query_pos):
    positions = first_pos + jnp.arange(key_rows.shape[0], dtype=jnp.int32)
    visible = positions[None, :] <= query_pos[:, None]
    return lax.cond(
        first_pos <= query_pos[-1],
        lambda current: absorb(current, grouped, key_rows, value_rows, visible),
        lambda current: current,
        state_now,
    )


def block_size(extent):
    return max(min(KEY_BLOCK, extent), extent // 8)


def empty_state(query_count):
    group_size = QH // KVH
    return (
        jnp.full((KVH, group_size, query_count), MASKED_SCORE, jnp.float32),
        jnp.zeros((KVH, group_size, query_count), jnp.float32),
        jnp.zeros((KVH, group_size, query_count, HD), jnp.float32),
    )


def attention_kernel(
    token_count,
    scalars,
    q_ref,
    k0_ref,
    k1_ref,
    k2_ref,
    k3_ref,
    v0_ref,
    v1_ref,
    v2_ref,
    v3_ref,
    kn_ref,
    vn_ref,
    o_ref,
    m_ref,
    l_ref,
    acc_ref,
    s_ref,
):
    length = scalars[0]
    hid_index = scalars[1]
    k_refs = (k0_ref, k1_ref, k2_ref, k3_ref)
    v_refs = (v0_ref, v1_ref, v2_ref, v3_ref)
    parts = len(k_refs)
    cache_rows = k0_ref.shape[0]
    rows = q_ref.shape[1]
    q = q_ref[0]
    m_ref[...] = jnp.full(m_ref.shape, MASKED_SCORE, jnp.float32)
    l_ref[...] = jnp.zeros(l_ref.shape, jnp.float32)
    acc_ref[...] = jnp.zeros(acc_ref.shape, jnp.float32)
    blocks = []
    for shift in range(parts):
        for first in range(0, cache_rows, KEY_BLOCK):
            blocks.append((shift, first, min(KEY_BLOCK, cache_rows - first), True))
    for part in range(parts):
        blocks.append((part, 0, token_count, False))

    def part_of(index, is_cache):
        return (hid_index - index + parts) % parts if is_cache else index

    def slot(index, first, is_cache):
        return index * cache_rows + first if is_cache else parts * cache_rows + index * token_count

    def live(index, first, size, is_cache):
        if is_cache:
            return part_of(index, True) * cache_rows + first < length
        return index <= hid_index

    def whole(index, first, size, is_cache):
        if is_cache:
            return part_of(index, True) * cache_rows + first + size <= length
        return index < hid_index

    def visible(index, first, size, is_cache):
        if is_cache:
            start = part_of(index, True) * cache_rows + first
            return start + lax.broadcasted_iota(jnp.int32, (1, size), 1) < length
        key_pos = index * token_count + lax.broadcasted_iota(jnp.int32, (1, size), 1)
        row_ids = lax.broadcasted_iota(jnp.int32, (rows, 1), 0)
        return key_pos <= hid_index * token_count + row_ids % token_count

    def first_pass(index, first, size, is_cache, masked):
        if is_cache:
            k = k_refs[index][pl.ds(first, size), :]
        else:
            k = kn_ref[index]
        raw = lax.dot_general(q, k, (((1,), (1,)), ((), ())), preferred_element_type=jnp.float32)
        s = raw * HD ** (-0.5)
        if masked:
            s = jnp.where(visible(index, first, size, is_cache), s, MASKED_SCORE)
        s_ref[:, pl.ds(slot(index, first, is_cache), size)] = s
        m_ref[...] = jnp.maximum(m_ref[...], jnp.max(s, axis=-1, keepdims=True))

    for index, first, size, is_cache in blocks:
        is_whole = whole(index, first, size, is_cache)
        pl.when(is_whole)(functools.partial(first_pass, index, first, size, is_cache, False))
        pl.when(jnp.logical_and(live(index, first, size, is_cache), jnp.logical_not(is_whole)))(
            functools.partial(first_pass, index, first, size, is_cache, True)
        )

    for index, first, size, is_cache in blocks:

        @pl.when(live(index, first, size, is_cache))
        def _():
            w = jnp.exp(s_ref[:, pl.ds(slot(index, first, is_cache), size)] - m_ref[...])
            l_ref[...] += jnp.sum(w, axis=-1, keepdims=True)
            v = v_refs[index][pl.ds(first, size), :] if is_cache else vn_ref[index]
            acc_ref[...] += jnp.dot(w.astype(jnp.bfloat16), v, preferred_element_type=jnp.float32)

    o_ref[0] = (acc_ref[...] / l_ref[...]).astype(o_ref.dtype)


def attention(grouped, shifted_kv, new_kv, length, hid_index, token_count, interpret=False):
    groups, rows, head = grouped.shape
    parts = len(shifted_kv)
    cache_rows = shifted_kv[0].shape[0]
    scalars = jnp.stack([length, hid_index]).astype(jnp.int32)
    k_spec = pl.BlockSpec((cache_rows, head), lambda g, s: (0, g))
    v_spec = pl.BlockSpec((cache_rows, head), lambda g, s: (0, groups + g))
    kn_spec = pl.BlockSpec((parts, token_count, head), lambda g, s: (0, 0, g))
    vn_spec = pl.BlockSpec((parts, token_count, head), lambda g, s: (0, 0, groups + g))
    row_spec = pl.BlockSpec((1, rows, head), lambda g, s: (g, 0, 0))
    return pl.pallas_call(
        functools.partial(attention_kernel, token_count),
        out_shape=jax.ShapeDtypeStruct((groups, rows, head), jnp.bfloat16),
        grid_spec=pltpu.PrefetchScalarGridSpec(
            num_scalar_prefetch=1,
            grid=(groups,),
            in_specs=[row_spec] + [k_spec] * parts + [v_spec] * parts + [kn_spec, vn_spec],
            out_specs=row_spec,
            scratch_shapes=[
                pltpu.VMEM((rows, 1), jnp.float32),
                pltpu.VMEM((rows, 1), jnp.float32),
                pltpu.VMEM((rows, head), jnp.float32),
                pltpu.VMEM((rows, parts * (cache_rows + token_count)), jnp.float32),
            ],
        ),
        interpret=interpret,
    )(scalars, grouped, *shifted_kv, *shifted_kv, new_kv, new_kv)


def ring_neighbours(shard, axis_name="hid"):
    count = lax.axis_size(axis_name)
    up = [(source, (source + 1) % count) for source in range(count)]
    down = [(source, (source - 1) % count) for source in range(count)]
    return lax.ppermute(shard, axis_name, up), lax.ppermute(shard, axis_name, down)


def ring_far(from_below, from_above, split_axis, axis_name="hid"):
    count = lax.axis_size(axis_name)
    up = [(source, (source + 1) % count) for source in range(count)]
    down = [(source, (source - 1) % count) for source in range(count)]
    extent = from_below.shape[split_axis]
    half = extent // 2
    return jnp.concatenate(
        [
            lax.ppermute(lax.slice_in_dim(from_below, 0, half, axis=split_axis), axis_name, up),
            lax.ppermute(lax.slice_in_dim(from_above, half, extent, axis=split_axis), axis_name, down),
        ],
        axis=split_axis,
    )


def ring_gather(shard, split_axis, axis_name="hid"):
    from_below, from_above = ring_neighbours(shard, axis_name)
    return [shard, from_below, ring_far(from_below, from_above, split_axis, axis_name), from_above]


def expert_activation(row_data, gate_weights):
    gate_out = jnp.dot(row_data, gate_weights[0], preferred_element_type=jnp.float32)
    up_out = jnp.dot(row_data, gate_weights[1], preferred_element_type=jnp.float32)
    return (jnp.maximum(gate_out, 0.0) * up_out).astype(jnp.bfloat16)


def body(
    hidden_in,
    queries,
    cache_keys,
    cache_values,
    lengths,
    routes,
    attn_gain,
    key_proj,
    value_proj,
    out_proj,
    moe_gain,
    router,
    gate_up,
    down_proj,
):
    own_count = hidden_in.shape[1]
    model_width = hidden_in.shape[2]
    hid_index = lax.axis_index("hid")
    hid_count = lax.axis_size("hid")
    group_size = QH // KVH
    normed = normalize(hidden_in[0], attn_gain).astype(jnp.bfloat16)
    key_width = key_proj.shape[1]
    new_kv = jnp.dot(
        normed, jnp.concatenate([key_proj, value_proj], axis=1), preferred_element_type=jnp.float32
    ).astype(jnp.bfloat16)
    new_keys = new_kv[:, :key_width]
    new_values = new_kv[:, key_width:]
    length = lengths[0]
    cache_local = cache_keys.shape[1]
    shifted_kv = ring_gather(jnp.concatenate([cache_keys[0], cache_values[0]], axis=1), 0)
    received = [new_kv]
    for shift in range(1, hid_count):
        pairs = [(source, source + shift) for source in range(hid_count - shift)]
        received.append(lax.ppermute(new_kv, "hid", pairs))
    new_parts = []
    for part in range(hid_count):
        distance = hid_index - part
        chosen = received[-1]
        for shift in range(hid_count - 2, -1, -1):
            chosen = jnp.where(distance == shift, received[shift], chosen)
        new_parts.append(chosen)
    new_parts = jnp.stack(new_parts)
    stacked_weights, _ = lax.optimization_barrier(
        (jnp.concatenate([gate_up[0], down_proj[0].T[None]], axis=0), shifted_kv[2])
    )
    weights_below, weights_above = ring_neighbours(stacked_weights)
    grouped = (
        queries[0]
        .reshape(own_count, KVH, group_size, HD)
        .transpose(1, 2, 0, 3)
        .reshape(KVH, group_size * own_count, HD)
    )
    attended = (
        attention(grouped, shifted_kv, new_parts, length, hid_index, own_count)
        .reshape(KVH, group_size, own_count, HD)
        .transpose(2, 0, 1, 3)
        .reshape(own_count, QH * HD)
    )
    mid_stream = (
        hidden_in[0].astype(jnp.float32)
        + jnp.dot(attended, out_proj, preferred_element_type=jnp.float32)
    ).astype(jnp.bfloat16)
    moe_in = normalize(mid_stream, moe_gain).astype(jnp.bfloat16)
    moe_in, weights_below, weights_above = lax.optimization_barrier(
        (moe_in, weights_below, weights_above)
    )
    shifted_weights = [
        stacked_weights,
        weights_below,
        ring_far(weights_below, weights_above, 1),
        weights_above,
    ]
    logits = jnp.dot(moe_in, router, preferred_element_type=jnp.float32)
    expert_count = router.shape[1]
    top_count = routes.shape[2]
    capacity = 2 * own_count * top_count // expert_count
    own_routes = lax.dynamic_slice_in_dim(routes[0], hid_index * own_count, own_count, axis=0)
    flat_routes = own_routes.reshape(-1)
    onehot = (flat_routes[:, None] == jnp.arange(expert_count, dtype=jnp.int32)[None, :]).astype(
        jnp.int32
    )
    slot_ids = jnp.sum((jnp.cumsum(onehot, axis=0) - 1) * onehot, axis=-1)
    targets = flat_routes * capacity + slot_ids
    slot_count = expert_count * capacity
    pick = targets[None, :] == jnp.arange(slot_count, dtype=jnp.int32)[:, None]
    pick_rows = jnp.any(pick.reshape(slot_count, own_count, top_count), axis=-1).astype(jnp.bfloat16)
    send_rows = jnp.dot(pick_rows, moe_in, preferred_element_type=jnp.float32).astype(jnp.bfloat16)
    grouped_rows = lax.all_to_all(
        send_rows.reshape(expert_count, capacity, model_width), "req", 0, 0, tiled=True
    )
    flat_rows = grouped_rows.reshape(-1, model_width)
    expert_sum = None
    for weights_now in shifted_weights:
        gate_out = jnp.dot(flat_rows, weights_now[0], preferred_element_type=jnp.float32)
        up_out = jnp.dot(flat_rows, weights_now[1], preferred_element_type=jnp.float32)
        activation = (jnp.maximum(gate_out, 0.0) * up_out).astype(jnp.bfloat16)
        partial = lax.dot_general(
            activation, weights_now[2], (((1,), (1,)), ((), ())), preferred_element_type=jnp.float32
        ).astype(jnp.bfloat16)
        expert_sum = partial.astype(jnp.float32) if expert_sum is None else expert_sum + partial
    expert_out = expert_sum.astype(jnp.bfloat16)
    returned = lax.all_to_all(
        expert_out.reshape(-1, capacity, model_width), "req", 0, 0, tiled=True
    )
    fetched = jnp.dot(
        pick.T.astype(jnp.bfloat16),
        returned.reshape(slot_count, model_width),
        preferred_element_type=jnp.float32,
    ).reshape(own_count, top_count, model_width)
    picked = jnp.take_along_axis(logits, own_routes, axis=1)
    gate_values = jax.nn.sigmoid(picked)
    weights = gate_values / jnp.sum(gate_values, axis=1, keepdims=True)
    moe_out = jnp.sum(weights[..., None] * fetched, axis=1)
    final_rows = (mid_stream.astype(jnp.float32) + moe_out).astype(jnp.bfloat16)
    return (final_rows[None], new_keys[None], new_values[None])


def solution(mesh):
    in_specs = (
        P("req", "hid", None),
        P("req", "hid", None),
        P("req", "hid", None),
        P("req", "hid", None),
        P("req"),
        P("req", None, None),
        P(),
        P(),
        P(),
        P(),
        P(),
        P(),
        P("req", None, None, "hid"),
        P("req", "hid", None),
    )
    out_specs = (P("req", "hid", None), P("req", "hid", None), P("req", "hid", None))
    return jax.shard_map(body, mesh=mesh, in_specs=in_specs, out_specs=out_specs, check_vma=False)
```

```python
import jax
import jax.numpy as jnp
from jax import lax
from jax.sharding import PartitionSpec as P
from jax.experimental import pallas as pl
from jax.experimental.pallas import tpu as pltpu
import functools

QH = 12
KVH = 2
HD = 128


EPS = 1e-06
MASKED_SCORE = -1e30
KEY_BLOCK = 512


def normalize(row_data, gain_vector):
    row_data = row_data.astype(jnp.float32)
    return (
        row_data
        * lax.rsqrt(jnp.mean(row_data * row_data, axis=-1, keepdims=True) + EPS)
        * gain_vector
    )


def absorb(state_now, grouped, key_rows, value_rows, visible):
    row_max, totals, accumulated = state_now
    scores = jnp.einsum(
        "tgsd,kgd->gstk", grouped, key_rows.reshape(-1, KVH, HD), preferred_element_type=jnp.float32
    ) * HD ** (-0.5)
    scores = jnp.where(visible, scores, MASKED_SCORE)
    new_max = jnp.maximum(row_max, jnp.max(scores, axis=-1))
    weights = jnp.where(visible, jnp.exp(scores - new_max[..., None]), 0.0)
    rescale = jnp.exp(row_max - new_max)
    totals = totals * rescale + jnp.sum(weights, axis=-1)
    accumulated = accumulated * rescale[..., None] + jnp.einsum(
        "gstk,kgd->gstd",
        weights.astype(jnp.bfloat16),
        value_rows.reshape(-1, KVH, HD),
        preferred_element_type=jnp.float32,
    )
    return (new_max, totals, accumulated)


def cache_block(state_now, grouped, key_rows, value_rows, first_pos, length):
    positions = first_pos + jnp.arange(key_rows.shape[0], dtype=jnp.int32)
    visible = (positions < length)[None, :]
    return lax.cond(
        first_pos < length,
        lambda current: absorb(current, grouped, key_rows, value_rows, visible),
        lambda current: current,
        state_now,
    )


def span_block(state_now, grouped, key_rows, value_rows, first_pos, query_pos):
    positions = first_pos + jnp.arange(key_rows.shape[0], dtype=jnp.int32)
    visible = positions[None, :] <= query_pos[:, None]
    return lax.cond(
        first_pos <= query_pos[-1],
        lambda current: absorb(current, grouped, key_rows, value_rows, visible),
        lambda current: current,
        state_now,
    )


def block_size(extent):
    return max(min(KEY_BLOCK, extent), extent // 8)


def empty_state(query_count):
    group_size = QH // KVH
    return (
        jnp.full((KVH, group_size, query_count), MASKED_SCORE, jnp.float32),
        jnp.zeros((KVH, group_size, query_count), jnp.float32),
        jnp.zeros((KVH, group_size, query_count, HD), jnp.float32),
    )


def attention_kernel(
    token_count,
    scalars,
    q_ref,
    k0_ref,
    k1_ref,
    k2_ref,
    k3_ref,
    v0_ref,
    v1_ref,
    v2_ref,
    v3_ref,
    kn_ref,
    vn_ref,
    o_ref,
    m_ref,
    l_ref,
    acc_ref,
    s_ref,
):
    length = scalars[0]
    hid_index = scalars[1]
    k_refs = (k0_ref, k1_ref, k2_ref, k3_ref)
    v_refs = (v0_ref, v1_ref, v2_ref, v3_ref)
    parts = len(k_refs)
    cache_rows = k0_ref.shape[0]
    rows = q_ref.shape[1]
    q = q_ref[0]
    m_ref[...] = jnp.full(m_ref.shape, MASKED_SCORE, jnp.float32)
    l_ref[...] = jnp.zeros(l_ref.shape, jnp.float32)
    acc_ref[...] = jnp.zeros(acc_ref.shape, jnp.float32)
    blocks = []
    for shift in range(parts):
        for first in range(0, cache_rows, KEY_BLOCK):
            blocks.append((shift, first, min(KEY_BLOCK, cache_rows - first), True))
    for part in range(parts):
        blocks.append((part, 0, token_count, False))

    def part_of(index, is_cache):
        return (hid_index - index + parts) % parts if is_cache else index

    def slot(index, first, is_cache):
        return index * cache_rows + first if is_cache else parts * cache_rows + index * token_count

    def live(index, first, size, is_cache):
        if is_cache:
            return part_of(index, True) * cache_rows + first < length
        return index <= hid_index

    def whole(index, first, size, is_cache):
        if is_cache:
            return part_of(index, True) * cache_rows + first + size <= length
        return index < hid_index

    def visible(index, first, size, is_cache):
        if is_cache:
            start = part_of(index, True) * cache_rows + first
            return start + lax.broadcasted_iota(jnp.int32, (1, size), 1) < length
        key_pos = index * token_count + lax.broadcasted_iota(jnp.int32, (1, size), 1)
        row_ids = lax.broadcasted_iota(jnp.int32, (rows, 1), 0)
        return key_pos <= hid_index * token_count + row_ids % token_count

    def first_pass(index, first, size, is_cache, masked):
        if is_cache:
            k = k_refs[index][pl.ds(first, size), :]
        else:
            k = kn_ref[index]
        raw = lax.dot_general(q, k, (((1,), (1,)), ((), ())), preferred_element_type=jnp.float32)
        s = raw * HD ** (-0.5)
        if masked:
            s = jnp.where(visible(index, first, size, is_cache), s, MASKED_SCORE)
        s_ref[:, pl.ds(slot(index, first, is_cache), size)] = s
        m_ref[...] = jnp.maximum(m_ref[...], jnp.max(s, axis=-1, keepdims=True))

    for index, first, size, is_cache in blocks:
        is_whole = whole(index, first, size, is_cache)
        pl.when(is_whole)(functools.partial(first_pass, index, first, size, is_cache, False))
        pl.when(jnp.logical_and(live(index, first, size, is_cache), jnp.logical_not(is_whole)))(
            functools.partial(first_pass, index, first, size, is_cache, True)
        )

    for index, first, size, is_cache in blocks:

        @pl.when(live(index, first, size, is_cache))
        def _():
            w = jnp.exp(s_ref[:, pl.ds(slot(index, first, is_cache), size)] - m_ref[...])
            l_ref[...] += jnp.sum(w, axis=-1, keepdims=True)
            v = v_refs[index][pl.ds(first, size), :] if is_cache else vn_ref[index]
            acc_ref[...] += jnp.dot(w.astype(jnp.bfloat16), v, preferred_element_type=jnp.float32)

    o_ref[0] = (acc_ref[...] / l_ref[...]).astype(o_ref.dtype)


def attention(grouped, shifted_kv, new_kv, length, hid_index, token_count, interpret=False):
    groups, rows, head = grouped.shape
    parts = len(shifted_kv)
    cache_rows = shifted_kv[0].shape[0]
    scalars = jnp.stack([length, hid_index]).astype(jnp.int32)
    k_spec = pl.BlockSpec((cache_rows, head), lambda g, s: (0, g))
    v_spec = pl.BlockSpec((cache_rows, head), lambda g, s: (0, groups + g))
    kn_spec = pl.BlockSpec((parts, token_count, head), lambda g, s: (0, 0, g))
    vn_spec = pl.BlockSpec((parts, token_count, head), lambda g, s: (0, 0, groups + g))
    row_spec = pl.BlockSpec((1, rows, head), lambda g, s: (g, 0, 0))
    return pl.pallas_call(
        functools.partial(attention_kernel, token_count),
        out_shape=jax.ShapeDtypeStruct((groups, rows, head), jnp.bfloat16),
        grid_spec=pltpu.PrefetchScalarGridSpec(
            num_scalar_prefetch=1,
            grid=(groups,),
            in_specs=[row_spec] + [k_spec] * parts + [v_spec] * parts + [kn_spec, vn_spec],
            out_specs=row_spec,
            scratch_shapes=[
                pltpu.VMEM((rows, 1), jnp.float32),
                pltpu.VMEM((rows, 1), jnp.float32),
                pltpu.VMEM((rows, head), jnp.float32),
                pltpu.VMEM((rows, parts * (cache_rows + token_count)), jnp.float32),
            ],
        ),
        interpret=interpret,
    )(scalars, grouped, *shifted_kv, *shifted_kv, new_kv, new_kv)


def ring_neighbours(shard, axis_name="hid"):
    count = lax.axis_size(axis_name)
    up = [(source, (source + 1) % count) for source in range(count)]
    down = [(source, (source - 1) % count) for source in range(count)]
    return lax.ppermute(shard, axis_name, up), lax.ppermute(shard, axis_name, down)


def ring_far(from_below, from_above, split_axis, axis_name="hid"):
    count = lax.axis_size(axis_name)
    up = [(source, (source + 1) % count) for source in range(count)]
    down = [(source, (source - 1) % count) for source in range(count)]
    extent = from_below.shape[split_axis]
    half = extent // 2
    return jnp.concatenate(
        [
            lax.ppermute(lax.slice_in_dim(from_below, 0, half, axis=split_axis), axis_name, up),
            lax.ppermute(lax.slice_in_dim(from_above, half, extent, axis=split_axis), axis_name, down),
        ],
        axis=split_axis,
    )


def ring_gather(shard, split_axis, axis_name="hid"):
    from_below, from_above = ring_neighbours(shard, axis_name)
    return [shard, from_below, ring_far(from_below, from_above, split_axis, axis_name), from_above]


def expert_activation(row_data, gate_weights):
    gate_out = jnp.dot(row_data, gate_weights[0], preferred_element_type=jnp.float32)
    up_out = jnp.dot(row_data, gate_weights[1], preferred_element_type=jnp.float32)
    return (jnp.maximum(gate_out, 0.0) * up_out).astype(jnp.bfloat16)


def body(
    hidden_in,
    queries,
    cache_keys,
    cache_values,
    lengths,
    routes,
    attn_gain,
    key_proj,
    value_proj,
    out_proj,
    moe_gain,
    router,
    gate_up,
    down_proj,
):
    own_count = hidden_in.shape[1]
    model_width = hidden_in.shape[2]
    hid_index = lax.axis_index("hid")
    hid_count = lax.axis_size("hid")
    group_size = QH // KVH
    normed = normalize(hidden_in[0], attn_gain).astype(jnp.bfloat16)
    key_width = key_proj.shape[1]
    new_kv = jnp.dot(
        normed, jnp.concatenate([key_proj, value_proj], axis=1), preferred_element_type=jnp.float32
    ).astype(jnp.bfloat16)
    new_keys = new_kv[:, :key_width]
    new_values = new_kv[:, key_width:]
    length = lengths[0]
    cache_local = cache_keys.shape[1]
    shifted_kv = ring_gather(jnp.concatenate([cache_keys[0], cache_values[0]], axis=1), 0)
    received = [new_kv]
    for shift in range(1, hid_count):
        pairs = [(source, source + shift) for source in range(hid_count - shift)]
        received.append(lax.ppermute(new_kv, "hid", pairs))
    new_parts = []
    for part in range(hid_count):
        distance = hid_index - part
        chosen = received[-1]
        for shift in range(hid_count - 2, -1, -1):
            chosen = jnp.where(distance == shift, received[shift], chosen)
        new_parts.append(chosen)
    new_parts = jnp.stack(new_parts)
    stacked_weights, _, _ = lax.optimization_barrier(
        (jnp.concatenate([gate_up[0], down_proj[0].T[None]], axis=0), shifted_kv[2], new_parts)
    )
    weights_below, weights_above = ring_neighbours(stacked_weights)
    grouped = (
        queries[0]
        .reshape(own_count, KVH, group_size, HD)
        .transpose(1, 2, 0, 3)
        .reshape(KVH, group_size * own_count, HD)
    )
    attended = (
        attention(grouped, shifted_kv, new_parts, length, hid_index, own_count)
        .reshape(KVH, group_size, own_count, HD)
        .transpose(2, 0, 1, 3)
        .reshape(own_count, QH * HD)
    )
    mid_stream = (
        hidden_in[0].astype(jnp.float32)
        + jnp.dot(attended, out_proj, preferred_element_type=jnp.float32)
    ).astype(jnp.bfloat16)
    moe_in = normalize(mid_stream, moe_gain).astype(jnp.bfloat16)
    moe_in, weights_below, weights_above = lax.optimization_barrier(
        (moe_in, weights_below, weights_above)
    )
    all_weights = jnp.stack(
        [stacked_weights, weights_below, ring_far(weights_below, weights_above, 1), weights_above]
    )
    logits = jnp.dot(moe_in, router, preferred_element_type=jnp.float32)
    expert_count = router.shape[1]
    top_count = routes.shape[2]
    capacity = 2 * own_count * top_count // expert_count
    own_routes = lax.dynamic_slice_in_dim(routes[0], hid_index * own_count, own_count, axis=0)
    flat_routes = own_routes.reshape(-1)
    onehot = (flat_routes[:, None] == jnp.arange(expert_count, dtype=jnp.int32)[None, :]).astype(
        jnp.int32
    )
    slot_ids = jnp.sum((jnp.cumsum(onehot, axis=0) - 1) * onehot, axis=-1)
    targets = flat_routes * capacity + slot_ids
    slot_count = expert_count * capacity
    pick = targets[None, :] == jnp.arange(slot_count, dtype=jnp.int32)[:, None]
    pick_rows = jnp.any(pick.reshape(slot_count, own_count, top_count), axis=-1).astype(jnp.bfloat16)
    send_rows = jnp.dot(pick_rows, moe_in, preferred_element_type=jnp.float32).astype(jnp.bfloat16)
    grouped_rows = lax.all_to_all(
        send_rows.reshape(expert_count, capacity, model_width), "req", 0, 0, tiled=True
    )
    flat_rows = grouped_rows.reshape(-1, model_width)
    gate_out = jnp.einsum(
        "nd,hdf->hnf", flat_rows, all_weights[:, 0], preferred_element_type=jnp.float32
    )
    up_out = jnp.einsum(
        "nd,hdf->hnf", flat_rows, all_weights[:, 1], preferred_element_type=jnp.float32
    )
    activation = (jnp.maximum(gate_out, 0.0) * up_out).astype(jnp.bfloat16)
    partials = jnp.einsum(
        "hnf,hdf->hnd", activation, all_weights[:, 2], preferred_element_type=jnp.float32
    ).astype(jnp.bfloat16)
    expert_out = jnp.sum(partials.astype(jnp.float32), axis=0).astype(jnp.bfloat16)
    returned = lax.all_to_all(
        expert_out.reshape(-1, capacity, model_width), "req", 0, 0, tiled=True
    )
    fetched = jnp.dot(
        pick.T.astype(jnp.bfloat16),
        returned.reshape(slot_count, model_width),
        preferred_element_type=jnp.float32,
    ).reshape(own_count, top_count, model_width)
    picked = jnp.take_along_axis(logits, own_routes, axis=1)
    gate_values = jax.nn.sigmoid(picked)
    weights = gate_values / jnp.sum(gate_values, axis=1, keepdims=True)
    moe_out = jnp.sum(weights[..., None] * fetched, axis=1)
    final_rows = (mid_stream.astype(jnp.float32) + moe_out).astype(jnp.bfloat16)
    return (final_rows[None], new_keys[None], new_values[None])


def solution(mesh):
    in_specs = (
        P("req", "hid", None),
        P("req", "hid", None),
        P("req", "hid", None),
        P("req", "hid", None),
        P("req"),
        P("req", None, None),
        P(),
        P(),
        P(),
        P(),
        P(),
        P(),
        P("req", None, None, "hid"),
        P("req", "hid", None),
    )
    out_specs = (P("req", "hid", None), P("req", "hid", None), P("req", "hid", None))
    return jax.shard_map(body, mesh=mesh, in_specs=in_specs, out_specs=out_specs, check_vma=False)
```

```python
import jax
import jax.numpy as jnp
from jax import lax
from jax.sharding import PartitionSpec as P
from jax.experimental import pallas as pl
from jax.experimental.pallas import tpu as pltpu
import functools

QH = 12
KVH = 2
HD = 128


EPS = 1e-06
MASKED_SCORE = -1e30
KEY_BLOCK = 512


def normalize(row_data, gain_vector):
    row_data = row_data.astype(jnp.float32)
    return (
        row_data
        * lax.rsqrt(jnp.mean(row_data * row_data, axis=-1, keepdims=True) + EPS)
        * gain_vector
    )


def absorb(state_now, grouped, key_rows, value_rows, visible):
    row_max, totals, accumulated = state_now
    scores = jnp.einsum(
        "tgsd,kgd->gstk", grouped, key_rows.reshape(-1, KVH, HD), preferred_element_type=jnp.float32
    ) * HD ** (-0.5)
    scores = jnp.where(visible, scores, MASKED_SCORE)
    new_max = jnp.maximum(row_max, jnp.max(scores, axis=-1))
    weights = jnp.where(visible, jnp.exp(scores - new_max[..., None]), 0.0)
    rescale = jnp.exp(row_max - new_max)
    totals = totals * rescale + jnp.sum(weights, axis=-1)
    accumulated = accumulated * rescale[..., None] + jnp.einsum(
        "gstk,kgd->gstd",
        weights.astype(jnp.bfloat16),
        value_rows.reshape(-1, KVH, HD),
        preferred_element_type=jnp.float32,
    )
    return (new_max, totals, accumulated)


def cache_block(state_now, grouped, key_rows, value_rows, first_pos, length):
    positions = first_pos + jnp.arange(key_rows.shape[0], dtype=jnp.int32)
    visible = (positions < length)[None, :]
    return lax.cond(
        first_pos < length,
        lambda current: absorb(current, grouped, key_rows, value_rows, visible),
        lambda current: current,
        state_now,
    )


def span_block(state_now, grouped, key_rows, value_rows, first_pos, query_pos):
    positions = first_pos + jnp.arange(key_rows.shape[0], dtype=jnp.int32)
    visible = positions[None, :] <= query_pos[:, None]
    return lax.cond(
        first_pos <= query_pos[-1],
        lambda current: absorb(current, grouped, key_rows, value_rows, visible),
        lambda current: current,
        state_now,
    )


def block_size(extent):
    return max(min(KEY_BLOCK, extent), extent // 8)


def empty_state(query_count):
    group_size = QH // KVH
    return (
        jnp.full((KVH, group_size, query_count), MASKED_SCORE, jnp.float32),
        jnp.zeros((KVH, group_size, query_count), jnp.float32),
        jnp.zeros((KVH, group_size, query_count, HD), jnp.float32),
    )


def attention_kernel(
    token_count,
    scalars,
    q_ref,
    k0_ref,
    k1_ref,
    k2_ref,
    k3_ref,
    v0_ref,
    v1_ref,
    v2_ref,
    v3_ref,
    kn_ref,
    vn_ref,
    o_ref,
    m_ref,
    l_ref,
    acc_ref,
    s_ref,
):
    length = scalars[0]
    hid_index = scalars[1]
    k_refs = (k0_ref, k1_ref, k2_ref, k3_ref)
    v_refs = (v0_ref, v1_ref, v2_ref, v3_ref)
    parts = len(k_refs)
    cache_rows = k0_ref.shape[0]
    rows = q_ref.shape[1]
    q = q_ref[0]
    m_ref[...] = jnp.full(m_ref.shape, MASKED_SCORE, jnp.float32)
    l_ref[...] = jnp.zeros(l_ref.shape, jnp.float32)
    acc_ref[...] = jnp.zeros(acc_ref.shape, jnp.float32)
    blocks = []
    for shift in range(parts):
        for first in range(0, cache_rows, KEY_BLOCK):
            blocks.append((shift, first, min(KEY_BLOCK, cache_rows - first), True))
    for part in range(parts):
        blocks.append((part, 0, token_count, False))

    def part_of(index, is_cache):
        return (hid_index - index + parts) % parts if is_cache else index

    def slot(index, first, is_cache):
        return index * cache_rows + first if is_cache else parts * cache_rows + index * token_count

    def live(index, first, size, is_cache):
        if is_cache:
            return part_of(index, True) * cache_rows + first < length
        return index <= hid_index

    def whole(index, first, size, is_cache):
        if is_cache:
            return part_of(index, True) * cache_rows + first + size <= length
        return index < hid_index

    def visible(index, first, size, is_cache):
        if is_cache:
            start = part_of(index, True) * cache_rows + first
            return start + lax.broadcasted_iota(jnp.int32, (1, size), 1) < length
        key_pos = index * token_count + lax.broadcasted_iota(jnp.int32, (1, size), 1)
        row_ids = lax.broadcasted_iota(jnp.int32, (rows, 1), 0)
        return key_pos <= hid_index * token_count + row_ids % token_count

    def first_pass(index, first, size, is_cache, masked):
        if is_cache:
            k = k_refs[index][pl.ds(first, size), :]
        else:
            k = kn_ref[index]
        raw = lax.dot_general(q, k, (((1,), (1,)), ((), ())), preferred_element_type=jnp.float32)
        s = raw * HD ** (-0.5)
        if masked:
            s = jnp.where(visible(index, first, size, is_cache), s, MASKED_SCORE)
        s_ref[:, pl.ds(slot(index, first, is_cache), size)] = s
        m_ref[...] = jnp.maximum(m_ref[...], jnp.max(s, axis=-1, keepdims=True))

    for index, first, size, is_cache in blocks:
        is_whole = whole(index, first, size, is_cache)
        pl.when(is_whole)(functools.partial(first_pass, index, first, size, is_cache, False))
        pl.when(jnp.logical_and(live(index, first, size, is_cache), jnp.logical_not(is_whole)))(
            functools.partial(first_pass, index, first, size, is_cache, True)
        )

    for index, first, size, is_cache in blocks:

        @pl.when(live(index, first, size, is_cache))
        def _():
            w = jnp.exp(s_ref[:, pl.ds(slot(index, first, is_cache), size)] - m_ref[...])
            l_ref[...] += jnp.sum(w, axis=-1, keepdims=True)
            v = v_refs[index][pl.ds(first, size), :] if is_cache else vn_ref[index]
            acc_ref[...] += jnp.dot(w.astype(jnp.bfloat16), v, preferred_element_type=jnp.float32)

    o_ref[0] = (acc_ref[...] / l_ref[...]).astype(o_ref.dtype)


def attention(grouped, shifted_kv, new_kv, length, hid_index, token_count, interpret=False):
    groups, rows, head = grouped.shape
    parts = len(shifted_kv)
    cache_rows = shifted_kv[0].shape[0]
    scalars = jnp.stack([length, hid_index]).astype(jnp.int32)
    k_spec = pl.BlockSpec((cache_rows, head), lambda g, s: (0, g))
    v_spec = pl.BlockSpec((cache_rows, head), lambda g, s: (0, groups + g))
    kn_spec = pl.BlockSpec((parts, token_count, head), lambda g, s: (0, 0, g))
    vn_spec = pl.BlockSpec((parts, token_count, head), lambda g, s: (0, 0, groups + g))
    row_spec = pl.BlockSpec((1, rows, head), lambda g, s: (g, 0, 0))
    return pl.pallas_call(
        functools.partial(attention_kernel, token_count),
        out_shape=jax.ShapeDtypeStruct((groups, rows, head), jnp.bfloat16),
        grid_spec=pltpu.PrefetchScalarGridSpec(
            num_scalar_prefetch=1,
            grid=(groups,),
            in_specs=[row_spec] + [k_spec] * parts + [v_spec] * parts + [kn_spec, vn_spec],
            out_specs=row_spec,
            scratch_shapes=[
                pltpu.VMEM((rows, 1), jnp.float32),
                pltpu.VMEM((rows, 1), jnp.float32),
                pltpu.VMEM((rows, head), jnp.float32),
                pltpu.VMEM((rows, parts * (cache_rows + token_count)), jnp.float32),
            ],
        ),
        interpret=interpret,
    )(scalars, grouped, *shifted_kv, *shifted_kv, new_kv, new_kv)


def ring_neighbours(shard, axis_name="hid"):
    count = lax.axis_size(axis_name)
    up = [(source, (source + 1) % count) for source in range(count)]
    down = [(source, (source - 1) % count) for source in range(count)]
    return lax.ppermute(shard, axis_name, up), lax.ppermute(shard, axis_name, down)


def ring_far(from_below, from_above, split_axis, axis_name="hid"):
    count = lax.axis_size(axis_name)
    up = [(source, (source + 1) % count) for source in range(count)]
    down = [(source, (source - 1) % count) for source in range(count)]
    extent = from_below.shape[split_axis]
    half = extent // 2
    return jnp.concatenate(
        [
            lax.ppermute(lax.slice_in_dim(from_below, 0, half, axis=split_axis), axis_name, up),
            lax.ppermute(lax.slice_in_dim(from_above, half, extent, axis=split_axis), axis_name, down),
        ],
        axis=split_axis,
    )


def ring_gather(shard, split_axis, axis_name="hid"):
    from_below, from_above = ring_neighbours(shard, axis_name)
    return [shard, from_below, ring_far(from_below, from_above, split_axis, axis_name), from_above]


def expert_activation(row_data, gate_weights):
    gate_out = jnp.dot(row_data, gate_weights[0], preferred_element_type=jnp.float32)
    up_out = jnp.dot(row_data, gate_weights[1], preferred_element_type=jnp.float32)
    return (jnp.maximum(gate_out, 0.0) * up_out).astype(jnp.bfloat16)


def body(
    hidden_in,
    queries,
    cache_keys,
    cache_values,
    lengths,
    routes,
    attn_gain,
    key_proj,
    value_proj,
    out_proj,
    moe_gain,
    router,
    gate_up,
    down_proj,
):
    own_count = hidden_in.shape[1]
    model_width = hidden_in.shape[2]
    hid_index = lax.axis_index("hid")
    hid_count = lax.axis_size("hid")
    group_size = QH // KVH
    normed = normalize(hidden_in[0], attn_gain).astype(jnp.bfloat16)
    key_width = key_proj.shape[1]
    new_kv = jnp.dot(
        normed, jnp.concatenate([key_proj, value_proj], axis=1), preferred_element_type=jnp.float32
    ).astype(jnp.bfloat16)
    new_keys = new_kv[:, :key_width]
    new_values = new_kv[:, key_width:]
    length = lengths[0]
    cache_local = cache_keys.shape[1]
    shifted_kv = ring_gather(jnp.concatenate([cache_keys[0], cache_values[0]], axis=1), 0)
    received = [new_kv]
    for shift in range(1, hid_count):
        pairs = [(source, source + shift) for source in range(hid_count - shift)]
        received.append(lax.ppermute(new_kv, "hid", pairs))
    new_parts = []
    for part in range(hid_count):
        distance = hid_index - part
        chosen = received[-1]
        for shift in range(hid_count - 2, -1, -1):
            chosen = jnp.where(distance == shift, received[shift], chosen)
        new_parts.append(chosen)
    new_parts = jnp.stack(new_parts)
    stacked_weights, _, _ = lax.optimization_barrier(
        (jnp.concatenate([gate_up[0], down_proj[0].T[None]], axis=0), shifted_kv[2], new_parts)
    )
    weights_below, weights_above = ring_neighbours(stacked_weights)
    grouped = (
        queries[0]
        .reshape(own_count, KVH, group_size, HD)
        .transpose(1, 2, 0, 3)
        .reshape(KVH, group_size * own_count, HD)
    )
    attended = (
        attention(grouped, shifted_kv, new_parts, length, hid_index, own_count)
        .reshape(KVH, group_size, own_count, HD)
        .transpose(2, 0, 1, 3)
        .reshape(own_count, QH * HD)
    )
    mid_stream = (
        hidden_in[0].astype(jnp.float32)
        + jnp.dot(attended, out_proj, preferred_element_type=jnp.float32)
    ).astype(jnp.bfloat16)
    moe_in = normalize(mid_stream, moe_gain).astype(jnp.bfloat16)
    logits = jnp.dot(moe_in, router, preferred_element_type=jnp.float32)
    expert_count = router.shape[1]
    top_count = routes.shape[2]
    capacity = 2 * own_count * top_count // expert_count
    own_routes = lax.dynamic_slice_in_dim(routes[0], hid_index * own_count, own_count, axis=0)
    flat_routes = own_routes.reshape(-1)
    onehot = (flat_routes[:, None] == jnp.arange(expert_count, dtype=jnp.int32)[None, :]).astype(
        jnp.int32
    )
    slot_ids = jnp.sum((jnp.cumsum(onehot, axis=0) - 1) * onehot, axis=-1)
    targets = flat_routes * capacity + slot_ids
    slot_count = expert_count * capacity
    pick = targets[None, :] == jnp.arange(slot_count, dtype=jnp.int32)[:, None]
    pick_rows = jnp.any(pick.reshape(slot_count, own_count, top_count), axis=-1).astype(jnp.bfloat16)
    send_rows = jnp.dot(pick_rows, moe_in, preferred_element_type=jnp.float32).astype(jnp.bfloat16)
    send_rows, weights_below, weights_above = lax.optimization_barrier(
        (send_rows, weights_below, weights_above)
    )
    all_weights = jnp.stack(
        [stacked_weights, weights_below, ring_far(weights_below, weights_above, 1), weights_above]
    )
    grouped_rows = lax.all_to_all(
        send_rows.reshape(expert_count, capacity, model_width), "req", 0, 0, tiled=True
    )
    flat_rows = grouped_rows.reshape(-1, model_width)
    gate_out = jnp.einsum(
        "nd,hdf->hnf", flat_rows, all_weights[:, 0], preferred_element_type=jnp.float32
    )
    up_out = jnp.einsum(
        "nd,hdf->hnf", flat_rows, all_weights[:, 1], preferred_element_type=jnp.float32
    )
    activation = (jnp.maximum(gate_out, 0.0) * up_out).astype(jnp.bfloat16)
    partials = jnp.einsum(
        "hnf,hdf->hnd", activation, all_weights[:, 2], preferred_element_type=jnp.float32
    ).astype(jnp.bfloat16)
    expert_out = jnp.sum(partials.astype(jnp.float32), axis=0).astype(jnp.bfloat16)
    returned = lax.all_to_all(
        expert_out.reshape(-1, capacity, model_width), "req", 0, 0, tiled=True
    )
    fetched = jnp.dot(
        pick.T.astype(jnp.bfloat16),
        returned.reshape(slot_count, model_width),
        preferred_element_type=jnp.float32,
    ).reshape(own_count, top_count, model_width)
    picked = jnp.take_along_axis(logits, own_routes, axis=1)
    gate_values = jax.nn.sigmoid(picked)
    weights = gate_values / jnp.sum(gate_values, axis=1, keepdims=True)
    moe_out = jnp.sum(weights[..., None] * fetched, axis=1)
    final_rows = (mid_stream.astype(jnp.float32) + moe_out).astype(jnp.bfloat16)
    return (final_rows[None], new_keys[None], new_values[None])


def solution(mesh):
    in_specs = (
        P("req", "hid", None),
        P("req", "hid", None),
        P("req", "hid", None),
        P("req", "hid", None),
        P("req"),
        P("req", None, None),
        P(),
        P(),
        P(),
        P(),
        P(),
        P(),
        P("req", None, None, "hid"),
        P("req", "hid", None),
    )
    out_specs = (P("req", "hid", None), P("req", "hid", None), P("req", "hid", None))
    return jax.shard_map(body, mesh=mesh, in_specs=in_specs, out_specs=out_specs, check_vma=False)
```

```python
import jax
import jax.numpy as jnp
from jax import lax
from jax.sharding import PartitionSpec as P
from jax.experimental import pallas as pl
from jax.experimental.pallas import tpu as pltpu
import functools

QH = 12
KVH = 2
HD = 128


EPS = 1e-06
MASKED_SCORE = -1e30
KEY_BLOCK = 512


def normalize(row_data, gain_vector):
    row_data = row_data.astype(jnp.float32)
    return (
        row_data
        * lax.rsqrt(jnp.mean(row_data * row_data, axis=-1, keepdims=True) + EPS)
        * gain_vector
    )


def absorb(state_now, grouped, key_rows, value_rows, visible):
    row_max, totals, accumulated = state_now
    scores = jnp.einsum(
        "tgsd,kgd->gstk", grouped, key_rows.reshape(-1, KVH, HD), preferred_element_type=jnp.float32
    ) * HD ** (-0.5)
    scores = jnp.where(visible, scores, MASKED_SCORE)
    new_max = jnp.maximum(row_max, jnp.max(scores, axis=-1))
    weights = jnp.where(visible, jnp.exp(scores - new_max[..., None]), 0.0)
    rescale = jnp.exp(row_max - new_max)
    totals = totals * rescale + jnp.sum(weights, axis=-1)
    accumulated = accumulated * rescale[..., None] + jnp.einsum(
        "gstk,kgd->gstd",
        weights.astype(jnp.bfloat16),
        value_rows.reshape(-1, KVH, HD),
        preferred_element_type=jnp.float32,
    )
    return (new_max, totals, accumulated)


def cache_block(state_now, grouped, key_rows, value_rows, first_pos, length):
    positions = first_pos + jnp.arange(key_rows.shape[0], dtype=jnp.int32)
    visible = (positions < length)[None, :]
    return lax.cond(
        first_pos < length,
        lambda current: absorb(current, grouped, key_rows, value_rows, visible),
        lambda current: current,
        state_now,
    )


def span_block(state_now, grouped, key_rows, value_rows, first_pos, query_pos):
    positions = first_pos + jnp.arange(key_rows.shape[0], dtype=jnp.int32)
    visible = positions[None, :] <= query_pos[:, None]
    return lax.cond(
        first_pos <= query_pos[-1],
        lambda current: absorb(current, grouped, key_rows, value_rows, visible),
        lambda current: current,
        state_now,
    )


def block_size(extent):
    return max(min(KEY_BLOCK, extent), extent // 8)


def empty_state(query_count):
    group_size = QH // KVH
    return (
        jnp.full((KVH, group_size, query_count), MASKED_SCORE, jnp.float32),
        jnp.zeros((KVH, group_size, query_count), jnp.float32),
        jnp.zeros((KVH, group_size, query_count, HD), jnp.float32),
    )


def attention_kernel(
    token_count,
    scalars,
    q_ref,
    k0_ref,
    k1_ref,
    k2_ref,
    k3_ref,
    v0_ref,
    v1_ref,
    v2_ref,
    v3_ref,
    kn_ref,
    vn_ref,
    o_ref,
    m_ref,
    l_ref,
    acc_ref,
    s_ref,
):
    length = scalars[0]
    hid_index = scalars[1]
    k_refs = (k0_ref, k1_ref, k2_ref, k3_ref)
    v_refs = (v0_ref, v1_ref, v2_ref, v3_ref)
    parts = len(k_refs)
    cache_rows = k0_ref.shape[0]
    rows = q_ref.shape[1]
    q = q_ref[0]
    m_ref[...] = jnp.full(m_ref.shape, MASKED_SCORE, jnp.float32)
    l_ref[...] = jnp.zeros(l_ref.shape, jnp.float32)
    acc_ref[...] = jnp.zeros(acc_ref.shape, jnp.float32)
    blocks = []
    for shift in range(parts):
        for first in range(0, cache_rows, KEY_BLOCK):
            blocks.append((shift, first, min(KEY_BLOCK, cache_rows - first), True))
    for part in range(parts):
        blocks.append((part, 0, token_count, False))

    def part_of(index, is_cache):
        return (hid_index - index + parts) % parts if is_cache else index

    def slot(index, first, is_cache):
        return index * cache_rows + first if is_cache else parts * cache_rows + index * token_count

    def live(index, first, size, is_cache):
        if is_cache:
            return part_of(index, True) * cache_rows + first < length
        return index <= hid_index

    def whole(index, first, size, is_cache):
        if is_cache:
            return part_of(index, True) * cache_rows + first + size <= length
        return index < hid_index

    def visible(index, first, size, is_cache):
        if is_cache:
            start = part_of(index, True) * cache_rows + first
            return start + lax.broadcasted_iota(jnp.int32, (1, size), 1) < length
        key_pos = index * token_count + lax.broadcasted_iota(jnp.int32, (1, size), 1)
        row_ids = lax.broadcasted_iota(jnp.int32, (rows, 1), 0)
        return key_pos <= hid_index * token_count + row_ids % token_count

    def first_pass(index, first, size, is_cache, masked):
        if is_cache:
            k = k_refs[index][pl.ds(first, size), :]
        else:
            k = kn_ref[index]
        raw = lax.dot_general(q, k, (((1,), (1,)), ((), ())), preferred_element_type=jnp.float32)
        s = raw * HD ** (-0.5)
        if masked:
            s = jnp.where(visible(index, first, size, is_cache), s, MASKED_SCORE)
        s_ref[:, pl.ds(slot(index, first, is_cache), size)] = s
        m_ref[...] = jnp.maximum(m_ref[...], jnp.max(s, axis=-1, keepdims=True))

    for index, first, size, is_cache in blocks:
        is_whole = whole(index, first, size, is_cache)
        pl.when(is_whole)(functools.partial(first_pass, index, first, size, is_cache, False))
        pl.when(jnp.logical_and(live(index, first, size, is_cache), jnp.logical_not(is_whole)))(
            functools.partial(first_pass, index, first, size, is_cache, True)
        )

    for index, first, size, is_cache in blocks:

        @pl.when(live(index, first, size, is_cache))
        def _():
            w = jnp.exp(s_ref[:, pl.ds(slot(index, first, is_cache), size)] - m_ref[...])
            l_ref[...] += jnp.sum(w, axis=-1, keepdims=True)
            v = v_refs[index][pl.ds(first, size), :] if is_cache else vn_ref[index]
            acc_ref[...] += jnp.dot(w.astype(jnp.bfloat16), v, preferred_element_type=jnp.float32)

    o_ref[0] = (acc_ref[...] / l_ref[...]).astype(o_ref.dtype)


def attention(grouped, shifted_kv, new_kv, length, hid_index, token_count, interpret=False):
    groups, rows, head = grouped.shape
    parts = len(shifted_kv)
    cache_rows = shifted_kv[0].shape[0]
    scalars = jnp.stack([length, hid_index]).astype(jnp.int32)
    k_spec = pl.BlockSpec((cache_rows, head), lambda g, s: (0, g))
    v_spec = pl.BlockSpec((cache_rows, head), lambda g, s: (0, groups + g))
    kn_spec = pl.BlockSpec((parts, token_count, head), lambda g, s: (0, 0, g))
    vn_spec = pl.BlockSpec((parts, token_count, head), lambda g, s: (0, 0, groups + g))
    row_spec = pl.BlockSpec((1, rows, head), lambda g, s: (g, 0, 0))
    return pl.pallas_call(
        functools.partial(attention_kernel, token_count),
        out_shape=jax.ShapeDtypeStruct((groups, rows, head), jnp.bfloat16),
        grid_spec=pltpu.PrefetchScalarGridSpec(
            num_scalar_prefetch=1,
            grid=(groups,),
            in_specs=[row_spec] + [k_spec] * parts + [v_spec] * parts + [kn_spec, vn_spec],
            out_specs=row_spec,
            scratch_shapes=[
                pltpu.VMEM((rows, 1), jnp.float32),
                pltpu.VMEM((rows, 1), jnp.float32),
                pltpu.VMEM((rows, head), jnp.float32),
                pltpu.VMEM((rows, parts * (cache_rows + token_count)), jnp.float32),
            ],
        ),
        interpret=interpret,
    )(scalars, grouped, *shifted_kv, *shifted_kv, new_kv, new_kv)


def ring_neighbours(shard, axis_name="hid"):
    count = lax.axis_size(axis_name)
    up = [(source, (source + 1) % count) for source in range(count)]
    down = [(source, (source - 1) % count) for source in range(count)]
    return lax.ppermute(shard, axis_name, up), lax.ppermute(shard, axis_name, down)


def ring_far(from_below, from_above, split_axis, axis_name="hid"):
    count = lax.axis_size(axis_name)
    up = [(source, (source + 1) % count) for source in range(count)]
    down = [(source, (source - 1) % count) for source in range(count)]
    extent = from_below.shape[split_axis]
    half = extent // 2
    return jnp.concatenate(
        [
            lax.ppermute(lax.slice_in_dim(from_below, 0, half, axis=split_axis), axis_name, up),
            lax.ppermute(lax.slice_in_dim(from_above, half, extent, axis=split_axis), axis_name, down),
        ],
        axis=split_axis,
    )


def ring_gather(shard, split_axis, axis_name="hid"):
    from_below, from_above = ring_neighbours(shard, axis_name)
    return [shard, from_below, ring_far(from_below, from_above, split_axis, axis_name), from_above]


def expert_activation(row_data, gate_weights):
    gate_out = jnp.dot(row_data, gate_weights[0], preferred_element_type=jnp.float32)
    up_out = jnp.dot(row_data, gate_weights[1], preferred_element_type=jnp.float32)
    return (jnp.maximum(gate_out, 0.0) * up_out).astype(jnp.bfloat16)


def body(
    hidden_in,
    queries,
    cache_keys,
    cache_values,
    lengths,
    routes,
    attn_gain,
    key_proj,
    value_proj,
    out_proj,
    moe_gain,
    router,
    gate_up,
    down_proj,
):
    own_count = hidden_in.shape[1]
    model_width = hidden_in.shape[2]
    hid_index = lax.axis_index("hid")
    hid_count = lax.axis_size("hid")
    group_size = QH // KVH
    normed = normalize(hidden_in[0], attn_gain).astype(jnp.bfloat16)
    key_width = key_proj.shape[1]
    new_kv = jnp.dot(
        normed, jnp.concatenate([key_proj, value_proj], axis=1), preferred_element_type=jnp.float32
    ).astype(jnp.bfloat16)
    new_keys = new_kv[:, :key_width]
    new_values = new_kv[:, key_width:]
    length = lengths[0]
    cache_local = cache_keys.shape[1]
    shifted_kv = ring_gather(jnp.concatenate([cache_keys[0], cache_values[0]], axis=1), 0)
    received = [new_kv]
    for shift in range(1, hid_count):
        pairs = [(source, source + shift) for source in range(hid_count - shift)]
        received.append(lax.ppermute(new_kv, "hid", pairs))
    new_parts = []
    for part in range(hid_count):
        distance = hid_index - part
        chosen = received[-1]
        for shift in range(hid_count - 2, -1, -1):
            chosen = jnp.where(distance == shift, received[shift], chosen)
        new_parts.append(chosen)
    new_parts = jnp.stack(new_parts)
    stacked_weights, _, _ = lax.optimization_barrier(
        (jnp.concatenate([gate_up[0], down_proj[0].T[None]], axis=0), shifted_kv[2], new_parts)
    )
    weights_below, weights_above = ring_neighbours(stacked_weights[:2])
    grouped = (
        queries[0]
        .reshape(own_count, KVH, group_size, HD)
        .transpose(1, 2, 0, 3)
        .reshape(KVH, group_size * own_count, HD)
    )
    attended = (
        attention(grouped, shifted_kv, new_parts, length, hid_index, own_count)
        .reshape(KVH, group_size, own_count, HD)
        .transpose(2, 0, 1, 3)
        .reshape(own_count, QH * HD)
    )
    mid_stream = (
        hidden_in[0].astype(jnp.float32)
        + jnp.dot(attended, out_proj, preferred_element_type=jnp.float32)
    ).astype(jnp.bfloat16)
    moe_in = normalize(mid_stream, moe_gain).astype(jnp.bfloat16)
    logits = jnp.dot(moe_in, router, preferred_element_type=jnp.float32)
    expert_count = router.shape[1]
    top_count = routes.shape[2]
    capacity = 2 * own_count * top_count // expert_count
    own_routes = lax.dynamic_slice_in_dim(routes[0], hid_index * own_count, own_count, axis=0)
    flat_routes = own_routes.reshape(-1)
    onehot = (flat_routes[:, None] == jnp.arange(expert_count, dtype=jnp.int32)[None, :]).astype(
        jnp.int32
    )
    slot_ids = jnp.sum((jnp.cumsum(onehot, axis=0) - 1) * onehot, axis=-1)
    targets = flat_routes * capacity + slot_ids
    slot_count = expert_count * capacity
    pick = targets[None, :] == jnp.arange(slot_count, dtype=jnp.int32)[:, None]
    pick_rows = jnp.any(pick.reshape(slot_count, own_count, top_count), axis=-1).astype(jnp.bfloat16)
    send_rows = jnp.dot(pick_rows, moe_in, preferred_element_type=jnp.float32).astype(jnp.bfloat16)
    send_rows, weights_below, weights_above = lax.optimization_barrier(
        (send_rows, weights_below, weights_above)
    )
    shifted_down = ring_gather(stacked_weights[2:], 1)
    shifted_gate_up = [
        stacked_weights[:2],
        weights_below,
        ring_far(weights_below, weights_above, 1),
        weights_above,
    ]
    all_weights = jnp.stack(
        [jnp.concatenate([both, down], axis=0) for both, down in zip(shifted_gate_up, shifted_down)]
    )
    grouped_rows = lax.all_to_all(
        send_rows.reshape(expert_count, capacity, model_width), "req", 0, 0, tiled=True
    )
    flat_rows = grouped_rows.reshape(-1, model_width)
    gate_out = jnp.einsum(
        "nd,hdf->hnf", flat_rows, all_weights[:, 0], preferred_element_type=jnp.float32
    )
    up_out = jnp.einsum(
        "nd,hdf->hnf", flat_rows, all_weights[:, 1], preferred_element_type=jnp.float32
    )
    activation = (jnp.maximum(gate_out, 0.0) * up_out).astype(jnp.bfloat16)
    partials = jnp.einsum(
        "hnf,hdf->hnd", activation, all_weights[:, 2], preferred_element_type=jnp.float32
    ).astype(jnp.bfloat16)
    expert_out = jnp.sum(partials.astype(jnp.float32), axis=0).astype(jnp.bfloat16)
    returned = lax.all_to_all(
        expert_out.reshape(-1, capacity, model_width), "req", 0, 0, tiled=True
    )
    fetched = jnp.dot(
        pick.T.astype(jnp.bfloat16),
        returned.reshape(slot_count, model_width),
        preferred_element_type=jnp.float32,
    ).reshape(own_count, top_count, model_width)
    picked = jnp.take_along_axis(logits, own_routes, axis=1)
    gate_values = jax.nn.sigmoid(picked)
    weights = gate_values / jnp.sum(gate_values, axis=1, keepdims=True)
    moe_out = jnp.sum(weights[..., None] * fetched, axis=1)
    final_rows = (mid_stream.astype(jnp.float32) + moe_out).astype(jnp.bfloat16)
    return (final_rows[None], new_keys[None], new_values[None])


def solution(mesh):
    in_specs = (
        P("req", "hid", None),
        P("req", "hid", None),
        P("req", "hid", None),
        P("req", "hid", None),
        P("req"),
        P("req", None, None),
        P(),
        P(),
        P(),
        P(),
        P(),
        P(),
        P("req", None, None, "hid"),
        P("req", "hid", None),
    )
    out_specs = (P("req", "hid", None), P("req", "hid", None), P("req", "hid", None))
    return jax.shard_map(body, mesh=mesh, in_specs=in_specs, out_specs=out_specs, check_vma=False)
```

```python
import jax
import jax.numpy as jnp
from jax import lax
from jax.sharding import PartitionSpec as P
from jax.experimental import pallas as pl
from jax.experimental.pallas import tpu as pltpu
import functools

QH = 12
KVH = 2
HD = 128


EPS = 1e-06
MASKED_SCORE = -1e30
KEY_BLOCK = 512
LANES = 128


def normalize(row_data, gain_vector):
    row_data = row_data.astype(jnp.float32)
    return (
        row_data
        * lax.rsqrt(jnp.mean(row_data * row_data, axis=-1, keepdims=True) + EPS)
        * gain_vector
    )


def absorb(state_now, grouped, key_rows, value_rows, visible):
    row_max, totals, accumulated = state_now
    scores = jnp.einsum(
        "tgsd,kgd->gstk", grouped, key_rows.reshape(-1, KVH, HD), preferred_element_type=jnp.float32
    ) * HD ** (-0.5)
    scores = jnp.where(visible, scores, MASKED_SCORE)
    new_max = jnp.maximum(row_max, jnp.max(scores, axis=-1))
    weights = jnp.where(visible, jnp.exp(scores - new_max[..., None]), 0.0)
    rescale = jnp.exp(row_max - new_max)
    totals = totals * rescale + jnp.sum(weights, axis=-1)
    accumulated = accumulated * rescale[..., None] + jnp.einsum(
        "gstk,kgd->gstd",
        weights.astype(jnp.bfloat16),
        value_rows.reshape(-1, KVH, HD),
        preferred_element_type=jnp.float32,
    )
    return (new_max, totals, accumulated)


def cache_block(state_now, grouped, key_rows, value_rows, first_pos, length):
    positions = first_pos + jnp.arange(key_rows.shape[0], dtype=jnp.int32)
    visible = (positions < length)[None, :]
    return lax.cond(
        first_pos < length,
        lambda current: absorb(current, grouped, key_rows, value_rows, visible),
        lambda current: current,
        state_now,
    )


def span_block(state_now, grouped, key_rows, value_rows, first_pos, query_pos):
    positions = first_pos + jnp.arange(key_rows.shape[0], dtype=jnp.int32)
    visible = positions[None, :] <= query_pos[:, None]
    return lax.cond(
        first_pos <= query_pos[-1],
        lambda current: absorb(current, grouped, key_rows, value_rows, visible),
        lambda current: current,
        state_now,
    )


def block_size(extent):
    return max(min(KEY_BLOCK, extent), extent // 8)


def empty_state(query_count):
    group_size = QH // KVH
    return (
        jnp.full((KVH, group_size, query_count), MASKED_SCORE, jnp.float32),
        jnp.zeros((KVH, group_size, query_count), jnp.float32),
        jnp.zeros((KVH, group_size, query_count, HD), jnp.float32),
    )


def attention_kernel(
    token_count,
    scalars,
    q_ref,
    k0_ref,
    k1_ref,
    k2_ref,
    k3_ref,
    v0_ref,
    v1_ref,
    v2_ref,
    v3_ref,
    kn_ref,
    vn_ref,
    o_ref,
    m_ref,
    l_ref,
    acc_ref,
    s_ref,
):
    length = scalars[0]
    hid_index = scalars[1]
    k_refs = (k0_ref, k1_ref, k2_ref, k3_ref)
    v_refs = (v0_ref, v1_ref, v2_ref, v3_ref)
    parts = len(k_refs)
    cache_rows = k0_ref.shape[0]
    rows = q_ref.shape[1]
    q = q_ref[0]
    m_ref[...] = jnp.full(m_ref.shape, MASKED_SCORE, jnp.float32)
    l_ref[...] = jnp.zeros(l_ref.shape, jnp.float32)
    acc_ref[...] = jnp.zeros(acc_ref.shape, jnp.float32)
    blocks = []
    for shift in range(parts):
        for first in range(0, cache_rows, KEY_BLOCK):
            blocks.append((shift, first, min(KEY_BLOCK, cache_rows - first), True))
    for part in range(parts):
        blocks.append((part, 0, token_count, False))

    def part_of(index, is_cache):
        return (hid_index - index + parts) % parts if is_cache else index

    def slot(index, first, is_cache):
        return index * cache_rows + first if is_cache else parts * cache_rows + index * token_count

    def live(index, first, size, is_cache):
        if is_cache:
            return part_of(index, True) * cache_rows + first < length
        return index <= hid_index

    def whole(index, first, size, is_cache):
        if is_cache:
            return part_of(index, True) * cache_rows + first + size <= length
        return index < hid_index

    def visible(index, first, size, is_cache):
        if is_cache:
            start = part_of(index, True) * cache_rows + first
            return start + lax.broadcasted_iota(jnp.int32, (1, size), 1) < length
        key_pos = index * token_count + lax.broadcasted_iota(jnp.int32, (1, size), 1)
        row_ids = lax.broadcasted_iota(jnp.int32, (rows, 1), 0)
        return key_pos <= hid_index * token_count + row_ids % token_count

    def first_pass(index, first, size, is_cache, masked):
        if is_cache:
            k = k_refs[index][pl.ds(first, size), :]
        else:
            k = kn_ref[index]
        raw = lax.dot_general(q, k, (((1,), (1,)), ((), ())), preferred_element_type=jnp.float32)
        s = raw * HD ** (-0.5)
        if masked:
            s = jnp.where(visible(index, first, size, is_cache), s, MASKED_SCORE)
        s_ref[:, pl.ds(slot(index, first, is_cache), size)] = s
        tile_max = s[:, 0:LANES]
        for lane in range(LANES, size, LANES):
            tile_max = jnp.maximum(tile_max, s[:, lane : lane + LANES])
        m_ref[...] = jnp.maximum(m_ref[...], tile_max)

    for index, first, size, is_cache in blocks:
        is_whole = whole(index, first, size, is_cache)
        pl.when(is_whole)(functools.partial(first_pass, index, first, size, is_cache, False))
        pl.when(jnp.logical_and(live(index, first, size, is_cache), jnp.logical_not(is_whole)))(
            functools.partial(first_pass, index, first, size, is_cache, True)
        )

    row_max = jnp.max(m_ref[...], axis=-1, keepdims=True)

    for index, first, size, is_cache in blocks:

        @pl.when(live(index, first, size, is_cache))
        def _():
            w = jnp.exp(s_ref[:, pl.ds(slot(index, first, is_cache), size)] - row_max)
            tile_sum = w[:, 0:LANES]
            for lane in range(LANES, size, LANES):
                tile_sum = tile_sum + w[:, lane : lane + LANES]
            l_ref[...] += tile_sum
            v = v_refs[index][pl.ds(first, size), :] if is_cache else vn_ref[index]
            acc_ref[...] += jnp.dot(w.astype(jnp.bfloat16), v, preferred_element_type=jnp.float32)

    o_ref[0] = (acc_ref[...] / jnp.sum(l_ref[...], axis=-1, keepdims=True)).astype(o_ref.dtype)


def attention(grouped, shifted_kv, new_kv, length, hid_index, token_count, interpret=False):
    groups, rows, head = grouped.shape
    parts = len(shifted_kv)
    cache_rows = shifted_kv[0].shape[0]
    scalars = jnp.stack([length, hid_index]).astype(jnp.int32)
    k_spec = pl.BlockSpec((cache_rows, head), lambda g, s: (0, g))
    v_spec = pl.BlockSpec((cache_rows, head), lambda g, s: (0, groups + g))
    kn_spec = pl.BlockSpec((parts, token_count, head), lambda g, s: (0, 0, g))
    vn_spec = pl.BlockSpec((parts, token_count, head), lambda g, s: (0, 0, groups + g))
    row_spec = pl.BlockSpec((1, rows, head), lambda g, s: (g, 0, 0))
    return pl.pallas_call(
        functools.partial(attention_kernel, token_count),
        out_shape=jax.ShapeDtypeStruct((groups, rows, head), jnp.bfloat16),
        grid_spec=pltpu.PrefetchScalarGridSpec(
            num_scalar_prefetch=1,
            grid=(groups,),
            in_specs=[row_spec] + [k_spec] * parts + [v_spec] * parts + [kn_spec, vn_spec],
            out_specs=row_spec,
            scratch_shapes=[
                pltpu.VMEM((rows, LANES), jnp.float32),
                pltpu.VMEM((rows, LANES), jnp.float32),
                pltpu.VMEM((rows, head), jnp.float32),
                pltpu.VMEM((rows, parts * (cache_rows + token_count)), jnp.float32),
            ],
        ),
        interpret=interpret,
    )(scalars, grouped, *shifted_kv, *shifted_kv, new_kv, new_kv)


def ring_neighbours(shard, axis_name="hid"):
    count = lax.axis_size(axis_name)
    up = [(source, (source + 1) % count) for source in range(count)]
    down = [(source, (source - 1) % count) for source in range(count)]
    return lax.ppermute(shard, axis_name, up), lax.ppermute(shard, axis_name, down)


def ring_far(from_below, from_above, split_axis, axis_name="hid"):
    count = lax.axis_size(axis_name)
    up = [(source, (source + 1) % count) for source in range(count)]
    down = [(source, (source - 1) % count) for source in range(count)]
    extent = from_below.shape[split_axis]
    half = extent // 2
    return jnp.concatenate(
        [
            lax.ppermute(lax.slice_in_dim(from_below, 0, half, axis=split_axis), axis_name, up),
            lax.ppermute(lax.slice_in_dim(from_above, half, extent, axis=split_axis), axis_name, down),
        ],
        axis=split_axis,
    )


def ring_gather(shard, split_axis, axis_name="hid"):
    from_below, from_above = ring_neighbours(shard, axis_name)
    return [shard, from_below, ring_far(from_below, from_above, split_axis, axis_name), from_above]


def expert_activation(row_data, gate_weights):
    gate_out = jnp.dot(row_data, gate_weights[0], preferred_element_type=jnp.float32)
    up_out = jnp.dot(row_data, gate_weights[1], preferred_element_type=jnp.float32)
    return (jnp.maximum(gate_out, 0.0) * up_out).astype(jnp.bfloat16)


def body(
    hidden_in,
    queries,
    cache_keys,
    cache_values,
    lengths,
    routes,
    attn_gain,
    key_proj,
    value_proj,
    out_proj,
    moe_gain,
    router,
    gate_up,
    down_proj,
):
    own_count = hidden_in.shape[1]
    model_width = hidden_in.shape[2]
    hid_index = lax.axis_index("hid")
    hid_count = lax.axis_size("hid")
    group_size = QH // KVH
    normed = normalize(hidden_in[0], attn_gain).astype(jnp.bfloat16)
    key_width = key_proj.shape[1]
    new_kv = jnp.dot(
        normed, jnp.concatenate([key_proj, value_proj], axis=1), preferred_element_type=jnp.float32
    ).astype(jnp.bfloat16)
    new_keys = new_kv[:, :key_width]
    new_values = new_kv[:, key_width:]
    length = lengths[0]
    cache_local = cache_keys.shape[1]
    shifted_kv = ring_gather(jnp.concatenate([cache_keys[0], cache_values[0]], axis=1), 0)
    received = [new_kv]
    for shift in range(1, hid_count):
        pairs = [(source, source + shift) for source in range(hid_count - shift)]
        received.append(lax.ppermute(new_kv, "hid", pairs))
    new_parts = []
    for part in range(hid_count):
        distance = hid_index - part
        chosen = received[-1]
        for shift in range(hid_count - 2, -1, -1):
            chosen = jnp.where(distance == shift, received[shift], chosen)
        new_parts.append(chosen)
    new_parts = jnp.stack(new_parts)
    stacked_weights, _, _ = lax.optimization_barrier(
        (jnp.concatenate([gate_up[0], down_proj[0].T[None]], axis=0), shifted_kv[2], new_parts)
    )
    weights_below, weights_above = ring_neighbours(stacked_weights[:2])
    grouped = (
        queries[0]
        .reshape(own_count, KVH, group_size, HD)
        .transpose(1, 2, 0, 3)
        .reshape(KVH, group_size * own_count, HD)
    )
    attended = (
        attention(grouped, shifted_kv, new_parts, length, hid_index, own_count)
        .reshape(KVH, group_size, own_count, HD)
        .transpose(2, 0, 1, 3)
        .reshape(own_count, QH * HD)
    )
    mid_stream = (
        hidden_in[0].astype(jnp.float32)
        + jnp.dot(attended, out_proj, preferred_element_type=jnp.float32)
    ).astype(jnp.bfloat16)
    moe_in = normalize(mid_stream, moe_gain).astype(jnp.bfloat16)
    logits = jnp.dot(moe_in, router, preferred_element_type=jnp.float32)
    expert_count = router.shape[1]
    top_count = routes.shape[2]
    capacity = 2 * own_count * top_count // expert_count
    own_routes = lax.dynamic_slice_in_dim(routes[0], hid_index * own_count, own_count, axis=0)
    flat_routes = own_routes.reshape(-1)
    onehot = (flat_routes[:, None] == jnp.arange(expert_count, dtype=jnp.int32)[None, :]).astype(
        jnp.int32
    )
    slot_ids = jnp.sum((jnp.cumsum(onehot, axis=0) - 1) * onehot, axis=-1)
    targets = flat_routes * capacity + slot_ids
    slot_count = expert_count * capacity
    pick = targets[None, :] == jnp.arange(slot_count, dtype=jnp.int32)[:, None]
    pick_rows = jnp.any(pick.reshape(slot_count, own_count, top_count), axis=-1).astype(jnp.bfloat16)
    send_rows = jnp.dot(pick_rows, moe_in, preferred_element_type=jnp.float32).astype(jnp.bfloat16)
    send_rows, weights_below, weights_above = lax.optimization_barrier(
        (send_rows, weights_below, weights_above)
    )
    shifted_down = ring_gather(stacked_weights[2:], 1)
    shifted_gate_up = [
        stacked_weights[:2],
        weights_below,
        ring_far(weights_below, weights_above, 1),
        weights_above,
    ]
    all_weights = jnp.stack(
        [jnp.concatenate([both, down], axis=0) for both, down in zip(shifted_gate_up, shifted_down)]
    )
    grouped_rows = lax.all_to_all(
        send_rows.reshape(expert_count, capacity, model_width), "req", 0, 0, tiled=True
    )
    flat_rows = grouped_rows.reshape(-1, model_width)
    gate_out = jnp.einsum(
        "nd,hdf->hnf", flat_rows, all_weights[:, 0], preferred_element_type=jnp.float32
    )
    up_out = jnp.einsum(
        "nd,hdf->hnf", flat_rows, all_weights[:, 1], preferred_element_type=jnp.float32
    )
    activation = (jnp.maximum(gate_out, 0.0) * up_out).astype(jnp.bfloat16)
    partials = jnp.einsum(
        "hnf,hdf->hnd", activation, all_weights[:, 2], preferred_element_type=jnp.float32
    ).astype(jnp.bfloat16)
    expert_out = jnp.sum(partials.astype(jnp.float32), axis=0).astype(jnp.bfloat16)
    returned = lax.all_to_all(
        expert_out.reshape(-1, capacity, model_width), "req", 0, 0, tiled=True
    )
    fetched = jnp.dot(
        pick.T.astype(jnp.bfloat16),
        returned.reshape(slot_count, model_width),
        preferred_element_type=jnp.float32,
    ).reshape(own_count, top_count, model_width)
    picked = jnp.take_along_axis(logits, own_routes, axis=1)
    gate_values = jax.nn.sigmoid(picked)
    weights = gate_values / jnp.sum(gate_values, axis=1, keepdims=True)
    moe_out = jnp.sum(weights[..., None] * fetched, axis=1)
    final_rows = (mid_stream.astype(jnp.float32) + moe_out).astype(jnp.bfloat16)
    return (final_rows[None], new_keys[None], new_values[None])


def solution(mesh):
    in_specs = (
        P("req", "hid", None),
        P("req", "hid", None),
        P("req", "hid", None),
        P("req", "hid", None),
        P("req"),
        P("req", None, None),
        P(),
        P(),
        P(),
        P(),
        P(),
        P(),
        P("req", None, None, "hid"),
        P("req", "hid", None),
    )
    out_specs = (P("req", "hid", None), P("req", "hid", None), P("req", "hid", None))
    return jax.shard_map(body, mesh=mesh, in_specs=in_specs, out_specs=out_specs, check_vma=False)
```

```python
import jax
import jax.numpy as jnp
from jax import lax
from jax.sharding import PartitionSpec as P
from jax.experimental import pallas as pl
from jax.experimental.pallas import tpu as pltpu
import functools

QH = 12
KVH = 2
HD = 128


EPS = 1e-06
MASKED_SCORE = -1e30
KEY_BLOCK = 1024
LANES = 128


def normalize(row_data, gain_vector):
    row_data = row_data.astype(jnp.float32)
    return (
        row_data
        * lax.rsqrt(jnp.mean(row_data * row_data, axis=-1, keepdims=True) + EPS)
        * gain_vector
    )


def absorb(state_now, grouped, key_rows, value_rows, visible):
    row_max, totals, accumulated = state_now
    scores = jnp.einsum(
        "tgsd,kgd->gstk", grouped, key_rows.reshape(-1, KVH, HD), preferred_element_type=jnp.float32
    ) * HD ** (-0.5)
    scores = jnp.where(visible, scores, MASKED_SCORE)
    new_max = jnp.maximum(row_max, jnp.max(scores, axis=-1))
    weights = jnp.where(visible, jnp.exp(scores - new_max[..., None]), 0.0)
    rescale = jnp.exp(row_max - new_max)
    totals = totals * rescale + jnp.sum(weights, axis=-1)
    accumulated = accumulated * rescale[..., None] + jnp.einsum(
        "gstk,kgd->gstd",
        weights.astype(jnp.bfloat16),
        value_rows.reshape(-1, KVH, HD),
        preferred_element_type=jnp.float32,
    )
    return (new_max, totals, accumulated)


def cache_block(state_now, grouped, key_rows, value_rows, first_pos, length):
    positions = first_pos + jnp.arange(key_rows.shape[0], dtype=jnp.int32)
    visible = (positions < length)[None, :]
    return lax.cond(
        first_pos < length,
        lambda current: absorb(current, grouped, key_rows, value_rows, visible),
        lambda current: current,
        state_now,
    )


def span_block(state_now, grouped, key_rows, value_rows, first_pos, query_pos):
    positions = first_pos + jnp.arange(key_rows.shape[0], dtype=jnp.int32)
    visible = positions[None, :] <= query_pos[:, None]
    return lax.cond(
        first_pos <= query_pos[-1],
        lambda current: absorb(current, grouped, key_rows, value_rows, visible),
        lambda current: current,
        state_now,
    )


def block_size(extent):
    return max(min(KEY_BLOCK, extent), extent // 8)


def empty_state(query_count):
    group_size = QH // KVH
    return (
        jnp.full((KVH, group_size, query_count), MASKED_SCORE, jnp.float32),
        jnp.zeros((KVH, group_size, query_count), jnp.float32),
        jnp.zeros((KVH, group_size, query_count, HD), jnp.float32),
    )


def attention_kernel(
    token_count,
    scalars,
    q_ref,
    k0_ref,
    k1_ref,
    k2_ref,
    k3_ref,
    v0_ref,
    v1_ref,
    v2_ref,
    v3_ref,
    kn_ref,
    vn_ref,
    o_ref,
    m_ref,
    l_ref,
    acc_ref,
    s_ref,
):
    length = scalars[0]
    hid_index = scalars[1]
    k_refs = (k0_ref, k1_ref, k2_ref, k3_ref)
    v_refs = (v0_ref, v1_ref, v2_ref, v3_ref)
    parts = len(k_refs)
    cache_rows = k0_ref.shape[0]
    rows = q_ref.shape[1]
    q = q_ref[0]
    m_ref[...] = jnp.full(m_ref.shape, MASKED_SCORE, jnp.float32)
    l_ref[...] = jnp.zeros(l_ref.shape, jnp.float32)
    acc_ref[...] = jnp.zeros(acc_ref.shape, jnp.float32)
    blocks = []
    for shift in range(parts):
        for first in range(0, cache_rows, KEY_BLOCK):
            blocks.append((shift, first, min(KEY_BLOCK, cache_rows - first), True))
    for part in range(parts):
        blocks.append((part, 0, token_count, False))

    def part_of(index, is_cache):
        return (hid_index - index + parts) % parts if is_cache else index

    def slot(index, first, is_cache):
        return index * cache_rows + first if is_cache else parts * cache_rows + index * token_count

    def live(index, first, size, is_cache):
        if is_cache:
            return part_of(index, True) * cache_rows + first < length
        return index <= hid_index

    def whole(index, first, size, is_cache):
        if is_cache:
            return part_of(index, True) * cache_rows + first + size <= length
        return index < hid_index

    def visible(index, first, size, is_cache):
        if is_cache:
            start = part_of(index, True) * cache_rows + first
            return start + lax.broadcasted_iota(jnp.int32, (1, size), 1) < length
        key_pos = index * token_count + lax.broadcasted_iota(jnp.int32, (1, size), 1)
        row_ids = lax.broadcasted_iota(jnp.int32, (rows, 1), 0)
        return key_pos <= hid_index * token_count + row_ids % token_count

    def first_pass(index, first, size, is_cache, masked):
        if is_cache:
            k = k_refs[index][pl.ds(first, size), :]
        else:
            k = kn_ref[index]
        raw = lax.dot_general(q, k, (((1,), (1,)), ((), ())), preferred_element_type=jnp.float32)
        s = raw * HD ** (-0.5)
        if masked:
            s = jnp.where(visible(index, first, size, is_cache), s, MASKED_SCORE)
        s_ref[:, pl.ds(slot(index, first, is_cache), size)] = s
        tile_max = s[:, 0:LANES]
        for lane in range(LANES, size, LANES):
            tile_max = jnp.maximum(tile_max, s[:, lane : lane + LANES])
        m_ref[...] = jnp.maximum(m_ref[...], tile_max)

    for index, first, size, is_cache in blocks:
        is_whole = whole(index, first, size, is_cache)
        pl.when(is_whole)(functools.partial(first_pass, index, first, size, is_cache, False))
        pl.when(jnp.logical_and(live(index, first, size, is_cache), jnp.logical_not(is_whole)))(
            functools.partial(first_pass, index, first, size, is_cache, True)
        )

    row_max = jnp.max(m_ref[...], axis=-1, keepdims=True)

    for index, first, size, is_cache in blocks:

        @pl.when(live(index, first, size, is_cache))
        def _():
            w = jnp.exp(s_ref[:, pl.ds(slot(index, first, is_cache), size)] - row_max)
            tile_sum = w[:, 0:LANES]
            for lane in range(LANES, size, LANES):
                tile_sum = tile_sum + w[:, lane : lane + LANES]
            l_ref[...] += tile_sum
            v = v_refs[index][pl.ds(first, size), :] if is_cache else vn_ref[index]
            acc_ref[...] += jnp.dot(w.astype(jnp.bfloat16), v, preferred_element_type=jnp.float32)

    o_ref[0] = (acc_ref[...] / jnp.sum(l_ref[...], axis=-1, keepdims=True)).astype(o_ref.dtype)


def attention(grouped, shifted_kv, new_kv, length, hid_index, token_count, interpret=False):
    groups, rows, head = grouped.shape
    parts = len(shifted_kv)
    cache_rows = shifted_kv[0].shape[0]
    scalars = jnp.stack([length, hid_index]).astype(jnp.int32)
    k_spec = pl.BlockSpec((cache_rows, head), lambda g, s: (0, g))
    v_spec = pl.BlockSpec((cache_rows, head), lambda g, s: (0, groups + g))
    kn_spec = pl.BlockSpec((parts, token_count, head), lambda g, s: (0, 0, g))
    vn_spec = pl.BlockSpec((parts, token_count, head), lambda g, s: (0, 0, groups + g))
    row_spec = pl.BlockSpec((1, rows, head), lambda g, s: (g, 0, 0))
    return pl.pallas_call(
        functools.partial(attention_kernel, token_count),
        out_shape=jax.ShapeDtypeStruct((groups, rows, head), jnp.bfloat16),
        grid_spec=pltpu.PrefetchScalarGridSpec(
            num_scalar_prefetch=1,
            grid=(groups,),
            in_specs=[row_spec] + [k_spec] * parts + [v_spec] * parts + [kn_spec, vn_spec],
            out_specs=row_spec,
            scratch_shapes=[
                pltpu.VMEM((rows, LANES), jnp.float32),
                pltpu.VMEM((rows, LANES), jnp.float32),
                pltpu.VMEM((rows, head), jnp.float32),
                pltpu.VMEM((rows, parts * (cache_rows + token_count)), jnp.float32),
            ],
        ),
        interpret=interpret,
    )(scalars, grouped, *shifted_kv, *shifted_kv, new_kv, new_kv)


def ring_neighbours(shard, axis_name="hid"):
    count = lax.axis_size(axis_name)
    up = [(source, (source + 1) % count) for source in range(count)]
    down = [(source, (source - 1) % count) for source in range(count)]
    return lax.ppermute(shard, axis_name, up), lax.ppermute(shard, axis_name, down)


def ring_far(from_below, from_above, split_axis, axis_name="hid"):
    count = lax.axis_size(axis_name)
    up = [(source, (source + 1) % count) for source in range(count)]
    down = [(source, (source - 1) % count) for source in range(count)]
    extent = from_below.shape[split_axis]
    half = extent // 2
    return jnp.concatenate(
        [
            lax.ppermute(lax.slice_in_dim(from_below, 0, half, axis=split_axis), axis_name, up),
            lax.ppermute(lax.slice_in_dim(from_above, half, extent, axis=split_axis), axis_name, down),
        ],
        axis=split_axis,
    )


def ring_gather(shard, split_axis, axis_name="hid"):
    from_below, from_above = ring_neighbours(shard, axis_name)
    return [shard, from_below, ring_far(from_below, from_above, split_axis, axis_name), from_above]


def expert_activation(row_data, gate_weights):
    gate_out = jnp.dot(row_data, gate_weights[0], preferred_element_type=jnp.float32)
    up_out = jnp.dot(row_data, gate_weights[1], preferred_element_type=jnp.float32)
    return (jnp.maximum(gate_out, 0.0) * up_out).astype(jnp.bfloat16)


def body(
    hidden_in,
    queries,
    cache_keys,
    cache_values,
    lengths,
    routes,
    attn_gain,
    key_proj,
    value_proj,
    out_proj,
    moe_gain,
    router,
    gate_up,
    down_proj,
):
    own_count = hidden_in.shape[1]
    model_width = hidden_in.shape[2]
    hid_index = lax.axis_index("hid")
    hid_count = lax.axis_size("hid")
    group_size = QH // KVH
    normed = normalize(hidden_in[0], attn_gain).astype(jnp.bfloat16)
    key_width = key_proj.shape[1]
    new_kv = jnp.dot(
        normed, jnp.concatenate([key_proj, value_proj], axis=1), preferred_element_type=jnp.float32
    ).astype(jnp.bfloat16)
    new_keys = new_kv[:, :key_width]
    new_values = new_kv[:, key_width:]
    length = lengths[0]
    cache_local = cache_keys.shape[1]
    shifted_kv = ring_gather(jnp.concatenate([cache_keys[0], cache_values[0]], axis=1), 0)
    received = [new_kv]
    for shift in range(1, hid_count):
        pairs = [(source, source + shift) for source in range(hid_count - shift)]
        received.append(lax.ppermute(new_kv, "hid", pairs))
    new_parts = []
    for part in range(hid_count):
        distance = hid_index - part
        chosen = received[-1]
        for shift in range(hid_count - 2, -1, -1):
            chosen = jnp.where(distance == shift, received[shift], chosen)
        new_parts.append(chosen)
    new_parts = jnp.stack(new_parts)
    stacked_weights, _, _ = lax.optimization_barrier(
        (jnp.concatenate([gate_up[0], down_proj[0].T[None]], axis=0), shifted_kv[2], new_parts)
    )
    weights_below, weights_above = ring_neighbours(stacked_weights[:2])
    grouped = (
        queries[0]
        .reshape(own_count, KVH, group_size, HD)
        .transpose(1, 2, 0, 3)
        .reshape(KVH, group_size * own_count, HD)
    )
    attended = (
        attention(grouped, shifted_kv, new_parts, length, hid_index, own_count)
        .reshape(KVH, group_size, own_count, HD)
        .transpose(2, 0, 1, 3)
        .reshape(own_count, QH * HD)
    )
    mid_stream = (
        hidden_in[0].astype(jnp.float32)
        + jnp.dot(attended, out_proj, preferred_element_type=jnp.float32)
    ).astype(jnp.bfloat16)
    moe_in = normalize(mid_stream, moe_gain).astype(jnp.bfloat16)
    logits = jnp.dot(moe_in, router, preferred_element_type=jnp.float32)
    expert_count = router.shape[1]
    top_count = routes.shape[2]
    capacity = 2 * own_count * top_count // expert_count
    own_routes = lax.dynamic_slice_in_dim(routes[0], hid_index * own_count, own_count, axis=0)
    flat_routes = own_routes.reshape(-1)
    onehot = (flat_routes[:, None] == jnp.arange(expert_count, dtype=jnp.int32)[None, :]).astype(
        jnp.int32
    )
    slot_ids = jnp.sum((jnp.cumsum(onehot, axis=0) - 1) * onehot, axis=-1)
    targets = flat_routes * capacity + slot_ids
    slot_count = expert_count * capacity
    pick = targets[None, :] == jnp.arange(slot_count, dtype=jnp.int32)[:, None]
    pick_rows = jnp.any(pick.reshape(slot_count, own_count, top_count), axis=-1).astype(jnp.bfloat16)
    send_rows = jnp.dot(pick_rows, moe_in, preferred_element_type=jnp.float32).astype(jnp.bfloat16)
    send_rows, weights_below, weights_above = lax.optimization_barrier(
        (send_rows, weights_below, weights_above)
    )
    shifted_down = ring_gather(stacked_weights[2:], 1)
    shifted_gate_up = [
        stacked_weights[:2],
        weights_below,
        ring_far(weights_below, weights_above, 1),
        weights_above,
    ]
    all_weights = jnp.stack(
        [jnp.concatenate([both, down], axis=0) for both, down in zip(shifted_gate_up, shifted_down)]
    )
    grouped_rows = lax.all_to_all(
        send_rows.reshape(expert_count, capacity, model_width), "req", 0, 0, tiled=True
    )
    flat_rows = grouped_rows.reshape(-1, model_width)
    gate_out = jnp.einsum(
        "nd,hdf->hnf", flat_rows, all_weights[:, 0], preferred_element_type=jnp.float32
    )
    up_out = jnp.einsum(
        "nd,hdf->hnf", flat_rows, all_weights[:, 1], preferred_element_type=jnp.float32
    )
    activation = (jnp.maximum(gate_out, 0.0) * up_out).astype(jnp.bfloat16)
    partials = jnp.einsum(
        "hnf,hdf->hnd", activation, all_weights[:, 2], preferred_element_type=jnp.float32
    ).astype(jnp.bfloat16)
    expert_out = jnp.sum(partials.astype(jnp.float32), axis=0).astype(jnp.bfloat16)
    returned = lax.all_to_all(
        expert_out.reshape(-1, capacity, model_width), "req", 0, 0, tiled=True
    )
    fetched = jnp.dot(
        pick.T.astype(jnp.bfloat16),
        returned.reshape(slot_count, model_width),
        preferred_element_type=jnp.float32,
    ).reshape(own_count, top_count, model_width)
    picked = jnp.take_along_axis(logits, own_routes, axis=1)
    gate_values = jax.nn.sigmoid(picked)
    weights = gate_values / jnp.sum(gate_values, axis=1, keepdims=True)
    moe_out = jnp.sum(weights[..., None] * fetched, axis=1)
    final_rows = (mid_stream.astype(jnp.float32) + moe_out).astype(jnp.bfloat16)
    return (final_rows[None], new_keys[None], new_values[None])


def solution(mesh):
    in_specs = (
        P("req", "hid", None),
        P("req", "hid", None),
        P("req", "hid", None),
        P("req", "hid", None),
        P("req"),
        P("req", None, None),
        P(),
        P(),
        P(),
        P(),
        P(),
        P(),
        P("req", None, None, "hid"),
        P("req", "hid", None),
    )
    out_specs = (P("req", "hid", None), P("req", "hid", None), P("req", "hid", None))
    return jax.shard_map(body, mesh=mesh, in_specs=in_specs, out_specs=out_specs, check_vma=False)
```
